32 devices in a mesh: depth: 8 (over z, y), rows: 4 (over x, core).
Axes of the slice: x: 2, y: 2, z: 4, core: 2. Of those that a mesh axis runs over, the one named last changes fastest.
Arguments:
- density_raw: bfloat16 [256, 64, 1024], P('depth', 'rows'), may hold values from -6 to 6
- colour_raw: bfloat16 [3, 256, 64, 1024], P(None, 'depth', 'rows'), may hold values from -6 to 6
- target: float32 [3, 64, 1024], P(None, 'rows'), may hold values from 0 to 1
- slab_rank: int32 [8], replicated, may hold values from 0 to 7, each once
Outputs:
- grad_density: float32 [256, 64, 1024], P('depth', 'rows')
- grad_colour: float32 [3, 256, 64, 1024], P(None, 'depth', 'rows')
The draws below stay inside these ranges and needn't reach their ends.
Inputs may be any that keep to these rules, and one draw needn't show every extreme that they name: slab_rank is a permutation: every slab has its own position along the rays.
All inputs are finite; a program needn't handle non-finite values.
Results may differ from the reference program's by a relative error of at most 0.0003.
Values may be sent and summed in bfloat16 or wider, within the bound.
No kernel may reach another device: no remote copies, remote signals or barrier semaphores. Data moves between devices by JAX's collectives and lax.ppermute only.
A program may use at most 128 MiB of HBM per device.

```python
import jax
import jax.numpy as jnp
from jax import lax

SLICES_DEV = 32
WIDTH = 1024
SLICES = 256
IMAGE_ROWS = 64
SLABS = 8


def levels(own_key, dims, pieces, least, high):
    def one(axis_at, parts):
        heights = jax.random.uniform(jax.random.fold_in(jax.random.fold_in(own_key, 6), axis_at), (parts,), jnp.float32, least / len(pieces), high / len(pieces))
        return jnp.repeat(jnp.exp(heights), dims[axis_at] // parts).reshape((-1,) + (1,) * (len(dims) - axis_at - 1))

    level = one(*pieces[0])
    for cut in pieces[1:]:
        level = level * one(*cut)
    return level


def gaussian(rng, dims, spread, most, shards=(), held_as=jnp.bfloat16):
    loudness = levels(rng, dims, shards, -0.22, 0.18) if shards else 1.0
    array = jax.random.normal(rng, dims, jnp.float32) * spread * loudness
    return jnp.minimum(jnp.maximum(array, -most), most).astype(held_as)


def setup_inputs(seed: int = 0) -> dict:
    seeds = jax.random.split(jax.random.key(seed), 5)
    return {
        "density_raw": gaussian(seeds[0], (SLICES, IMAGE_ROWS, WIDTH), 1.0, 6.0, ((0, 8), (1, 4))),
        "colour_raw": gaussian(seeds[1], (3, SLICES, IMAGE_ROWS, WIDTH), 1.0, 6.0, ((1, 8), (2, 4))),
        "target": jnp.clip(1.0 * jax.random.uniform(seeds[2], (3, IMAGE_ROWS, WIDTH), jnp.float32) ** levels(seeds[2], (3, IMAGE_ROWS, WIDTH), ((1, 4),), -0.2, 0.2), 0.0, 1.0),
        "slab_rank": jax.random.permutation(seeds[3], SLABS).astype(jnp.int32),
    }


optical_depth = 2.5
smooth_weight = 0.05


def along_rays(matrix, values):
    shape = values.shape
    flat = values.reshape(shape[0], shape[1], -1)
    mixed = jnp.einsum("ij,cjp->cip", matrix, flat, precision=lax.Precision.HIGHEST)
    return mixed.reshape(shape)


def triangles(count):
    index = jnp.arange(count, dtype=jnp.int32)
    before = (index[None, :] < index[:, None]).astype(jnp.float32)
    after = (index[None, :] > index[:, None]).astype(jnp.float32)
    return before, after


def slab_terms(density, colour_raw, step_depth):
    dense = density.astype(jnp.float32)
    colour = jax.nn.sigmoid(colour_raw.astype(jnp.float32))
    depth_term = step_depth * jax.nn.softplus(dense)
    opacity = -jnp.expm1(-depth_term)
    kept = jnp.exp(-depth_term)
    before, after = triangles(dense.shape[0])
    front_light = jnp.exp(-along_rays(before, depth_term[None]))[0]
    through = front_light * kept
    passing = jnp.exp(-jnp.sum(depth_term, axis=0))
    weighted = front_light[None] * opacity[None] * colour
    behind_local = along_rays(after, weighted) / through[None]
    after_light = passing[None] / through
    partial_value = jnp.concatenate([jnp.sum(weighted, axis=1), passing[None]], axis=0)
    return partial_value, (dense, colour, opacity, behind_local, after_light, front_light)


def slab_gradients(saved, scaled_residual, scaled_behind, slices_total):
    dense, colour, opacity, behind_local, after_light, front_light = saved
    lit = front_light * opacity
    grad_colour = slices_total * scaled_residual[:, None] * lit[None] * colour * (1.0 - colour)
    inner = jnp.sum(scaled_residual[:, None] * (colour - behind_local), axis=0) - after_light * scaled_behind[None]
    grad_density = optical_depth * front_light * (1.0 - opacity) * jax.nn.sigmoid(dense) * inner
    return grad_density, grad_colour


def composite(partials, slab_rank, target_piece):
    count = partials.shape[1]
    one_hot = (slab_rank[:, None] == jnp.arange(count, dtype=jnp.int32)[None]).astype(partials.dtype)
    ordered = jnp.einsum("sk,csl->ckl", one_hot, partials, precision=lax.Precision.HIGHEST)
    emitted, kept = ordered[:3], ordered[3:]
    before, after = triangles(count)
    front = jnp.exp(along_rays(before, jnp.log(kept)))
    weighted = front * emitted
    behind = along_rays(after, weighted) / (front * kept)
    residual = jnp.sum(weighted, axis=1) - target_piece
    scaled_residual = front * residual[:, None]
    scaled_behind = front * jnp.sum(residual[:, None] * behind, axis=0, keepdims=True)
    stacked = jnp.concatenate([scaled_residual, scaled_behind], axis=0)
    return jnp.einsum("sk,ckl->csl", one_hot, stacked, precision=lax.Precision.HIGHEST)


def smooth_gradient(dense):
    along_z = dense[1:] - dense[:-1]
    along_y = dense[:, 1:] - dense[:, :-1]
    grad_z = jnp.pad(along_z, ((1, 0), (0, 0), (0, 0))) - jnp.pad(along_z, ((0, 1), (0, 0), (0, 0)))
    grad_y = jnp.pad(along_y, ((0, 0), (1, 0), (0, 0))) - jnp.pad(along_y, ((0, 0), (0, 1), (0, 0)))
    return 2.0 * smooth_weight * (grad_z + grad_y)


def reference(density_raw, colour_raw, target, slab_rank):
    step_depth = optical_depth / SLICES
    dens_slabs = density_raw.reshape(SLABS, SLICES_DEV, IMAGE_ROWS, WIDTH)
    colour_slabs = jnp.moveaxis(colour_raw.reshape(3, SLABS, SLICES_DEV, IMAGE_ROWS, WIDTH), 1, 0)

    def forward(item):
        return slab_terms(item[0], item[1], step_depth)[0]

    partial_all = lax.map(forward, (dens_slabs, colour_slabs))
    partials = jnp.moveaxis(partial_all, 0, 1).reshape(4, SLABS, IMAGE_ROWS * WIDTH)
    returned = composite(partials, slab_rank, target.reshape(3, IMAGE_ROWS * WIDTH))
    returned = jnp.moveaxis(returned.reshape(4, SLABS, IMAGE_ROWS, WIDTH), 1, 0)

    def backward(item):
        partial_value, saved = slab_terms(item[0], item[1], step_depth)
        return slab_gradients(saved, item[2][:3], item[2][3], SLICES)

    grad_dens, grad_col = lax.map(backward, (dens_slabs, colour_slabs, returned))
    grad_density = grad_dens.reshape(SLICES, IMAGE_ROWS, WIDTH) + smooth_gradient(density_raw.astype(jnp.float32))
    grad_colour = jnp.moveaxis(grad_col, 0, 1).reshape(3, SLICES, IMAGE_ROWS, WIDTH)
    return grad_density, grad_colour
```

```python
import functools

import jax
import jax.numpy as jnp
from jax import lax
from jax.experimental import pallas as pl
from jax.experimental.pallas import tpu as pltpu
from jax.sharding import PartitionSpec as P

optical_depth = 2.5
smooth_weight = 0.05
lanes = 128


def softplus(x):
    return jnp.maximum(x, 0.0) + jnp.log1p(jnp.exp(-jnp.abs(x)))


def forward_kernel(d_ref, c_ref, out_ref, *, step):
    slices = d_ref.shape[0]
    shape = d_ref.shape[1:]

    def body(z, carry):
        acc, e0, e1, e2 = carry
        dt = step * softplus(d_ref[z].astype(jnp.float32))
        opacity = 1.0 - jnp.exp(-dt)
        lit = jnp.exp(-acc) * opacity
        e0 = e0 + lit * jax.nn.sigmoid(c_ref[0, z].astype(jnp.float32))
        e1 = e1 + lit * jax.nn.sigmoid(c_ref[1, z].astype(jnp.float32))
        e2 = e2 + lit * jax.nn.sigmoid(c_ref[2, z].astype(jnp.float32))
        return (acc + dt, e0, e1, e2)

    zero = jnp.zeros(shape, jnp.float32)
    acc, e0, e1, e2 = lax.fori_loop(0, slices, body, (zero, zero, zero, zero), unroll=4)
    out_ref[0] = e0
    out_ref[1] = e1
    out_ref[2] = e2
    out_ref[3] = jnp.exp(-acc)


def backward_kernel(d_ref, c_ref, part_ref, ans_ref, smooth_ref, gd_ref, gc_ref, *, step, slices_total):
    slices = d_ref.shape[0]
    shape = d_ref.shape[1:]

    def body(z, carry):
        acc, front, w0, w1, w2 = carry
        d = d_ref[z].astype(jnp.float32)
        sp = softplus(d)
        dt = step * sp
        opacity = 1.0 - jnp.exp(-dt)
        acc_next = acc + dt
        through = jnp.exp(-acc_next)
        inv = 1.0 / through
        lit = front * opacity
        col = [jax.nn.sigmoid(c_ref[c, z].astype(jnp.float32)) for c in range(3)]
        w = [w0 + lit * col[0], w1 + lit * col[1], w2 + lit * col[2]]
        inner = -(part_ref[3] * inv) * ans_ref[3]
        for c in range(3):
            sr = ans_ref[c]
            inner = inner + sr * (col[c] - (part_ref[c] - w[c]) * inv)
            gc_ref[c, z] = slices_total * sr * lit * col[c] * (1.0 - col[c])
        gd_ref[z] = optical_depth * through * jnp.exp(d - sp) * inner + smooth_ref[z]
        return (acc_next, through, w[0], w[1], w[2])

    zero = jnp.zeros(shape, jnp.float32)
    one = jnp.ones(shape, jnp.float32)
    lax.fori_loop(0, slices, body, (zero, one, zero, zero, zero), unroll=2)


def forward_partial(density, colour_raw, step):
    slices, rows, width = density.shape
    return pl.pallas_call(
        functools.partial(forward_kernel, step=step),
        grid=(width // lanes,),
        in_specs=[
            pl.BlockSpec((slices, rows, lanes), lambda i: (0, 0, i)),
            pl.BlockSpec((3, slices, rows, lanes), lambda i: (0, 0, 0, i)),
        ],
        out_specs=pl.BlockSpec((4, rows, lanes), lambda i: (0, 0, i)),
        out_shape=jax.ShapeDtypeStruct((4, rows, width), jnp.float32),
    )(density, colour_raw)


def backward_grads(density, colour_raw, partial_value, answers, smooth, step, slices_total):
    slices, rows, width = density.shape
    slab = pl.BlockSpec((slices, rows, lanes), lambda i: (0, 0, i))
    colours = pl.BlockSpec((3, slices, rows, lanes), lambda i: (0, 0, 0, i))
    pixel = pl.BlockSpec((4, rows, lanes), lambda i: (0, 0, i))
    return pl.pallas_call(
        functools.partial(backward_kernel, step=step, slices_total=float(slices_total)),
        grid=(width // lanes,),
        in_specs=[slab, colours, pixel, pixel, slab],
        out_specs=[slab, colours],
        out_shape=[
            jax.ShapeDtypeStruct((slices, rows, width), jnp.float32),
            jax.ShapeDtypeStruct((3, slices, rows, width), jnp.float32),
        ],
        input_output_aliases={4: 0},
    )(density, colour_raw, partial_value, answers, smooth)


def composite(parts, slab_rank, target_piece):
    emitted, passing = (parts[:3], parts[3])
    earlier = (slab_rank[None, :] < slab_rank[:, None]).astype(jnp.float32)
    later = (slab_rank[None, :] > slab_rank[:, None]).astype(jnp.float32)
    front = jnp.exp(jnp.sum(earlier[:, :, None] * jnp.log(passing)[None], axis=1))
    weighted = front[None] * emitted
    behind = jnp.sum(later[None, :, :, None] * weighted[:, None], axis=2) / (front * passing)[None]
    residual = jnp.sum(weighted, axis=1) - target_piece
    scaled_residual = front[None] * residual[:, None]
    scaled_behind = front * jnp.sum(residual[:, None] * behind, axis=0)
    return jnp.concatenate([scaled_residual, scaled_behind[None]], axis=0)


def smooth_rims(density_raw, slices_dev, rows_dev):
    depth_count = lax.axis_size("depth")
    rows_count = lax.axis_size("rows")
    depth_at = lax.axis_index("depth")
    rows_at = lax.axis_index("rows")
    up_d = [(i, i + 1) for i in range(depth_count - 1)]
    up_r = [(i, i + 1) for i in range(rows_count - 1)]
    first_slice = density_raw[:1]
    last_slice = density_raw[-1:]
    first_row = density_raw[:, :1]
    last_row = density_raw[:, -1:]
    prev_slice = lax.ppermute(last_slice, "depth", up_d)
    next_slice = lax.ppermute(first_slice, "depth", [(j, i) for i, j in up_d])
    prev_row = lax.ppermute(last_row, "rows", up_r)
    next_row = lax.ppermute(first_row, "rows", [(j, i) for i, j in up_r])
    prev_slice = jnp.where(depth_at > 0, prev_slice, first_slice)
    next_slice = jnp.where(depth_at < depth_count - 1, next_slice, last_slice)
    prev_row = jnp.where(rows_at > 0, prev_row, first_row)
    next_row = jnp.where(rows_at < rows_count - 1, next_row, last_row)
    dense = density_raw.astype(jnp.float32)
    below = jnp.concatenate([prev_slice, density_raw[:-1]], axis=0).astype(jnp.float32)
    above = jnp.concatenate([density_raw[1:], next_slice], axis=0).astype(jnp.float32)
    upper = jnp.concatenate([prev_row, density_raw[:, :-1]], axis=1).astype(jnp.float32)
    lower = jnp.concatenate([density_raw[:, 1:], next_row], axis=1).astype(jnp.float32)
    return 2.0 * smooth_weight * ((dense - below) + (dense - above) + (dense - upper) + (dense - lower))


def local(density_raw, colour_raw, target, slab_rank):
    slices_dev, rows_dev, width = density_raw.shape
    depth_count = lax.axis_size("depth")
    slices_total = slices_dev * depth_count
    step = optical_depth / slices_total
    pixels = rows_dev * width
    chunk = pixels // depth_count
    partial_value = forward_partial(density_raw, colour_raw, step)
    sent = partial_value.reshape(4, depth_count, chunk)
    received = lax.all_to_all(sent, "depth", 1, 1, tiled=True)
    position = lax.axis_index("depth")
    target_piece = lax.dynamic_slice_in_dim(target.reshape(3, pixels), position * chunk, chunk, axis=1)
    answers = composite(received, slab_rank, target_piece)
    returned = lax.all_to_all(answers, "depth", 1, 1, tiled=True)
    returned = returned.reshape(4, rows_dev, width)
    smooth = smooth_rims(density_raw, slices_dev, rows_dev)
    return backward_grads(density_raw, colour_raw, partial_value, returned, smooth, step, slices_total)


def solution(mesh):
    placed = (P("depth", "rows", None), P(None, "depth", "rows", None), P(None, "rows", None), P())
    return jax.shard_map(
        local,
        mesh=mesh,
        in_specs=placed,
        out_specs=(P("depth", "rows", None), P(None, "depth", "rows", None)),
        check_vma=False,
    )
```

```python
import functools

import jax
import jax.numpy as jnp
from jax import lax
from jax.experimental import pallas as pl
from jax.experimental.pallas import tpu as pltpu
from jax.sharding import PartitionSpec as P

optical_depth = 2.5
smooth_weight = 0.05
lanes = 128


def softplus(x):
    return jnp.maximum(x, 0.0) + jnp.log1p(jnp.exp(-jnp.abs(x)))


def chunking(rows, width, depth_count):
    tiles = width // lanes
    per_tile = max(depth_count // tiles, 1)
    return tiles, per_tile, rows // per_tile


def forward_kernel(d_ref, c_ref, out_ref, *, step):
    slices = d_ref.shape[0]
    shape = d_ref.shape[1:]
    per_tile, _, chunk_rows, _ = out_ref.shape

    def body(z, carry):
        acc, e0, e1, e2 = carry
        dt = step * softplus(d_ref[z].astype(jnp.float32))
        opacity = 1.0 - jnp.exp(-dt)
        lit = jnp.exp(-acc) * opacity
        e0 = e0 + lit * jax.nn.sigmoid(c_ref[0, z].astype(jnp.float32))
        e1 = e1 + lit * jax.nn.sigmoid(c_ref[1, z].astype(jnp.float32))
        e2 = e2 + lit * jax.nn.sigmoid(c_ref[2, z].astype(jnp.float32))
        return (acc + dt, e0, e1, e2)

    zero = jnp.zeros(shape, jnp.float32)
    acc, e0, e1, e2 = lax.fori_loop(0, slices, body, (zero, zero, zero, zero), unroll=4)
    values = (e0, e1, e2, jnp.exp(-acc))
    for g in range(per_tile):
        for c in range(4):
            out_ref[g, c] = values[c][g * chunk_rows:(g + 1) * chunk_rows]


def backward_kernel(
    d_ref, c_ref, part_ref, ans_ref, zhalo_ref, rhalo_ref, gd_ref, gc_ref, *, step, slices_total
):
    slices = d_ref.shape[0]
    shape = d_ref.shape[1:]
    per_tile = part_ref.shape[0]

    def pixel(ref, c):
        if per_tile == 1:
            return ref[0, c]
        return jnp.concatenate([ref[g, c] for g in range(per_tile)], axis=0)

    row = lax.broadcasted_iota(jnp.int32, shape, 0)
    first_row = row == 0
    last_row = row == shape[0] - 1

    def body(z, carry):
        acc, front, w0, w1, w2, d_prev, d = carry
        d_next = jnp.where(
            z + 1 < slices,
            d_ref[jnp.minimum(z + 1, slices - 1)].astype(jnp.float32),
            zhalo_ref[1],
        )
        rims = rhalo_ref[z]
        upper = jnp.where(first_row, rims[0:1], pltpu.roll(d, 1, 0))
        lower = jnp.where(last_row, rims[1:2], pltpu.roll(d, shape[0] - 1, 0))
        smooth = 2.0 * smooth_weight * ((d - d_prev) + (d - d_next) + (d - upper) + (d - lower))
        sp = softplus(d)
        dt = step * sp
        opacity = 1.0 - jnp.exp(-dt)
        acc_next = acc + dt
        through = jnp.exp(-acc_next)
        inv = 1.0 / through
        lit = front * opacity
        col = [jax.nn.sigmoid(c_ref[c, z].astype(jnp.float32)) for c in range(3)]
        w = [w0 + lit * col[0], w1 + lit * col[1], w2 + lit * col[2]]
        inner = -(pixel(part_ref, 3) * inv) * pixel(ans_ref, 3)
        for c in range(3):
            sr = pixel(ans_ref, c)
            inner = inner + sr * (col[c] - (pixel(part_ref, c) - w[c]) * inv)
            gc_ref[c, z] = slices_total * sr * lit * col[c] * (1.0 - col[c])
        gd_ref[z] = optical_depth * through * jnp.exp(d - sp) * inner + smooth
        return (acc_next, through, w[0], w[1], w[2], d, d_next)

    zero = jnp.zeros(shape, jnp.float32)
    one = jnp.ones(shape, jnp.float32)
    start = (zero, one, zero, zero, zero, zhalo_ref[0], d_ref[0].astype(jnp.float32))
    lax.fori_loop(0, slices, body, start, unroll=2)


def forward_partial(density, colour_raw, step, depth_count):
    slices, rows, width = density.shape
    tiles, per_tile, chunk_rows = chunking(rows, width, depth_count)
    return pl.pallas_call(
        functools.partial(forward_kernel, step=step),
        grid=(tiles,),
        in_specs=[
            pl.BlockSpec((slices, rows, lanes), lambda i: (0, 0, i)),
            pl.BlockSpec((3, slices, rows, lanes), lambda i: (0, 0, 0, i)),
        ],
        out_specs=pl.BlockSpec((per_tile, 4, chunk_rows, lanes), lambda i: (i, 0, 0, 0)),
        out_shape=jax.ShapeDtypeStruct((tiles * per_tile, 4, chunk_rows, lanes), jnp.float32),
    )(density, colour_raw)


def backward_grads(density, colour_raw, partial_value, answers, zhalo, rhalo, step, slices_total):
    slices, rows, width = density.shape
    per_tile, _, chunk_rows, _ = answers.shape
    per_tile = per_tile // (width // lanes)
    slab = pl.BlockSpec((slices, rows, lanes), lambda i: (0, 0, i))
    colours = pl.BlockSpec((3, slices, rows, lanes), lambda i: (0, 0, 0, i))
    pixel = pl.BlockSpec((per_tile, 4, chunk_rows, lanes), lambda i: (i, 0, 0, 0))
    return pl.pallas_call(
        functools.partial(backward_kernel, step=step, slices_total=float(slices_total)),
        grid=(width // lanes,),
        in_specs=[
            slab,
            colours,
            pixel,
            pixel,
            pl.BlockSpec((2, rows, lanes), lambda i: (0, 0, i)),
            pl.BlockSpec((slices, 2, lanes), lambda i: (0, 0, i)),
        ],
        out_specs=[slab, colours],
        out_shape=[
            jax.ShapeDtypeStruct((slices, rows, width), jnp.float32),
            jax.ShapeDtypeStruct((3, slices, rows, width), jnp.float32),
        ],
    )(density, colour_raw, partial_value, answers, zhalo, rhalo)


def composite(parts, slab_rank, target_piece):
    emitted, passing = (parts[:, :3], parts[:, 3])
    earlier = (slab_rank[None, :] < slab_rank[:, None]).astype(jnp.float32)[:, :, None, None]
    later = (slab_rank[None, :] > slab_rank[:, None]).astype(jnp.float32)[:, :, None, None, None]
    front = jnp.exp(jnp.sum(earlier * jnp.log(passing)[None], axis=1))
    weighted = front[:, None] * emitted
    behind = jnp.sum(later * weighted[None], axis=1) / (front * passing)[:, None]
    residual = jnp.sum(weighted, axis=0) - target_piece
    scaled_residual = front[:, None] * residual[None]
    scaled_behind = front * jnp.sum(residual[None] * behind, axis=1)
    return jnp.concatenate([scaled_residual, scaled_behind[:, None]], axis=1)


def halos(density_raw):
    depth_count = lax.axis_size("depth")
    rows_count = lax.axis_size("rows")
    depth_at = lax.axis_index("depth")
    rows_at = lax.axis_index("rows")
    up_d = [(i, i + 1) for i in range(depth_count - 1)]
    up_r = [(i, i + 1) for i in range(rows_count - 1)]
    first_slice = density_raw[:1]
    last_slice = density_raw[-1:]
    first_row = density_raw[:, :1]
    last_row = density_raw[:, -1:]
    prev_slice = lax.ppermute(last_slice, "depth", up_d)
    next_slice = lax.ppermute(first_slice, "depth", [(j, i) for i, j in up_d])
    prev_row = lax.ppermute(last_row, "rows", up_r)
    next_row = lax.ppermute(first_row, "rows", [(j, i) for i, j in up_r])
    prev_slice = jnp.where(depth_at > 0, prev_slice, first_slice)
    next_slice = jnp.where(depth_at < depth_count - 1, next_slice, last_slice)
    prev_row = jnp.where(rows_at > 0, prev_row, first_row)
    next_row = jnp.where(rows_at < rows_count - 1, next_row, last_row)
    zhalo = jnp.concatenate([prev_slice, next_slice], axis=0).astype(jnp.float32)
    rhalo = jnp.concatenate([prev_row, next_row], axis=1).astype(jnp.float32)
    return zhalo, rhalo


def local(density_raw, colour_raw, target, slab_rank):
    slices_dev, rows_dev, width = density_raw.shape
    depth_count = lax.axis_size("depth")
    slices_total = slices_dev * depth_count
    step = optical_depth / slices_total
    tiles, per_tile, chunk_rows = chunking(rows_dev, width, depth_count)
    zhalo, rhalo = halos(density_raw)
    partial_value = forward_partial(density_raw, colour_raw, step, depth_count)
    received = lax.all_to_all(partial_value, "depth", 0, 0, tiled=True)
    position = lax.axis_index("depth")
    target_piece = lax.dynamic_slice(
        target,
        (0, (position % per_tile) * chunk_rows, (position // per_tile) * lanes),
        (3, chunk_rows, lanes),
    )
    answers = composite(received, slab_rank, target_piece)
    returned = lax.all_to_all(answers, "depth", 0, 0, tiled=True)
    return backward_grads(
        density_raw, colour_raw, partial_value, returned, zhalo, rhalo, step, slices_total
    )


def solution(mesh):
    placed = (P("depth", "rows", None), P(None, "depth", "rows", None), P(None, "rows", None), P())
    return jax.shard_map(
        local,
        mesh=mesh,
        in_specs=placed,
        out_specs=(P("depth", "rows", None), P(None, "depth", "rows", None)),
        check_vma=False,
    )
```

```python
import functools

import jax
import jax.numpy as jnp
from jax import lax
from jax.experimental import pallas as pl
from jax.experimental.pallas import tpu as pltpu
from jax.sharding import PartitionSpec as P

optical_depth = 2.5
smooth_weight = 0.05
lanes = 128


log2e = 1.4426950408889634
ln2 = 0.6931471805599453


def softplus(x):
    return jnp.maximum(x, 0.0) + ln2 * jnp.log2(1.0 + jnp.exp2(jnp.abs(x) * -log2e))


def chunking(rows, width, depth_count):
    tiles = width // lanes
    per_tile = max(depth_count // tiles, 1)
    return tiles, per_tile, rows // per_tile


def forward_kernel(d_ref, c_ref, out_ref, *, step):
    slices = d_ref.shape[0]
    shape = d_ref.shape[1:]
    per_tile, _, chunk_rows, _ = out_ref.shape
    scale = -step * log2e

    def body(z, carry):
        n, front, e0, e1, e2 = carry
        dtn = softplus(d_ref[z].astype(jnp.float32)) * scale
        lit = front * (1.0 - jnp.exp2(dtn))
        n = n + dtn
        e0 = e0 + lit * jax.nn.sigmoid(c_ref[0, z].astype(jnp.float32))
        e1 = e1 + lit * jax.nn.sigmoid(c_ref[1, z].astype(jnp.float32))
        e2 = e2 + lit * jax.nn.sigmoid(c_ref[2, z].astype(jnp.float32))
        return (n, jnp.exp2(n), e0, e1, e2)

    zero = jnp.zeros(shape, jnp.float32)
    one = jnp.ones(shape, jnp.float32)
    _, passing, e0, e1, e2 = lax.fori_loop(0, slices, body, (zero, one, zero, zero, zero), unroll=4)
    values = (e0, e1, e2, passing)
    for g in range(per_tile):
        for c in range(4):
            out_ref[g, c] = values[c][g * chunk_rows:(g + 1) * chunk_rows]


def backward_kernel(d_ref, c_ref, ans_ref, zhalo_ref, rhalo_ref, gd_ref, gc_ref, *, step, slices_total):
    slices = d_ref.shape[0]
    shape = d_ref.shape[1:]
    per_tile = ans_ref.shape[0]
    scale = -step * log2e
    gain = optical_depth / slices_total

    def pixel(ref, c):
        if per_tile == 1:
            return ref[0, c]
        return jnp.concatenate([ref[g, c] for g in range(per_tile)], axis=0)

    row = lax.broadcasted_iota(jnp.int32, shape, 0)
    first_row = row == 0
    last_row = row == shape[0] - 1

    def body(z, carry):
        n, front, w0, w1, w2, d_prev, d = carry
        d_next = jnp.where(
            z + 1 < slices,
            d_ref[jnp.minimum(z + 1, slices - 1)].astype(jnp.float32),
            zhalo_ref[1],
        )
        rims = rhalo_ref[z]
        upper = jnp.where(first_row, rims[0:1], pltpu.roll(d, 1, 0))
        lower = jnp.where(last_row, rims[1:2], pltpu.roll(d, shape[0] - 1, 0))
        smooth = 2.0 * smooth_weight * ((d - d_prev) + (d - d_next) + (d - upper) + (d - lower))
        dtn = softplus(d) * scale
        lit = front * (1.0 - jnp.exp2(dtn))
        n_next = n + dtn
        through = jnp.exp2(n_next)
        inv = jnp.exp2(-n_next)
        col = [jax.nn.sigmoid(c_ref[c, z].astype(jnp.float32)) for c in range(3)]
        lit_col = [lit * col[c] for c in range(3)]
        w = [w0 + lit_col[0], w1 + lit_col[1], w2 + lit_col[2]]
        res = [pixel(ans_ref, c) for c in range(3)]
        emitted = res[0] * col[0] + res[1] * col[1] + res[2] * col[2]
        left = res[0] * w[0] + res[1] * w[1] + res[2] * w[2]
        inner = emitted - inv * (pixel(ans_ref, 3) - left)
        for c in range(3):
            gc_ref[c, z] = res[c] * lit_col[c] * (1.0 - col[c])
        gd_ref[z] = gain * through * jax.nn.sigmoid(d) * inner + smooth
        return (n_next, through, w[0], w[1], w[2], d, d_next)

    zero = jnp.zeros(shape, jnp.float32)
    one = jnp.ones(shape, jnp.float32)
    start = (zero, one, zero, zero, zero, zhalo_ref[0], d_ref[0].astype(jnp.float32))
    lax.fori_loop(0, slices, body, start, unroll=2)


def forward_partial(density, colour_raw, step, depth_count):
    slices, rows, width = density.shape
    tiles, per_tile, chunk_rows = chunking(rows, width, depth_count)
    return pl.pallas_call(
        functools.partial(forward_kernel, step=step),
        grid=(tiles,),
        in_specs=[
            pl.BlockSpec((slices, rows, lanes), lambda i: (0, 0, i)),
            pl.BlockSpec((3, slices, rows, lanes), lambda i: (0, 0, 0, i)),
        ],
        out_specs=pl.BlockSpec((per_tile, 4, chunk_rows, lanes), lambda i: (i, 0, 0, 0)),
        out_shape=jax.ShapeDtypeStruct((tiles * per_tile, 4, chunk_rows, lanes), jnp.float32),
    )(density, colour_raw)


def backward_grads(density, colour_raw, answers, zhalo, rhalo, step, slices_total):
    slices, rows, width = density.shape
    per_tile, _, chunk_rows, _ = answers.shape
    per_tile = per_tile // (width // lanes)
    slab = pl.BlockSpec((slices, rows, lanes), lambda i: (0, 0, i))
    colours = pl.BlockSpec((3, slices, rows, lanes), lambda i: (0, 0, 0, i))
    pixel = pl.BlockSpec((per_tile, 4, chunk_rows, lanes), lambda i: (i, 0, 0, 0))
    return pl.pallas_call(
        functools.partial(backward_kernel, step=step, slices_total=float(slices_total)),
        grid=(width // lanes,),
        in_specs=[
            slab,
            colours,
            pixel,
            pl.BlockSpec((2, rows, lanes), lambda i: (0, 0, i)),
            pl.BlockSpec((slices, 2, lanes), lambda i: (0, 0, i)),
        ],
        out_specs=[slab, colours],
        out_shape=[
            jax.ShapeDtypeStruct((slices, rows, width), jnp.float32),
            jax.ShapeDtypeStruct((3, slices, rows, width), jnp.float32),
        ],
    )(density, colour_raw, answers, zhalo, rhalo)


def composite(parts, slab_rank, target_piece, slices_total):
    emitted, passing = (parts[:, :3], parts[:, 3])
    earlier = (slab_rank[None, :] < slab_rank[:, None]).astype(jnp.float32)[:, :, None, None]
    later = (slab_rank[None, :] > slab_rank[:, None]).astype(jnp.float32)[:, :, None, None, None]
    front = jnp.exp(jnp.sum(earlier * jnp.log(passing)[None], axis=1))
    weighted = front[:, None] * emitted
    behind = jnp.sum(later * weighted[None], axis=1) / (front * passing)[:, None]
    residual = jnp.sum(weighted, axis=0) - target_piece
    scaled_residual = slices_total * (front[:, None] * residual[None])
    scaled_behind = slices_total * (front * jnp.sum(residual[None] * behind, axis=1))
    folded = jnp.sum(scaled_residual * emitted, axis=1) + passing * scaled_behind
    return jnp.concatenate([scaled_residual, folded[:, None]], axis=1)


def halos(density_raw):
    depth_count = lax.axis_size("depth")
    rows_count = lax.axis_size("rows")
    depth_at = lax.axis_index("depth")
    rows_at = lax.axis_index("rows")
    up_d = [(i, i + 1) for i in range(depth_count - 1)]
    up_r = [(i, i + 1) for i in range(rows_count - 1)]
    first_slice = density_raw[:1]
    last_slice = density_raw[-1:]
    first_row = density_raw[:, :1]
    last_row = density_raw[:, -1:]
    prev_slice = lax.ppermute(last_slice, "depth", up_d)
    next_slice = lax.ppermute(first_slice, "depth", [(j, i) for i, j in up_d])
    prev_row = lax.ppermute(last_row, "rows", up_r)
    next_row = lax.ppermute(first_row, "rows", [(j, i) for i, j in up_r])
    prev_slice = jnp.where(depth_at > 0, prev_slice, first_slice)
    next_slice = jnp.where(depth_at < depth_count - 1, next_slice, last_slice)
    prev_row = jnp.where(rows_at > 0, prev_row, first_row)
    next_row = jnp.where(rows_at < rows_count - 1, next_row, last_row)
    zhalo = jnp.concatenate([prev_slice, next_slice], axis=0).astype(jnp.float32)
    rhalo = jnp.concatenate([prev_row, next_row], axis=1).astype(jnp.float32)
    return zhalo, rhalo


def local(density_raw, colour_raw, target, slab_rank):
    slices_dev, rows_dev, width = density_raw.shape
    depth_count = lax.axis_size("depth")
    slices_total = slices_dev * depth_count
    step = optical_depth / slices_total
    tiles, per_tile, chunk_rows = chunking(rows_dev, width, depth_count)
    zhalo, rhalo = halos(density_raw)
    partial_value = forward_partial(density_raw, colour_raw, step, depth_count)
    received = lax.all_to_all(partial_value, "depth", 0, 0, tiled=True)
    position = lax.axis_index("depth")
    target_piece = lax.dynamic_slice(
        target,
        (0, (position % per_tile) * chunk_rows, (position // per_tile) * lanes),
        (3, chunk_rows, lanes),
    )
    answers = composite(received, slab_rank, target_piece, float(slices_total))
    returned = lax.all_to_all(answers, "depth", 0, 0, tiled=True)
    return backward_grads(
        density_raw, colour_raw, returned, zhalo, rhalo, step, slices_total
    )


def solution(mesh):
    placed = (P("depth", "rows", None), P(None, "depth", "rows", None), P(None, "rows", None), P())
    return jax.shard_map(
        local,
        mesh=mesh,
        in_specs=placed,
        out_specs=(P("depth", "rows", None), P(None, "depth", "rows", None)),
        check_vma=False,
    )
```

```python
import functools

import jax
import jax.numpy as jnp
from jax import lax
from jax.experimental import pallas as pl
from jax.experimental.pallas import tpu as pltpu
from jax.sharding import PartitionSpec as P

optical_depth = 2.5
smooth_weight = 0.05
lanes = 128


log2e = 1.4426950408889634
ln2 = 0.6931471805599453


def softplus(x):
    return jnp.maximum(x, 0.0) + ln2 * jnp.log2(1.0 + jnp.exp2(jnp.abs(x) * -log2e))


def chunking(rows, width, depth_count):
    tiles = width // lanes
    per_tile = max(depth_count // tiles, 1)
    return tiles, per_tile, rows // per_tile


def forward_kernel(d_ref, c_ref, out_ref, *, step):
    slices = d_ref.shape[0]
    shape = d_ref.shape[1:]
    per_tile, _, chunk_rows, _ = out_ref.shape
    scale = -step * log2e

    def body(z, carry):
        n, front, e0, e1, e2 = carry
        dtn = softplus(d_ref[z].astype(jnp.float32)) * scale
        lit = front * (1.0 - jnp.exp2(dtn))
        n = n + dtn
        e0 = e0 + lit * jax.nn.sigmoid(c_ref[0, z].astype(jnp.float32))
        e1 = e1 + lit * jax.nn.sigmoid(c_ref[1, z].astype(jnp.float32))
        e2 = e2 + lit * jax.nn.sigmoid(c_ref[2, z].astype(jnp.float32))
        return (n, jnp.exp2(n), e0, e1, e2)

    zero = jnp.zeros(shape, jnp.float32)
    one = jnp.ones(shape, jnp.float32)
    _, passing, e0, e1, e2 = lax.fori_loop(0, slices, body, (zero, one, zero, zero, zero), unroll=4)
    values = (e0, e1, e2, passing)
    for g in range(per_tile):
        for c in range(4):
            out_ref[g, c] = values[c][g * chunk_rows:(g + 1) * chunk_rows]


def backward_kernel(d_ref, c_ref, ans_ref, zhalo_ref, rhalo_ref, gd_ref, gc_ref, *, step, slices_total):
    slices = d_ref.shape[0]
    shape = d_ref.shape[1:]
    per_tile = ans_ref.shape[0]
    scale = -step * log2e
    gain = optical_depth / slices_total

    def pixel(ref, c):
        if per_tile == 1:
            return ref[0, c]
        return jnp.concatenate([ref[g, c] for g in range(per_tile)], axis=0)

    row = lax.broadcasted_iota(jnp.int32, shape, 0)
    first_row = row == 0
    last_row = row == shape[0] - 1

    def body(z, carry):
        n, front, w0, w1, w2, d_prev, d = carry
        d_next = jnp.where(
            z + 1 < slices,
            d_ref[jnp.minimum(z + 1, slices - 1)].astype(jnp.float32),
            zhalo_ref[1],
        )
        rims = rhalo_ref[z]
        upper = jnp.where(first_row, rims[0:1], pltpu.roll(d, 1, 0))
        lower = jnp.where(last_row, rims[1:2], pltpu.roll(d, shape[0] - 1, 0))
        smooth = 2.0 * smooth_weight * ((d - d_prev) + (d - d_next) + (d - upper) + (d - lower))
        dtn = softplus(d) * scale
        lit = front * (1.0 - jnp.exp2(dtn))
        n_next = n + dtn
        through = jnp.exp2(n_next)
        inv = jnp.exp2(-n_next)
        col = [jax.nn.sigmoid(c_ref[c, z].astype(jnp.float32)) for c in range(3)]
        lit_col = [lit * col[c] for c in range(3)]
        w = [w0 + lit_col[0], w1 + lit_col[1], w2 + lit_col[2]]
        res = [pixel(ans_ref, c) for c in range(3)]
        emitted = res[0] * col[0] + res[1] * col[1] + res[2] * col[2]
        left = res[0] * w[0] + res[1] * w[1] + res[2] * w[2]
        inner = emitted - inv * (pixel(ans_ref, 3) - left)
        for c in range(3):
            gc_ref[c, z] = res[c] * lit_col[c] * (1.0 - col[c])
        gd_ref[z] = gain * through * jax.nn.sigmoid(d) * inner + smooth
        return (n_next, through, w[0], w[1], w[2], d, d_next)

    zero = jnp.zeros(shape, jnp.float32)
    one = jnp.ones(shape, jnp.float32)
    start = (zero, one, zero, zero, zero, zhalo_ref[0], d_ref[0].astype(jnp.float32))
    lax.fori_loop(0, slices, body, start, unroll=2)


def forward_partial(density, colour_raw, step, depth_count):
    slices, rows, width = density.shape
    tiles, per_tile, chunk_rows = chunking(rows, width, depth_count)
    return pl.pallas_call(
        functools.partial(forward_kernel, step=step),
        grid=(tiles,),
        in_specs=[
            pl.BlockSpec((slices, rows, lanes), lambda i: (0, 0, i)),
            pl.BlockSpec((3, slices, rows, lanes), lambda i: (0, 0, 0, i)),
        ],
        out_specs=pl.BlockSpec((per_tile, 4, chunk_rows, lanes), lambda i: (i, 0, 0, 0)),
        out_shape=jax.ShapeDtypeStruct((tiles * per_tile, 4, chunk_rows, lanes), jnp.float32),
    )(density, colour_raw)


def backward_grads(density, colour_raw, answers, zhalo, rhalo, step, slices_total):
    slices, rows, width = density.shape
    per_tile, _, chunk_rows, _ = answers.shape
    per_tile = per_tile // (width // lanes)
    slab = pl.BlockSpec((slices, rows, lanes), lambda i: (0, 0, i))
    colours = pl.BlockSpec((3, slices, rows, lanes), lambda i: (0, 0, 0, i))
    pixel = pl.BlockSpec((per_tile, 4, chunk_rows, lanes), lambda i: (i, 0, 0, 0))
    return pl.pallas_call(
        functools.partial(backward_kernel, step=step, slices_total=float(slices_total)),
        grid=(width // lanes,),
        in_specs=[
            slab,
            colours,
            pixel,
            pl.BlockSpec((2, rows, lanes), lambda i: (0, 0, i)),
            pl.BlockSpec((slices, 2, lanes), lambda i: (0, 0, i)),
        ],
        out_specs=[slab, colours],
        out_shape=[
            jax.ShapeDtypeStruct((slices, rows, width), jnp.float32),
            jax.ShapeDtypeStruct((3, slices, rows, width), jnp.float32),
        ],
    )(density, colour_raw, answers, zhalo, rhalo)


def composite(parts, slab_rank, target_piece, slices_total):
    emitted, passing = (parts[:, :3], parts[:, 3])
    earlier = (slab_rank[None, :] < slab_rank[:, None]).astype(jnp.float32)[:, :, None, None]
    later = (slab_rank[None, :] > slab_rank[:, None]).astype(jnp.float32)[:, :, None, None, None]
    front = jnp.exp(jnp.sum(earlier * jnp.log(passing)[None], axis=1))
    weighted = front[:, None] * emitted
    behind = jnp.sum(later * weighted[None], axis=1) / (front * passing)[:, None]
    residual = jnp.sum(weighted, axis=0) - target_piece
    scaled_residual = slices_total * (front[:, None] * residual[None])
    scaled_behind = slices_total * (front * jnp.sum(residual[None] * behind, axis=1))
    folded = jnp.sum(scaled_residual * emitted, axis=1) + passing * scaled_behind
    return jnp.concatenate([scaled_residual, folded[:, None]], axis=1)


def halos(density_raw):
    depth_count = lax.axis_size("depth")
    rows_count = lax.axis_size("rows")
    depth_at = lax.axis_index("depth")
    rows_at = lax.axis_index("rows")
    up_d = [(i, i + 1) for i in range(depth_count - 1)]
    up_r = [(i, i + 1) for i in range(rows_count - 1)]
    first_slice = density_raw[:1]
    last_slice = density_raw[-1:]
    first_row = density_raw[:, :1]
    last_row = density_raw[:, -1:]
    prev_slice = lax.ppermute(last_slice, "depth", up_d)
    next_slice = lax.ppermute(first_slice, "depth", [(j, i) for i, j in up_d])
    prev_row = lax.ppermute(last_row, "rows", up_r)
    next_row = lax.ppermute(first_row, "rows", [(j, i) for i, j in up_r])
    prev_slice = jnp.where(depth_at > 0, prev_slice, first_slice)
    next_slice = jnp.where(depth_at < depth_count - 1, next_slice, last_slice)
    prev_row = jnp.where(rows_at > 0, prev_row, first_row)
    next_row = jnp.where(rows_at < rows_count - 1, next_row, last_row)
    zhalo = jnp.concatenate([prev_slice, next_slice], axis=0).astype(jnp.float32)
    rhalo = jnp.concatenate([prev_row, next_row], axis=1).astype(jnp.float32)
    return zhalo, rhalo


def local(density_raw, colour_raw, target, slab_rank):
    slices_dev, rows_dev, width = density_raw.shape
    depth_count = lax.axis_size("depth")
    slices_total = slices_dev * depth_count
    step = optical_depth / slices_total
    tiles, per_tile, chunk_rows = chunking(rows_dev, width, depth_count)
    partial_value = forward_partial(density_raw, colour_raw, step, depth_count)
    partial_value, after_forward = lax.optimization_barrier((partial_value, density_raw))
    zhalo, rhalo = halos(after_forward)
    received = lax.all_to_all(partial_value, "depth", 0, 0, tiled=True)
    position = lax.axis_index("depth")
    target_piece = lax.dynamic_slice(
        target,
        (0, (position % per_tile) * chunk_rows, (position // per_tile) * lanes),
        (3, chunk_rows, lanes),
    )
    answers = composite(received, slab_rank, target_piece, float(slices_total))
    returned = lax.all_to_all(answers, "depth", 0, 0, tiled=True)
    return backward_grads(
        density_raw, colour_raw, returned, zhalo, rhalo, step, slices_total
    )


def solution(mesh):
    placed = (P("depth", "rows", None), P(None, "depth", "rows", None), P(None, "rows", None), P())
    return jax.shard_map(
        local,
        mesh=mesh,
        in_specs=placed,
        out_specs=(P("depth", "rows", None), P(None, "depth", "rows", None)),
        check_vma=False,
    )
```

```python
import functools

import jax
import jax.numpy as jnp
from jax import lax
from jax.experimental import pallas as pl
from jax.experimental.pallas import tpu as pltpu
from jax.sharding import PartitionSpec as P

optical_depth = 2.5
smooth_weight = 0.05
lanes = 128


log2e = 1.4426950408889634
ln2 = 0.6931471805599453


def softplus(x):
    return jnp.maximum(x, 0.0) + ln2 * jnp.log2(1.0 + jnp.exp2(jnp.abs(x) * -log2e))


def chunking(rows, width, depth_count):
    tiles = width // lanes
    per_tile = max(depth_count // tiles, 1)
    return tiles, per_tile, rows // per_tile


def forward_kernel(d_ref, c_ref, out_ref, *, step):
    slices = d_ref.shape[0]
    shape = d_ref.shape[1:]
    per_tile, _, chunk_rows, _ = out_ref.shape
    scale = -step * log2e

    def body(z, carry):
        n, front, e0, e1, e2 = carry
        dtn = softplus(d_ref[z].astype(jnp.float32)) * scale
        lit = front * (1.0 - jnp.exp2(dtn))
        n = n + dtn
        e0 = e0 + lit * jax.nn.sigmoid(c_ref[0, z].astype(jnp.float32))
        e1 = e1 + lit * jax.nn.sigmoid(c_ref[1, z].astype(jnp.float32))
        e2 = e2 + lit * jax.nn.sigmoid(c_ref[2, z].astype(jnp.float32))
        return (n, jnp.exp2(n), e0, e1, e2)

    zero = jnp.zeros(shape, jnp.float32)
    one = jnp.ones(shape, jnp.float32)
    _, passing, e0, e1, e2 = lax.fori_loop(0, slices, body, (zero, one, zero, zero, zero), unroll=4)
    values = (e0, e1, e2, passing)
    for g in range(per_tile):
        for c in range(4):
            out_ref[g, c] = values[c][g * chunk_rows:(g + 1) * chunk_rows]


def backward_kernel(d_ref, c_ref, ans_ref, zhalo_ref, rhalo_ref, gd_ref, gc_ref, *, step, slices_total):
    slices = d_ref.shape[0]
    shape = d_ref.shape[1:]
    per_tile = ans_ref.shape[0]
    scale = -step * log2e
    gain = optical_depth / slices_total

    def pixel(ref, c):
        if per_tile == 1:
            return ref[0, c]
        return jnp.concatenate([ref[g, c] for g in range(per_tile)], axis=0)

    row = lax.broadcasted_iota(jnp.int32, shape, 0)
    first_row = row == 0
    last_row = row == shape[0] - 1

    def body(z, carry):
        n, front, w0, w1, w2, d_prev, d = carry
        d_next = jnp.where(
            z + 1 < slices,
            d_ref[jnp.minimum(z + 1, slices - 1)].astype(jnp.float32),
            zhalo_ref[1],
        )
        rims = rhalo_ref[z]
        upper = jnp.where(first_row, rims[0:1], pltpu.roll(d, 1, 0))
        lower = jnp.where(last_row, rims[1:2], pltpu.roll(d, shape[0] - 1, 0))
        smooth = 2.0 * smooth_weight * ((d - d_prev) + (d - d_next) + (d - upper) + (d - lower))
        dtn = softplus(d) * scale
        lit = front * (1.0 - jnp.exp2(dtn))
        n_next = n + dtn
        through = jnp.exp2(n_next)
        inv = jnp.exp2(-n_next)
        col = [jax.nn.sigmoid(c_ref[c, z].astype(jnp.float32)) for c in range(3)]
        lit_col = [lit * col[c] for c in range(3)]
        w = [w0 + lit_col[0], w1 + lit_col[1], w2 + lit_col[2]]
        res = [pixel(ans_ref, c) for c in range(3)]
        emitted = res[0] * col[0] + res[1] * col[1] + res[2] * col[2]
        left = res[0] * w[0] + res[1] * w[1] + res[2] * w[2]
        inner = emitted - inv * (pixel(ans_ref, 3) - left)
        for c in range(3):
            gc_ref[c, z] = res[c] * lit_col[c] * (1.0 - col[c])
        gd_ref[z] = gain * through * jax.nn.sigmoid(d) * inner + smooth
        return (n_next, through, w[0], w[1], w[2], d, d_next)

    zero = jnp.zeros(shape, jnp.float32)
    one = jnp.ones(shape, jnp.float32)
    start = (zero, one, zero, zero, zero, zhalo_ref[0], d_ref[0].astype(jnp.float32))
    lax.fori_loop(0, slices, body, start, unroll=2)


def forward_partial(density, colour_raw, step, depth_count):
    slices, rows, width = density.shape
    tiles, per_tile, chunk_rows = chunking(rows, width, depth_count)
    return pl.pallas_call(
        functools.partial(forward_kernel, step=step),
        grid=(tiles,),
        in_specs=[
            pl.BlockSpec((slices, rows, lanes), lambda i: (0, 0, i)),
            pl.BlockSpec((3, slices, rows, lanes), lambda i: (0, 0, 0, i)),
        ],
        out_specs=pl.BlockSpec((per_tile, 4, chunk_rows, lanes), lambda i: (i, 0, 0, 0)),
        out_shape=jax.ShapeDtypeStruct((tiles * per_tile, 4, chunk_rows, lanes), jnp.float32),
    )(density, colour_raw)


def backward_grads(density, colour_raw, answers, zhalo, rhalo, step, slices_total):
    slices, rows, width = density.shape
    per_tile, _, chunk_rows, _ = answers.shape
    per_tile = per_tile // (width // lanes)
    slab = pl.BlockSpec((slices, rows, lanes), lambda i: (0, 0, i))
    colours = pl.BlockSpec((3, slices, rows, lanes), lambda i: (0, 0, 0, i))
    pixel = pl.BlockSpec((per_tile, 4, chunk_rows, lanes), lambda i: (i, 0, 0, 0))
    return pl.pallas_call(
        functools.partial(backward_kernel, step=step, slices_total=float(slices_total)),
        grid=(width // lanes,),
        in_specs=[
            slab,
            colours,
            pixel,
            pl.BlockSpec((2, rows, lanes), lambda i: (0, 0, i)),
            pl.BlockSpec((slices, 2, lanes), lambda i: (0, 0, i)),
        ],
        out_specs=[slab, colours],
        out_shape=[
            jax.ShapeDtypeStruct((slices, rows, width), jnp.float32),
            jax.ShapeDtypeStruct((3, slices, rows, width), jnp.float32),
        ],
    )(density, colour_raw, answers, zhalo, rhalo)


def composite(parts, slab_rank, target_piece, slices_total):
    emitted, passing = (parts[:, :3], parts[:, 3])
    earlier = (slab_rank[None, :] < slab_rank[:, None]).astype(jnp.float32)[:, :, None, None]
    later = (slab_rank[None, :] > slab_rank[:, None]).astype(jnp.float32)[:, :, None, None, None]
    front = jnp.exp(jnp.sum(earlier * jnp.log(passing)[None], axis=1))
    weighted = front[:, None] * emitted
    behind = jnp.sum(later * weighted[None], axis=1) / (front * passing)[:, None]
    residual = jnp.sum(weighted, axis=0) - target_piece
    scaled_residual = slices_total * (front[:, None] * residual[None])
    scaled_behind = slices_total * (front * jnp.sum(residual[None] * behind, axis=1))
    folded = jnp.sum(scaled_residual * emitted, axis=1) + passing * scaled_behind
    return jnp.concatenate([scaled_residual, folded[:, None]], axis=1)


def halos(density_raw):
    depth_count = lax.axis_size("depth")
    rows_count = lax.axis_size("rows")
    depth_at = lax.axis_index("depth")
    rows_at = lax.axis_index("rows")
    up_d = [(i, i + 1) for i in range(depth_count - 1)]
    up_r = [(i, i + 1) for i in range(rows_count - 1)]
    first_slice = density_raw[:1]
    last_slice = density_raw[-1:]
    first_row = density_raw[:, :1]
    last_row = density_raw[:, -1:]
    prev_slice = lax.ppermute(last_slice, "depth", up_d)
    next_slice = lax.ppermute(first_slice, "depth", [(j, i) for i, j in up_d])
    prev_row = lax.ppermute(last_row, "rows", up_r)
    next_row = lax.ppermute(first_row, "rows", [(j, i) for i, j in up_r])
    prev_slice = jnp.where(depth_at > 0, prev_slice, first_slice)
    next_slice = jnp.where(depth_at < depth_count - 1, next_slice, last_slice)
    prev_row = jnp.where(rows_at > 0, prev_row, first_row)
    next_row = jnp.where(rows_at < rows_count - 1, next_row, last_row)
    zhalo = jnp.concatenate([prev_slice, next_slice], axis=0).astype(jnp.float32)
    rhalo = jnp.concatenate([prev_row, next_row], axis=1).astype(jnp.float32)
    return zhalo, rhalo


def exchange(x, axis):
    count = lax.axis_size(axis)
    me = lax.axis_index(axis)
    result = lax.dynamic_update_index_in_dim(
        jnp.zeros_like(x), lax.dynamic_index_in_dim(x, me, 0, keepdims=True), me, 0
    )
    for shift in range(1, count):
        perm = [(i, (i + shift) % count) for i in range(count)]
        send = lax.dynamic_index_in_dim(x, (me + shift) % count, 0, keepdims=True)
        got = lax.ppermute(send, axis, perm)
        result = lax.dynamic_update_index_in_dim(result, got, (me + count - shift) % count, 0)
    return result


def local(density_raw, colour_raw, target, slab_rank):
    slices_dev, rows_dev, width = density_raw.shape
    depth_count = lax.axis_size("depth")
    slices_total = slices_dev * depth_count
    step = optical_depth / slices_total
    tiles, per_tile, chunk_rows = chunking(rows_dev, width, depth_count)
    partial_value = forward_partial(density_raw, colour_raw, step, depth_count)
    partial_value, after_forward = lax.optimization_barrier((partial_value, density_raw))
    zhalo, rhalo = halos(after_forward)
    received = exchange(partial_value, "depth")
    position = lax.axis_index("depth")
    target_piece = lax.dynamic_slice(
        target,
        (0, (position % per_tile) * chunk_rows, (position // per_tile) * lanes),
        (3, chunk_rows, lanes),
    )
    answers = composite(received, slab_rank, target_piece, float(slices_total))
    returned = exchange(answers, "depth")
    return backward_grads(
        density_raw, colour_raw, returned, zhalo, rhalo, step, slices_total
    )


def solution(mesh):
    placed = (P("depth", "rows", None), P(None, "depth", "rows", None), P(None, "rows", None), P())
    return jax.shard_map(
        local,
        mesh=mesh,
        in_specs=placed,
        out_specs=(P("depth", "rows", None), P(None, "depth", "rows", None)),
        check_vma=False,
    )
```

```python
import functools

import jax
import jax.numpy as jnp
from jax import lax
from jax.experimental import pallas as pl
from jax.experimental.pallas import tpu as pltpu
from jax.sharding import PartitionSpec as P

optical_depth = 2.5
smooth_weight = 0.05
lanes = 128


log2e = 1.4426950408889634
ln2 = 0.6931471805599453


def softplus(x):
    return jnp.maximum(x, 0.0) + ln2 * jnp.log2(1.0 + jnp.exp2(jnp.abs(x) * -log2e))


def chunking(rows, width, depth_count):
    tiles = width // lanes
    per_tile = max(depth_count // tiles, 1)
    return tiles, per_tile, rows // per_tile


def forward_kernel(d_ref, c_ref, out_ref, *, step):
    slices = d_ref.shape[0]
    shape = d_ref.shape[1:]
    per_tile, _, chunk_rows, _ = out_ref.shape
    scale = -step * log2e

    def body(z, carry):
        n, front, e0, e1, e2 = carry
        dtn = softplus(d_ref[z].astype(jnp.float32)) * scale
        kept = jnp.exp2(dtn)
        lit = front * (1.0 - kept)
        n = n + dtn
        e0 = e0 + lit * jax.nn.sigmoid(c_ref[0, z].astype(jnp.float32))
        e1 = e1 + lit * jax.nn.sigmoid(c_ref[1, z].astype(jnp.float32))
        e2 = e2 + lit * jax.nn.sigmoid(c_ref[2, z].astype(jnp.float32))
        return (n, front * kept, e0, e1, e2)

    zero = jnp.zeros(shape, jnp.float32)
    one = jnp.ones(shape, jnp.float32)
    n, _, e0, e1, e2 = lax.fori_loop(0, slices, body, (zero, one, zero, zero, zero), unroll=4)
    values = (e0, e1, e2, jnp.exp2(n))
    for g in range(per_tile):
        for c in range(4):
            out_ref[g, c] = values[c][g * chunk_rows:(g + 1) * chunk_rows]


def backward_kernel(d_ref, c_ref, ans_ref, zhalo_ref, rhalo_ref, gd_ref, gc_ref, *, step, slices_total):
    slices = d_ref.shape[0]
    shape = d_ref.shape[1:]
    per_tile = ans_ref.shape[0] // pl.num_programs(0)
    scale = -step * log2e
    gain = optical_depth / slices_total

    base = pl.program_id(0) * per_tile

    def pixel(ref, c):
        if per_tile == 1:
            return ref[base, c]
        return jnp.concatenate([ref[base + g, c] for g in range(per_tile)], axis=0)

    row = lax.broadcasted_iota(jnp.int32, shape, 0)
    first_row = row == 0
    last_row = row == shape[0] - 1

    def body(z, carry):
        n, front, w0, w1, w2, d_prev, d = carry
        d_next = jnp.where(
            z + 1 < slices,
            d_ref[jnp.minimum(z + 1, slices - 1)].astype(jnp.float32),
            zhalo_ref[1],
        )
        rims = rhalo_ref[z]
        upper = jnp.where(first_row, rims[0:1], pltpu.roll(d, 1, 0))
        lower = jnp.where(last_row, rims[1:2], pltpu.roll(d, shape[0] - 1, 0))
        smooth = 2.0 * smooth_weight * ((d - d_prev) + (d - d_next) + (d - upper) + (d - lower))
        dtn = softplus(d) * scale
        lit = front * (1.0 - jnp.exp2(dtn))
        n_next = n + dtn
        through = jnp.exp2(n_next)
        inv = jnp.exp2(-n_next)
        col = [jax.nn.sigmoid(c_ref[c, z].astype(jnp.float32)) for c in range(3)]
        lit_col = [lit * col[c] for c in range(3)]
        w = [w0 + lit_col[0], w1 + lit_col[1], w2 + lit_col[2]]
        res = [pixel(ans_ref, c) for c in range(3)]
        emitted = res[0] * col[0] + res[1] * col[1] + res[2] * col[2]
        left = res[0] * w[0] + res[1] * w[1] + res[2] * w[2]
        inner = emitted - inv * (pixel(ans_ref, 3) - left)
        for c in range(3):
            gc_ref[c, z] = res[c] * lit_col[c] * (1.0 - col[c])
        gd_ref[z] = gain * through * jax.nn.sigmoid(d) * inner + smooth
        return (n_next, through, w[0], w[1], w[2], d, d_next)

    zero = jnp.zeros(shape, jnp.float32)
    one = jnp.ones(shape, jnp.float32)
    start = (zero, one, zero, zero, zero, zhalo_ref[0], d_ref[0].astype(jnp.float32))
    lax.fori_loop(0, slices, body, start, unroll=2)


def forward_partial(density, colour_raw, step, depth_count):
    slices, rows, width = density.shape
    tiles, per_tile, chunk_rows = chunking(rows, width, depth_count)
    return pl.pallas_call(
        functools.partial(forward_kernel, step=step),
        grid=(tiles,),
        in_specs=[
            pl.BlockSpec((slices, rows, lanes), lambda i: (0, 0, i)),
            pl.BlockSpec((3, slices, rows, lanes), lambda i: (0, 0, 0, i)),
        ],
        out_specs=pl.BlockSpec((per_tile, 4, chunk_rows, lanes), lambda i: (i, 0, 0, 0)),
        out_shape=jax.ShapeDtypeStruct((tiles * per_tile, 4, chunk_rows, lanes), jnp.float32),
    )(density, colour_raw)


def backward_grads(density, colour_raw, answers, zhalo, rhalo, step, slices_total):
    slices, rows, width = density.shape
    per_tile, _, chunk_rows, _ = answers.shape
    per_tile = per_tile // (width // lanes)
    slab = pl.BlockSpec((slices, rows, lanes), lambda i: (0, 0, i))
    colours = pl.BlockSpec((3, slices, rows, lanes), lambda i: (0, 0, 0, i))
    pixel = pl.BlockSpec((per_tile, 4, chunk_rows, lanes), lambda i: (i, 0, 0, 0))
    return pl.pallas_call(
        functools.partial(backward_kernel, step=step, slices_total=float(slices_total)),
        grid=(width // lanes,),
        in_specs=[
            slab,
            colours,
            pl.BlockSpec(memory_space=pltpu.VMEM),
            pl.BlockSpec((2, rows, lanes), lambda i: (0, 0, i)),
            pl.BlockSpec((slices, 2, lanes), lambda i: (0, 0, i)),
        ],
        out_specs=[slab, colours],
        out_shape=[
            jax.ShapeDtypeStruct((slices, rows, width), jnp.float32),
            jax.ShapeDtypeStruct((3, slices, rows, width), jnp.float32),
        ],
    )(density, colour_raw, answers, zhalo, rhalo)


def composite(parts, slab_rank, target_piece, slices_total):
    emitted, passing = (parts[:, :3], parts[:, 3])
    earlier = (slab_rank[None, :] < slab_rank[:, None]).astype(jnp.float32)[:, :, None, None]
    later = (slab_rank[None, :] > slab_rank[:, None]).astype(jnp.float32)[:, :, None, None, None]
    front = jnp.exp(jnp.sum(earlier * jnp.log(passing)[None], axis=1))
    weighted = front[:, None] * emitted
    behind = jnp.sum(later * weighted[None], axis=1) / (front * passing)[:, None]
    residual = jnp.sum(weighted, axis=0) - target_piece
    scaled_residual = slices_total * (front[:, None] * residual[None])
    scaled_behind = slices_total * (front * jnp.sum(residual[None] * behind, axis=1))
    folded = jnp.sum(scaled_residual * emitted, axis=1) + passing * scaled_behind
    return jnp.concatenate([scaled_residual, folded[:, None]], axis=1)


def halos(density_raw):
    depth_count = lax.axis_size("depth")
    rows_count = lax.axis_size("rows")
    depth_at = lax.axis_index("depth")
    rows_at = lax.axis_index("rows")
    up_d = [(i, i + 1) for i in range(depth_count - 1)]
    up_r = [(i, i + 1) for i in range(rows_count - 1)]
    first_slice = density_raw[:1]
    last_slice = density_raw[-1:]
    first_row = density_raw[:, :1]
    last_row = density_raw[:, -1:]
    prev_slice = lax.ppermute(last_slice, "depth", up_d)
    next_slice = lax.ppermute(first_slice, "depth", [(j, i) for i, j in up_d])
    prev_row = lax.ppermute(last_row, "rows", up_r)
    next_row = lax.ppermute(first_row, "rows", [(j, i) for i, j in up_r])
    prev_slice = jnp.where(depth_at > 0, prev_slice, first_slice)
    next_slice = jnp.where(depth_at < depth_count - 1, next_slice, last_slice)
    prev_row = jnp.where(rows_at > 0, prev_row, first_row)
    next_row = jnp.where(rows_at < rows_count - 1, next_row, last_row)
    zhalo = jnp.concatenate([prev_slice, next_slice], axis=0).astype(jnp.float32)
    rhalo = jnp.concatenate([prev_row, next_row], axis=1).astype(jnp.float32)
    return zhalo, rhalo


def local(density_raw, colour_raw, target, slab_rank):
    slices_dev, rows_dev, width = density_raw.shape
    depth_count = lax.axis_size("depth")
    slices_total = slices_dev * depth_count
    step = optical_depth / slices_total
    tiles, per_tile, chunk_rows = chunking(rows_dev, width, depth_count)
    partial_value = forward_partial(density_raw, colour_raw, step, depth_count)
    partial_value, after_forward = lax.optimization_barrier((partial_value, density_raw))
    zhalo, rhalo = halos(after_forward)
    received = lax.all_to_all(partial_value, "depth", 0, 0, tiled=True)
    position = lax.axis_index("depth")
    target_piece = lax.dynamic_slice(
        target,
        (0, (position % per_tile) * chunk_rows, (position // per_tile) * lanes),
        (3, chunk_rows, lanes),
    )
    answers = composite(received, slab_rank, target_piece, float(slices_total))
    returned = lax.all_to_all(answers, "depth", 0, 0, tiled=True)
    return backward_grads(
        density_raw, colour_raw, returned, zhalo, rhalo, step, slices_total
    )


def solution(mesh):
    placed = (P("depth", "rows", None), P(None, "depth", "rows", None), P(None, "rows", None), P())
    return jax.shard_map(
        local,
        mesh=mesh,
        in_specs=placed,
        out_specs=(P("depth", "rows", None), P(None, "depth", "rows", None)),
        check_vma=False,
    )
```

```python
import functools

import jax
import jax.numpy as jnp
from jax import lax
from jax.experimental import pallas as pl
from jax.experimental.pallas import tpu as pltpu
from jax.sharding import PartitionSpec as P

optical_depth = 2.5
smooth_weight = 0.05
lanes = 128
forward_subs = 4
backward_subs = 2


log2e = 1.4426950408889634
ln2 = 0.6931471805599453


def softplus(x):
    return jnp.maximum(x, 0.0) + ln2 * jnp.log2(1.0 + jnp.exp2(jnp.abs(x) * -log2e))


def chunking(rows, width, depth_count):
    tiles = width // lanes
    per_tile = max(depth_count // tiles, 1)
    return tiles, per_tile, rows // per_tile


def forward_kernel(d_ref, c_ref, out_ref, *, step):
    slices, rows, block = d_ref.shape
    shape = (rows, lanes)
    subs = block // lanes
    per_tile = out_ref.shape[0] // subs
    chunk_rows = out_ref.shape[2]
    scale = -step * log2e

    for j in range(subs):
        cols = pl.ds(j * lanes, lanes)

        def body(z, carry):
            n, front, e0, e1, e2 = carry
            dtn = softplus(d_ref[z, :, cols].astype(jnp.float32)) * scale
            kept = jnp.exp2(dtn)
            lit = front * (1.0 - kept)
            n = n + dtn
            e0 = e0 + lit * jax.nn.sigmoid(c_ref[0, z, :, cols].astype(jnp.float32))
            e1 = e1 + lit * jax.nn.sigmoid(c_ref[1, z, :, cols].astype(jnp.float32))
            e2 = e2 + lit * jax.nn.sigmoid(c_ref[2, z, :, cols].astype(jnp.float32))
            return (n, front * kept, e0, e1, e2)

        zero = jnp.zeros(shape, jnp.float32)
        one = jnp.ones(shape, jnp.float32)
        n, _, e0, e1, e2 = lax.fori_loop(0, slices, body, (zero, one, zero, zero, zero), unroll=4)
        values = (e0, e1, e2, jnp.exp2(n))
        for g in range(per_tile):
            for c in range(4):
                out_ref[j * per_tile + g, c] = values[c][g * chunk_rows:(g + 1) * chunk_rows]


def backward_kernel(d_ref, c_ref, ans_ref, zhalo_ref, rhalo_ref, gd_ref, gc_ref, *, step, slices_total):
    slices, rows, block = d_ref.shape
    shape = (rows, lanes)
    subs = block // lanes
    per_tile = ans_ref.shape[0] // (pl.num_programs(0) * subs)
    scale = -step * log2e
    gain = optical_depth / slices_total
    row = lax.broadcasted_iota(jnp.int32, shape, 0)
    first_row = row == 0
    last_row = row == shape[0] - 1

    for j in range(subs):
        cols = pl.ds(j * lanes, lanes)
        base = (pl.program_id(0) * subs + j) * per_tile

        def pixel(c):
            if per_tile == 1:
                return ans_ref[base, c]
            return jnp.concatenate([ans_ref[base + g, c] for g in range(per_tile)], axis=0)

        def body(z, carry):
            n, front, w0, w1, w2, d_prev, d = carry
            d_next = jnp.where(
                z + 1 < slices,
                d_ref[jnp.minimum(z + 1, slices - 1), :, cols].astype(jnp.float32),
                zhalo_ref[1, :, cols],
            )
            rims = rhalo_ref[z, :, cols]
            upper = jnp.where(first_row, rims[0:1], pltpu.roll(d, 1, 0))
            lower = jnp.where(last_row, rims[1:2], pltpu.roll(d, shape[0] - 1, 0))
            smooth = 2.0 * smooth_weight * ((d - d_prev) + (d - d_next) + (d - upper) + (d - lower))
            dtn = softplus(d) * scale
            lit = front * (1.0 - jnp.exp2(dtn))
            n_next = n + dtn
            through = jnp.exp2(n_next)
            inv = jnp.exp2(-n_next)
            col = [jax.nn.sigmoid(c_ref[c, z, :, cols].astype(jnp.float32)) for c in range(3)]
            lit_col = [lit * col[c] for c in range(3)]
            w = [w0 + lit_col[0], w1 + lit_col[1], w2 + lit_col[2]]
            res = [pixel(c) for c in range(3)]
            emitted = res[0] * col[0] + res[1] * col[1] + res[2] * col[2]
            left = res[0] * w[0] + res[1] * w[1] + res[2] * w[2]
            inner = emitted - inv * (pixel(3) - left)
            for c in range(3):
                gc_ref[c, z, :, cols] = res[c] * lit_col[c] * (1.0 - col[c])
            gd_ref[z, :, cols] = gain * through * jax.nn.sigmoid(d) * inner + smooth
            return (n_next, through, w[0], w[1], w[2], d, d_next)

        zero = jnp.zeros(shape, jnp.float32)
        one = jnp.ones(shape, jnp.float32)
        start = (
            zero, one, zero, zero, zero,
            zhalo_ref[0, :, cols],
            d_ref[0, :, cols].astype(jnp.float32),
        )
        lax.fori_loop(0, slices, body, start, unroll=2)


def forward_partial(density, colour_raw, step, depth_count):
    slices, rows, width = density.shape
    tiles, per_tile, chunk_rows = chunking(rows, width, depth_count)
    block = lanes * forward_subs if tiles % forward_subs == 0 else lanes
    return pl.pallas_call(
        functools.partial(forward_kernel, step=step),
        grid=(width // block,),
        in_specs=[
            pl.BlockSpec((slices, rows, block), lambda i: (0, 0, i)),
            pl.BlockSpec((3, slices, rows, block), lambda i: (0, 0, 0, i)),
        ],
        out_specs=pl.BlockSpec(
            (per_tile * (block // lanes), 4, chunk_rows, lanes), lambda i: (i, 0, 0, 0)
        ),
        out_shape=jax.ShapeDtypeStruct((tiles * per_tile, 4, chunk_rows, lanes), jnp.float32),
    )(density, colour_raw)


def backward_grads(density, colour_raw, answers, zhalo, rhalo, step, slices_total):
    slices, rows, width = density.shape
    tiles = width // lanes
    block = lanes * backward_subs if tiles % backward_subs == 0 else lanes
    slab = pl.BlockSpec((slices, rows, block), lambda i: (0, 0, i))
    colours = pl.BlockSpec((3, slices, rows, block), lambda i: (0, 0, 0, i))
    return pl.pallas_call(
        functools.partial(backward_kernel, step=step, slices_total=float(slices_total)),
        grid=(width // block,),
        in_specs=[
            slab,
            colours,
            pl.BlockSpec(memory_space=pltpu.VMEM),
            pl.BlockSpec((2, rows, block), lambda i: (0, 0, i)),
            pl.BlockSpec((slices, 2, block), lambda i: (0, 0, i)),
        ],
        out_specs=[slab, colours],
        out_shape=[
            jax.ShapeDtypeStruct((slices, rows, width), jnp.float32),
            jax.ShapeDtypeStruct((3, slices, rows, width), jnp.float32),
        ],
    )(density, colour_raw, answers, zhalo, rhalo)


def composite(parts, slab_rank, target_piece, slices_total):
    emitted, passing = (parts[:, :3], parts[:, 3])
    earlier = (slab_rank[None, :] < slab_rank[:, None]).astype(jnp.float32)[:, :, None, None]
    later = (slab_rank[None, :] > slab_rank[:, None]).astype(jnp.float32)[:, :, None, None, None]
    front = jnp.exp(jnp.sum(earlier * jnp.log(passing)[None], axis=1))
    weighted = front[:, None] * emitted
    behind = jnp.sum(later * weighted[None], axis=1) / (front * passing)[:, None]
    residual = jnp.sum(weighted, axis=0) - target_piece
    scaled_residual = slices_total * (front[:, None] * residual[None])
    scaled_behind = slices_total * (front * jnp.sum(residual[None] * behind, axis=1))
    folded = jnp.sum(scaled_residual * emitted, axis=1) + passing * scaled_behind
    return jnp.concatenate([scaled_residual, folded[:, None]], axis=1)


def halos(density_raw):
    depth_count = lax.axis_size("depth")
    rows_count = lax.axis_size("rows")
    depth_at = lax.axis_index("depth")
    rows_at = lax.axis_index("rows")
    up_d = [(i, i + 1) for i in range(depth_count - 1)]
    up_r = [(i, i + 1) for i in range(rows_count - 1)]
    first_slice = density_raw[:1]
    last_slice = density_raw[-1:]
    first_row = density_raw[:, :1]
    last_row = density_raw[:, -1:]
    prev_slice = lax.ppermute(last_slice, "depth", up_d)
    next_slice = lax.ppermute(first_slice, "depth", [(j, i) for i, j in up_d])
    prev_row = lax.ppermute(last_row, "rows", up_r)
    next_row = lax.ppermute(first_row, "rows", [(j, i) for i, j in up_r])
    prev_slice = jnp.where(depth_at > 0, prev_slice, first_slice)
    next_slice = jnp.where(depth_at < depth_count - 1, next_slice, last_slice)
    prev_row = jnp.where(rows_at > 0, prev_row, first_row)
    next_row = jnp.where(rows_at < rows_count - 1, next_row, last_row)
    zhalo = jnp.concatenate([prev_slice, next_slice], axis=0).astype(jnp.float32)
    rhalo = jnp.concatenate([prev_row, next_row], axis=1).astype(jnp.float32)
    return zhalo, rhalo


def local(density_raw, colour_raw, target, slab_rank):
    slices_dev, rows_dev, width = density_raw.shape
    depth_count = lax.axis_size("depth")
    slices_total = slices_dev * depth_count
    step = optical_depth / slices_total
    tiles, per_tile, chunk_rows = chunking(rows_dev, width, depth_count)
    partial_value = forward_partial(density_raw, colour_raw, step, depth_count)
    partial_value, after_forward = lax.optimization_barrier((partial_value, density_raw))
    zhalo, rhalo = halos(after_forward)
    received = lax.all_to_all(partial_value, "depth", 0, 0, tiled=True)
    position = lax.axis_index("depth")
    target_piece = lax.dynamic_slice(
        target,
        (0, (position % per_tile) * chunk_rows, (position // per_tile) * lanes),
        (3, chunk_rows, lanes),
    )
    answers = composite(received, slab_rank, target_piece, float(slices_total))
    returned = lax.all_to_all(answers, "depth", 0, 0, tiled=True)
    return backward_grads(
        density_raw, colour_raw, returned, zhalo, rhalo, step, slices_total
    )


def solution(mesh):
    placed = (P("depth", "rows", None), P(None, "depth", "rows", None), P(None, "rows", None), P())
    return jax.shard_map(
        local,
        mesh=mesh,
        in_specs=placed,
        out_specs=(P("depth", "rows", None), P(None, "depth", "rows", None)),
        check_vma=False,
    )
```

```python
import functools

import jax
import jax.numpy as jnp
from jax import lax
from jax.experimental import pallas as pl
from jax.experimental.pallas import tpu as pltpu
from jax.sharding import PartitionSpec as P

optical_depth = 2.5
smooth_weight = 0.05
lanes = 128
forward_subs = 4
backward_subs = 2


log2e = 1.4426950408889634
ln2 = 0.6931471805599453


def softplus(x):
    return jnp.maximum(x, 0.0) + ln2 * jnp.log2(1.0 + jnp.exp2(jnp.abs(x) * -log2e))


def chunking(rows, width, depth_count):
    tiles = width // lanes
    per_tile = max(depth_count // tiles, 1)
    return tiles, per_tile, rows // per_tile


def forward_kernel(d_ref, c_ref, out_ref, *, step):
    slices, rows, block = d_ref.shape
    shape = (rows, lanes)
    subs = block // lanes
    per_tile = out_ref.shape[0] // subs
    chunk_rows = out_ref.shape[2]
    scale = -step * log2e

    for j in range(subs):
        cols = pl.ds(j * lanes, lanes)

        def body(z, carry):
            n, front, e0, e1, e2 = carry
            dtn = softplus(d_ref[z, :, cols].astype(jnp.float32)) * scale
            kept = jnp.exp2(dtn)
            lit = front * (1.0 - kept)
            n = n + dtn
            e0 = e0 + lit * jax.nn.sigmoid(c_ref[0, z, :, cols].astype(jnp.float32))
            e1 = e1 + lit * jax.nn.sigmoid(c_ref[1, z, :, cols].astype(jnp.float32))
            e2 = e2 + lit * jax.nn.sigmoid(c_ref[2, z, :, cols].astype(jnp.float32))
            return (n, front * kept, e0, e1, e2)

        zero = jnp.zeros(shape, jnp.float32)
        one = jnp.ones(shape, jnp.float32)
        n, _, e0, e1, e2 = lax.fori_loop(0, slices, body, (zero, one, zero, zero, zero), unroll=4)
        values = (e0, e1, e2, jnp.exp2(n))
        for g in range(per_tile):
            for c in range(4):
                out_ref[j * per_tile + g, c] = values[c][g * chunk_rows:(g + 1) * chunk_rows]


def backward_kernel(d_ref, c_ref, ans_ref, zhalo_ref, rhalo_ref, gd_ref, gc_ref, *, step, slices_total):
    slices, rows, block = d_ref.shape
    shape = (rows, lanes)
    subs = block // lanes
    per_tile = ans_ref.shape[0] // (pl.num_programs(0) * subs)
    scale = -step * log2e
    gain = optical_depth / slices_total
    row = lax.broadcasted_iota(jnp.int32, shape, 0)
    first_row = row == 0
    last_row = row == shape[0] - 1

    for j in range(subs):
        cols = pl.ds(j * lanes, lanes)
        base = (pl.program_id(0) * subs + j) * per_tile

        def pixel(c):
            if per_tile == 1:
                return ans_ref[base, c]
            return jnp.concatenate([ans_ref[base + g, c] for g in range(per_tile)], axis=0)

        def body(z, carry):
            n, front, w0, w1, w2, d_prev, d = carry
            d_next = jnp.where(
                z + 1 < slices,
                d_ref[jnp.minimum(z + 1, slices - 1), :, cols].astype(jnp.float32),
                zhalo_ref[1, :, cols],
            )
            rims = rhalo_ref[z, :, cols]
            upper = jnp.where(first_row, rims[0:1], pltpu.roll(d, 1, 0))
            lower = jnp.where(last_row, rims[1:2], pltpu.roll(d, shape[0] - 1, 0))
            smooth = 2.0 * smooth_weight * ((d - d_prev) + (d - d_next) + (d - upper) + (d - lower))
            dtn = softplus(d) * scale
            lit = front * (1.0 - jnp.exp2(dtn))
            n_next = n + dtn
            through = jnp.exp2(n_next)
            inv = jnp.exp2(-n_next)
            col = [jax.nn.sigmoid(c_ref[c, z, :, cols].astype(jnp.float32)) for c in range(3)]
            lit_col = [lit * col[c] for c in range(3)]
            w = [w0 + lit_col[0], w1 + lit_col[1], w2 + lit_col[2]]
            res = [pixel(c) for c in range(3)]
            emitted = res[0] * col[0] + res[1] * col[1] + res[2] * col[2]
            left = res[0] * w[0] + res[1] * w[1] + res[2] * w[2]
            inner = emitted - inv * (pixel(3) - left)
            for c in range(3):
                gc_ref[c, z, :, cols] = res[c] * lit_col[c] * (1.0 - col[c])
            gd_ref[z, :, cols] = gain * through * jax.nn.sigmoid(d) * inner + smooth
            return (n_next, through, w[0], w[1], w[2], d, d_next)

        zero = jnp.zeros(shape, jnp.float32)
        one = jnp.ones(shape, jnp.float32)
        start = (
            zero, one, zero, zero, zero,
            zhalo_ref[0, :, cols],
            d_ref[0, :, cols].astype(jnp.float32),
        )
        lax.fori_loop(0, slices, body, start, unroll=2)


def forward_partial(density, colour_raw, step, depth_count):
    slices, rows, width = density.shape
    tiles, per_tile, chunk_rows = chunking(rows, width, depth_count)
    block = lanes * forward_subs if tiles % forward_subs == 0 else lanes
    return pl.pallas_call(
        functools.partial(forward_kernel, step=step),
        grid=(width // block,),
        in_specs=[
            pl.BlockSpec((slices, rows, block), lambda i: (0, 0, i)),
            pl.BlockSpec((3, slices, rows, block), lambda i: (0, 0, 0, i)),
        ],
        out_specs=pl.BlockSpec(
            (per_tile * (block // lanes), 4, chunk_rows, lanes), lambda i: (i, 0, 0, 0)
        ),
        out_shape=jax.ShapeDtypeStruct((tiles * per_tile, 4, chunk_rows, lanes), jnp.float32),
    )(density, colour_raw)


def backward_grads(density, colour_raw, answers, zhalo, rhalo, step, slices_total):
    slices, rows, width = density.shape
    tiles = width // lanes
    block = lanes * backward_subs if tiles % backward_subs == 0 else lanes
    slab = pl.BlockSpec((slices, rows, block), lambda i: (0, 0, i))
    colours = pl.BlockSpec((3, slices, rows, block), lambda i: (0, 0, 0, i))
    return pl.pallas_call(
        functools.partial(backward_kernel, step=step, slices_total=float(slices_total)),
        grid=(width // block,),
        in_specs=[
            slab,
            colours,
            pl.BlockSpec(memory_space=pltpu.VMEM),
            pl.BlockSpec((2, rows, block), lambda i: (0, 0, i)),
            pl.BlockSpec((slices, 2, block), lambda i: (0, 0, i)),
        ],
        out_specs=[slab, colours],
        out_shape=[
            jax.ShapeDtypeStruct((slices, rows, width), jnp.float32),
            jax.ShapeDtypeStruct((3, slices, rows, width), jnp.float32),
        ],
    )(density, colour_raw, answers, zhalo, rhalo)


def composite(parts, slab_rank, target_piece, slices_total):
    emitted, passing = (parts[:, :3], parts[:, 3])
    earlier = (slab_rank[None, :] < slab_rank[:, None]).astype(jnp.float32)[:, :, None, None]
    later = (slab_rank[None, :] > slab_rank[:, None]).astype(jnp.float32)[:, :, None, None, None]
    front = jnp.exp(jnp.sum(earlier * jnp.log(passing)[None], axis=1))
    weighted = front[:, None] * emitted
    behind = jnp.sum(later * weighted[None], axis=1) / (front * passing)[:, None]
    residual = jnp.sum(weighted, axis=0) - target_piece
    scaled_residual = slices_total * (front[:, None] * residual[None])
    scaled_behind = slices_total * (front * jnp.sum(residual[None] * behind, axis=1))
    folded = jnp.sum(scaled_residual * emitted, axis=1) + passing * scaled_behind
    return jnp.concatenate([scaled_residual, folded[:, None]], axis=1)


def halos(density_raw):
    depth_count = lax.axis_size("depth")
    rows_count = lax.axis_size("rows")
    depth_at = lax.axis_index("depth")
    rows_at = lax.axis_index("rows")
    up_d = [(i, i + 1) for i in range(depth_count - 1)]
    up_r = [(i, i + 1) for i in range(rows_count - 1)]
    first_slice = density_raw[:1]
    last_slice = density_raw[-1:]
    first_row = density_raw[:, :1]
    last_row = density_raw[:, -1:]
    prev_slice = lax.ppermute(last_slice, "depth", up_d)
    next_slice = lax.ppermute(first_slice, "depth", [(j, i) for i, j in up_d])
    prev_row = lax.ppermute(last_row, "rows", up_r)
    next_row = lax.ppermute(first_row, "rows", [(j, i) for i, j in up_r])
    prev_slice = jnp.where(depth_at > 0, prev_slice, first_slice)
    next_slice = jnp.where(depth_at < depth_count - 1, next_slice, last_slice)
    prev_row = jnp.where(rows_at > 0, prev_row, first_row)
    next_row = jnp.where(rows_at < rows_count - 1, next_row, last_row)
    zhalo = jnp.concatenate([prev_slice, next_slice], axis=0).astype(jnp.float32)
    rhalo = jnp.concatenate([prev_row, next_row], axis=1).astype(jnp.float32)
    return zhalo, rhalo


def exchange(x, axis):
    count = lax.axis_size(axis)
    if count % 2 or count == 2:
        return lax.all_to_all(x, axis, 0, 0, tiled=True)
    outer = count // 2
    pairs = [[2 * k, 2 * k + 1] for k in range(outer)]
    strides = [[b + 2 * k for k in range(outer)] for b in range(2)]
    x = x.reshape((outer, 2) + x.shape[1:])
    x = lax.all_to_all(x, axis, 1, 1, axis_index_groups=pairs, tiled=True)
    x = lax.all_to_all(x, axis, 0, 0, axis_index_groups=strides, tiled=True)
    return x.reshape((count,) + x.shape[2:])


def local(density_raw, colour_raw, target, slab_rank):
    slices_dev, rows_dev, width = density_raw.shape
    depth_count = lax.axis_size("depth")
    slices_total = slices_dev * depth_count
    step = optical_depth / slices_total
    tiles, per_tile, chunk_rows = chunking(rows_dev, width, depth_count)
    partial_value = forward_partial(density_raw, colour_raw, step, depth_count)
    partial_value, after_forward = lax.optimization_barrier((partial_value, density_raw))
    zhalo, rhalo = halos(after_forward)
    received = exchange(partial_value, "depth")
    position = lax.axis_index("depth")
    target_piece = lax.dynamic_slice(
        target,
        (0, (position % per_tile) * chunk_rows, (position // per_tile) * lanes),
        (3, chunk_rows, lanes),
    )
    answers = composite(received, slab_rank, target_piece, float(slices_total))
    returned = exchange(answers, "depth")
    return backward_grads(
        density_raw, colour_raw, returned, zhalo, rhalo, step, slices_total
    )


def solution(mesh):
    placed = (P("depth", "rows", None), P(None, "depth", "rows", None), P(None, "rows", None), P())
    return jax.shard_map(
        local,
        mesh=mesh,
        in_specs=placed,
        out_specs=(P("depth", "rows", None), P(None, "depth", "rows", None)),
        check_vma=False,
    )
```

```python
import functools

import jax
import jax.numpy as jnp
from jax import lax
from jax.experimental import pallas as pl
from jax.experimental.pallas import tpu as pltpu
from jax.sharding import PartitionSpec as P

optical_depth = 2.5
smooth_weight = 0.05
lanes = 128
forward_subs = 4
backward_subs = 2


log2e = 1.4426950408889634
ln2 = 0.6931471805599453


def softplus(x):
    return jnp.maximum(x, 0.0) + ln2 * jnp.log2(1.0 + jnp.exp2(jnp.abs(x) * -log2e))


def chunking(rows, width, depth_count):
    tiles = width // lanes
    per_tile = max(depth_count // tiles, 1)
    return tiles, per_tile, rows // per_tile


def forward_kernel(d_ref, c_ref, out_ref, *, step):
    slices, rows, block = d_ref.shape
    shape = (rows, lanes)
    subs = block // lanes
    per_tile = out_ref.shape[0] // subs
    chunk_rows = out_ref.shape[2]
    scale = -step * log2e

    for j in range(subs):
        cols = pl.ds(j * lanes, lanes)

        def body(z, carry):
            n, front, e0, e1, e2 = carry
            dtn = softplus(d_ref[z, :, cols].astype(jnp.float32)) * scale
            kept = jnp.exp2(dtn)
            lit = front * (1.0 - kept)
            n = n + dtn
            e0 = e0 + lit * jax.nn.sigmoid(c_ref[0, z, :, cols].astype(jnp.float32))
            e1 = e1 + lit * jax.nn.sigmoid(c_ref[1, z, :, cols].astype(jnp.float32))
            e2 = e2 + lit * jax.nn.sigmoid(c_ref[2, z, :, cols].astype(jnp.float32))
            return (n, front * kept, e0, e1, e2)

        zero = jnp.zeros(shape, jnp.float32)
        one = jnp.ones(shape, jnp.float32)
        n, _, e0, e1, e2 = lax.fori_loop(0, slices, body, (zero, one, zero, zero, zero), unroll=4)
        values = (e0, e1, e2, jnp.exp2(n))
        for g in range(per_tile):
            for c in range(4):
                out_ref[j * per_tile + g, c] = values[c][g * chunk_rows:(g + 1) * chunk_rows]


def smooth_kernel(d_ref, zhalo_ref, rhalo_ref, out_ref):
    slices, rows, block = d_ref.shape
    shape = (rows, lanes)
    row = lax.broadcasted_iota(jnp.int32, shape, 0)
    first_row = row == 0
    last_row = row == shape[0] - 1

    for j in range(block // lanes):
        cols = pl.ds(j * lanes, lanes)

        def body(z, carry):
            d_prev, d = carry
            d_next = jnp.where(
                z + 1 < slices,
                d_ref[jnp.minimum(z + 1, slices - 1), :, cols].astype(jnp.float32),
                zhalo_ref[1, :, cols],
            )
            rims = rhalo_ref[z, :, cols]
            upper = jnp.where(first_row, rims[0:1], pltpu.roll(d, 1, 0))
            lower = jnp.where(last_row, rims[1:2], pltpu.roll(d, shape[0] - 1, 0))
            out_ref[z, :, cols] = 2.0 * smooth_weight * (
                (d - d_prev) + (d - d_next) + (d - upper) + (d - lower)
            )
            return (d, d_next)

        start = (zhalo_ref[0, :, cols], d_ref[0, :, cols].astype(jnp.float32))
        lax.fori_loop(0, slices, body, start, unroll=2)


def backward_kernel(d_ref, c_ref, ans_ref, smooth_ref, gd_ref, gc_ref, *, step, slices_total):
    slices, rows, block = d_ref.shape
    shape = (rows, lanes)
    subs = block // lanes
    per_tile = ans_ref.shape[0] // (pl.num_programs(0) * subs)
    scale = -step * log2e
    gain = optical_depth / slices_total

    for j in range(subs):
        cols = pl.ds(j * lanes, lanes)
        base = (pl.program_id(0) * subs + j) * per_tile

        def pixel(c):
            if per_tile == 1:
                return ans_ref[base, c]
            return jnp.concatenate([ans_ref[base + g, c] for g in range(per_tile)], axis=0)

        def body(z, carry):
            n, front, w0, w1, w2 = carry
            d = d_ref[z, :, cols].astype(jnp.float32)
            dtn = softplus(d) * scale
            lit = front * (1.0 - jnp.exp2(dtn))
            n_next = n + dtn
            through = jnp.exp2(n_next)
            inv = jnp.exp2(-n_next)
            col = [jax.nn.sigmoid(c_ref[c, z, :, cols].astype(jnp.float32)) for c in range(3)]
            lit_col = [lit * col[c] for c in range(3)]
            w = [w0 + lit_col[0], w1 + lit_col[1], w2 + lit_col[2]]
            res = [pixel(c) for c in range(3)]
            emitted = res[0] * col[0] + res[1] * col[1] + res[2] * col[2]
            left = res[0] * w[0] + res[1] * w[1] + res[2] * w[2]
            inner = emitted - inv * (pixel(3) - left)
            for c in range(3):
                gc_ref[c, z, :, cols] = res[c] * lit_col[c] * (1.0 - col[c])
            gd_ref[z, :, cols] = gain * through * jax.nn.sigmoid(d) * inner + smooth_ref[z, :, cols]
            return (n_next, through, w[0], w[1], w[2])

        zero = jnp.zeros(shape, jnp.float32)
        one = jnp.ones(shape, jnp.float32)
        lax.fori_loop(0, slices, body, (zero, one, zero, zero, zero), unroll=2)


def forward_partial(density, colour_raw, step, depth_count):
    slices, rows, width = density.shape
    tiles, per_tile, chunk_rows = chunking(rows, width, depth_count)
    block = lanes * forward_subs if tiles % forward_subs == 0 else lanes
    return pl.pallas_call(
        functools.partial(forward_kernel, step=step),
        grid=(width // block,),
        in_specs=[
            pl.BlockSpec((slices, rows, block), lambda i: (0, 0, i)),
            pl.BlockSpec((3, slices, rows, block), lambda i: (0, 0, 0, i)),
        ],
        out_specs=pl.BlockSpec(
            (per_tile * (block // lanes), 4, chunk_rows, lanes), lambda i: (i, 0, 0, 0)
        ),
        out_shape=jax.ShapeDtypeStruct((tiles * per_tile, 4, chunk_rows, lanes), jnp.float32),
    )(density, colour_raw)


def smooth_term(density, zhalo, rhalo):
    slices, rows, width = density.shape
    tiles = width // lanes
    block = lanes * forward_subs if tiles % forward_subs == 0 else lanes
    slab = pl.BlockSpec((slices, rows, block), lambda i: (0, 0, i))
    return pl.pallas_call(
        smooth_kernel,
        grid=(width // block,),
        in_specs=[
            slab,
            pl.BlockSpec((2, rows, block), lambda i: (0, 0, i)),
            pl.BlockSpec((slices, 2, block), lambda i: (0, 0, i)),
        ],
        out_specs=slab,
        out_shape=jax.ShapeDtypeStruct((slices, rows, width), jnp.float32),
    )(density, zhalo, rhalo)


def backward_grads(density, colour_raw, answers, smooth, step, slices_total):
    slices, rows, width = density.shape
    tiles = width // lanes
    block = lanes * backward_subs if tiles % backward_subs == 0 else lanes
    slab = pl.BlockSpec((slices, rows, block), lambda i: (0, 0, i))
    colours = pl.BlockSpec((3, slices, rows, block), lambda i: (0, 0, 0, i))
    return pl.pallas_call(
        functools.partial(backward_kernel, step=step, slices_total=float(slices_total)),
        grid=(width // block,),
        in_specs=[slab, colours, pl.BlockSpec(memory_space=pltpu.VMEM), slab],
        out_specs=[slab, colours],
        out_shape=[
            jax.ShapeDtypeStruct((slices, rows, width), jnp.float32),
            jax.ShapeDtypeStruct((3, slices, rows, width), jnp.float32),
        ],
        input_output_aliases={3: 0},
    )(density, colour_raw, answers, smooth)


def composite(parts, slab_rank, target_piece, slices_total):
    emitted, passing = (parts[:, :3], parts[:, 3])
    earlier = (slab_rank[None, :] < slab_rank[:, None]).astype(jnp.float32)[:, :, None, None]
    later = (slab_rank[None, :] > slab_rank[:, None]).astype(jnp.float32)[:, :, None, None, None]
    front = jnp.exp(jnp.sum(earlier * jnp.log(passing)[None], axis=1))
    weighted = front[:, None] * emitted
    behind = jnp.sum(later * weighted[None], axis=1) / (front * passing)[:, None]
    residual = jnp.sum(weighted, axis=0) - target_piece
    scaled_residual = slices_total * (front[:, None] * residual[None])
    scaled_behind = slices_total * (front * jnp.sum(residual[None] * behind, axis=1))
    folded = jnp.sum(scaled_residual * emitted, axis=1) + passing * scaled_behind
    return jnp.concatenate([scaled_residual, folded[:, None]], axis=1)


def halos(density_raw):
    depth_count = lax.axis_size("depth")
    rows_count = lax.axis_size("rows")
    depth_at = lax.axis_index("depth")
    rows_at = lax.axis_index("rows")
    up_d = [(i, i + 1) for i in range(depth_count - 1)]
    up_r = [(i, i + 1) for i in range(rows_count - 1)]
    first_slice = density_raw[:1]
    last_slice = density_raw[-1:]
    first_row = density_raw[:, :1]
    last_row = density_raw[:, -1:]
    prev_slice = lax.ppermute(last_slice, "depth", up_d)
    next_slice = lax.ppermute(first_slice, "depth", [(j, i) for i, j in up_d])
    prev_row = lax.ppermute(last_row, "rows", up_r)
    next_row = lax.ppermute(first_row, "rows", [(j, i) for i, j in up_r])
    prev_slice = jnp.where(depth_at > 0, prev_slice, first_slice)
    next_slice = jnp.where(depth_at < depth_count - 1, next_slice, last_slice)
    prev_row = jnp.where(rows_at > 0, prev_row, first_row)
    next_row = jnp.where(rows_at < rows_count - 1, next_row, last_row)
    zhalo = jnp.concatenate([prev_slice, next_slice], axis=0).astype(jnp.float32)
    rhalo = jnp.concatenate([prev_row, next_row], axis=1).astype(jnp.float32)
    return zhalo, rhalo


def local(density_raw, colour_raw, target, slab_rank):
    slices_dev, rows_dev, width = density_raw.shape
    depth_count = lax.axis_size("depth")
    slices_total = slices_dev * depth_count
    step = optical_depth / slices_total
    tiles, per_tile, chunk_rows = chunking(rows_dev, width, depth_count)
    partial_value = forward_partial(density_raw, colour_raw, step, depth_count)
    partial_value, after_forward = lax.optimization_barrier((partial_value, density_raw))
    zhalo, rhalo = halos(after_forward)
    received = lax.all_to_all(partial_value, "depth", 0, 0, tiled=True)
    position = lax.axis_index("depth")
    target_piece = lax.dynamic_slice(
        target,
        (0, (position % per_tile) * chunk_rows, (position // per_tile) * lanes),
        (3, chunk_rows, lanes),
    )
    answers = composite(received, slab_rank, target_piece, float(slices_total))
    returned = lax.all_to_all(answers, "depth", 0, 0, tiled=True)
    smooth = smooth_term(density_raw, zhalo, rhalo)
    return backward_grads(density_raw, colour_raw, returned, smooth, step, slices_total)


def solution(mesh):
    placed = (P("depth", "rows", None), P(None, "depth", "rows", None), P(None, "rows", None), P())
    return jax.shard_map(
        local,
        mesh=mesh,
        in_specs=placed,
        out_specs=(P("depth", "rows", None), P(None, "depth", "rows", None)),
        check_vma=False,
    )
```

```python
import functools

import jax
import jax.numpy as jnp
from jax import lax
from jax.experimental import pallas as pl
from jax.experimental.pallas import tpu as pltpu
from jax.sharding import PartitionSpec as P

optical_depth = 2.5
smooth_weight = 0.05
lanes = 128
forward_subs = 4
backward_subs = 2


log2e = 1.4426950408889634
ln2 = 0.6931471805599453


def softplus(x):
    return jnp.maximum(x, 0.0) + ln2 * jnp.log2(1.0 + jnp.exp2(jnp.abs(x) * -log2e))


def chunking(rows, width, depth_count):
    tiles = width // lanes
    per_tile = max(depth_count // tiles, 1)
    return tiles, per_tile, rows // per_tile


def forward_kernel(d_ref, c_ref, out_ref, *, step):
    slices, rows, block = d_ref.shape
    shape = (rows, lanes)
    subs = block // lanes
    per_tile = out_ref.shape[0] // subs
    chunk_rows = out_ref.shape[2]
    scale = -step * log2e

    for j in range(subs):
        cols = pl.ds(j * lanes, lanes)

        def body(z, carry):
            n, front, e0, e1, e2 = carry
            dtn = softplus(d_ref[z, :, cols].astype(jnp.float32)) * scale
            kept = jnp.exp2(dtn)
            lit = front * (1.0 - kept)
            n = n + dtn
            e0 = e0 + lit * jax.nn.sigmoid(c_ref[0, z, :, cols].astype(jnp.float32))
            e1 = e1 + lit * jax.nn.sigmoid(c_ref[1, z, :, cols].astype(jnp.float32))
            e2 = e2 + lit * jax.nn.sigmoid(c_ref[2, z, :, cols].astype(jnp.float32))
            return (n, front * kept, e0, e1, e2)

        zero = jnp.zeros(shape, jnp.float32)
        one = jnp.ones(shape, jnp.float32)
        n, _, e0, e1, e2 = lax.fori_loop(0, slices, body, (zero, one, zero, zero, zero), unroll=4)
        values = (e0, e1, e2, jnp.exp2(n))
        for g in range(per_tile):
            for c in range(4):
                out_ref[j * per_tile + g, c] = values[c][g * chunk_rows:(g + 1) * chunk_rows]


def smooth_kernel(flags_ref, d_ref, zprev_ref, znext_ref, rprev_ref, rnext_ref, out_ref):
    slices, rows, block = d_ref.shape
    shape = (rows, lanes)
    row = lax.broadcasted_iota(jnp.int32, shape, 0)
    first_row = row == 0
    last_row = row == shape[0] - 1
    has_prev_slice = flags_ref[0] > 0
    has_next_slice = flags_ref[1] > 0
    has_prev_row = flags_ref[2] > 0
    has_next_row = flags_ref[3] > 0

    for j in range(block // lanes):
        cols = pl.ds(j * lanes, lanes)
        d_first = d_ref[0, :, cols].astype(jnp.float32)
        d_last = d_ref[slices - 1, :, cols].astype(jnp.float32)
        prev_slice = jnp.where(has_prev_slice, zprev_ref[0, :, cols].astype(jnp.float32), d_first)
        next_slice = jnp.where(has_next_slice, znext_ref[0, :, cols].astype(jnp.float32), d_last)

        def body(z, carry):
            d_prev, d = carry
            d_next = jnp.where(
                z + 1 < slices,
                d_ref[jnp.minimum(z + 1, slices - 1), :, cols].astype(jnp.float32),
                next_slice,
            )
            top = jnp.where(has_prev_row, rprev_ref[z, :, cols].astype(jnp.float32), d[0:1])
            bottom = jnp.where(
                has_next_row, rnext_ref[z, :, cols].astype(jnp.float32), d[rows - 1:rows]
            )
            upper = jnp.where(first_row, top, pltpu.roll(d, 1, 0))
            lower = jnp.where(last_row, bottom, pltpu.roll(d, shape[0] - 1, 0))
            out_ref[z, :, cols] = 2.0 * smooth_weight * (
                (d - d_prev) + (d - d_next) + (d - upper) + (d - lower)
            )
            return (d, d_next)

        lax.fori_loop(0, slices, body, (prev_slice, d_first), unroll=2)


def backward_kernel(d_ref, c_ref, ans_ref, smooth_ref, gd_ref, gc_ref, *, step, slices_total):
    slices, rows, block = d_ref.shape
    shape = (rows, lanes)
    subs = block // lanes
    per_tile = ans_ref.shape[0] // (pl.num_programs(0) * subs)
    scale = -step * log2e
    gain = optical_depth / slices_total

    for j in range(subs):
        cols = pl.ds(j * lanes, lanes)
        base = (pl.program_id(0) * subs + j) * per_tile

        def pixel(c):
            if per_tile == 1:
                return ans_ref[base, c]
            return jnp.concatenate([ans_ref[base + g, c] for g in range(per_tile)], axis=0)

        def body(z, carry):
            n, front, w0, w1, w2 = carry
            d = d_ref[z, :, cols].astype(jnp.float32)
            dtn = softplus(d) * scale
            lit = front * (1.0 - jnp.exp2(dtn))
            n_next = n + dtn
            through = jnp.exp2(n_next)
            inv = jnp.exp2(-n_next)
            col = [jax.nn.sigmoid(c_ref[c, z, :, cols].astype(jnp.float32)) for c in range(3)]
            lit_col = [lit * col[c] for c in range(3)]
            w = [w0 + lit_col[0], w1 + lit_col[1], w2 + lit_col[2]]
            res = [pixel(c) for c in range(3)]
            emitted = res[0] * col[0] + res[1] * col[1] + res[2] * col[2]
            left = res[0] * w[0] + res[1] * w[1] + res[2] * w[2]
            inner = emitted - inv * (pixel(3) - left)
            for c in range(3):
                gc_ref[c, z, :, cols] = res[c] * lit_col[c] * (1.0 - col[c])
            gd_ref[z, :, cols] = gain * through * jax.nn.sigmoid(d) * inner + smooth_ref[z, :, cols]
            return (n_next, through, w[0], w[1], w[2])

        zero = jnp.zeros(shape, jnp.float32)
        one = jnp.ones(shape, jnp.float32)
        lax.fori_loop(0, slices, body, (zero, one, zero, zero, zero), unroll=2)


def forward_partial(density, colour_raw, step, depth_count):
    slices, rows, width = density.shape
    tiles, per_tile, chunk_rows = chunking(rows, width, depth_count)
    block = lanes * forward_subs if tiles % forward_subs == 0 else lanes
    return pl.pallas_call(
        functools.partial(forward_kernel, step=step),
        grid=(width // block,),
        in_specs=[
            pl.BlockSpec((slices, rows, block), lambda i: (0, 0, i)),
            pl.BlockSpec((3, slices, rows, block), lambda i: (0, 0, 0, i)),
        ],
        out_specs=pl.BlockSpec(
            (per_tile * (block // lanes), 4, chunk_rows, lanes), lambda i: (i, 0, 0, 0)
        ),
        out_shape=jax.ShapeDtypeStruct((tiles * per_tile, 4, chunk_rows, lanes), jnp.float32),
    )(density, colour_raw)


def smooth_term(density, flags, zprev, znext, rprev, rnext):
    slices, rows, width = density.shape
    tiles = width // lanes
    block = lanes * forward_subs if tiles % forward_subs == 0 else lanes
    slab = pl.BlockSpec((slices, rows, block), lambda i: (0, 0, i))
    face = pl.BlockSpec((1, rows, block), lambda i: (0, 0, i))
    rim = pl.BlockSpec((slices, 1, block), lambda i: (0, 0, i))
    return pl.pallas_call(
        smooth_kernel,
        grid=(width // block,),
        in_specs=[pl.BlockSpec(memory_space=pltpu.SMEM), slab, face, face, rim, rim],
        out_specs=slab,
        out_shape=jax.ShapeDtypeStruct((slices, rows, width), jnp.float32),
    )(flags, density, zprev, znext, rprev, rnext)


def backward_grads(density, colour_raw, answers, smooth, step, slices_total):
    slices, rows, width = density.shape
    tiles = width // lanes
    block = lanes * backward_subs if tiles % backward_subs == 0 else lanes
    slab = pl.BlockSpec((slices, rows, block), lambda i: (0, 0, i))
    colours = pl.BlockSpec((3, slices, rows, block), lambda i: (0, 0, 0, i))
    return pl.pallas_call(
        functools.partial(backward_kernel, step=step, slices_total=float(slices_total)),
        grid=(width // block,),
        in_specs=[slab, colours, pl.BlockSpec(memory_space=pltpu.VMEM), slab],
        out_specs=[slab, colours],
        out_shape=[
            jax.ShapeDtypeStruct((slices, rows, width), jnp.float32),
            jax.ShapeDtypeStruct((3, slices, rows, width), jnp.float32),
        ],
        input_output_aliases={3: 0},
    )(density, colour_raw, answers, smooth)


def composite(parts, slab_rank, target_piece, slices_total):
    emitted, passing = (parts[:, :3], parts[:, 3])
    earlier = (slab_rank[None, :] < slab_rank[:, None]).astype(jnp.float32)[:, :, None, None]
    later = (slab_rank[None, :] > slab_rank[:, None]).astype(jnp.float32)[:, :, None, None, None]
    front = jnp.exp(jnp.sum(earlier * jnp.log(passing)[None], axis=1))
    weighted = front[:, None] * emitted
    behind = jnp.sum(later * weighted[None], axis=1) / (front * passing)[:, None]
    residual = jnp.sum(weighted, axis=0) - target_piece
    scaled_residual = slices_total * (front[:, None] * residual[None])
    scaled_behind = slices_total * (front * jnp.sum(residual[None] * behind, axis=1))
    folded = jnp.sum(scaled_residual * emitted, axis=1) + passing * scaled_behind
    return jnp.concatenate([scaled_residual, folded[:, None]], axis=1)


def depth_halos(density_raw):
    depth_count = lax.axis_size("depth")
    up = [(i, i + 1) for i in range(depth_count - 1)]
    prev_slice = lax.ppermute(density_raw[-1:], "depth", up)
    next_slice = lax.ppermute(density_raw[:1], "depth", [(j, i) for i, j in up])
    return prev_slice, next_slice


def row_halos(density_raw):
    rows_count = lax.axis_size("rows")
    up = [(i, i + 1) for i in range(rows_count - 1)]
    prev_row = lax.ppermute(density_raw[:, -1:], "rows", up)
    next_row = lax.ppermute(density_raw[:, :1], "rows", [(j, i) for i, j in up])
    return prev_row, next_row


def edge_flags():
    depth_at = lax.axis_index("depth")
    rows_at = lax.axis_index("rows")
    return jnp.stack(
        [
            depth_at > 0,
            depth_at < lax.axis_size("depth") - 1,
            rows_at > 0,
            rows_at < lax.axis_size("rows") - 1,
        ]
    ).astype(jnp.int32)


def local(density_raw, colour_raw, target, slab_rank):
    slices_dev, rows_dev, width = density_raw.shape
    depth_count = lax.axis_size("depth")
    slices_total = slices_dev * depth_count
    step = optical_depth / slices_total
    tiles, per_tile, chunk_rows = chunking(rows_dev, width, depth_count)
    partial_value = forward_partial(density_raw, colour_raw, step, depth_count)
    partial_value, after_forward = lax.optimization_barrier((partial_value, density_raw))
    zprev, znext = depth_halos(after_forward)
    received = lax.all_to_all(partial_value, "depth", 0, 0, tiled=True)
    received, zprev, znext = lax.optimization_barrier((received, zprev, znext))
    position = lax.axis_index("depth")
    target_piece = lax.dynamic_slice(
        target,
        (0, (position % per_tile) * chunk_rows, (position // per_tile) * lanes),
        (3, chunk_rows, lanes),
    )
    answers = composite(received, slab_rank, target_piece, float(slices_total))
    answers, after_composite = lax.optimization_barrier((answers, density_raw))
    rprev, rnext = row_halos(after_composite)
    returned = lax.all_to_all(answers, "depth", 0, 0, tiled=True)
    smooth = smooth_term(density_raw, edge_flags(), zprev, znext, rprev, rnext)
    return backward_grads(density_raw, colour_raw, returned, smooth, step, slices_total)


def solution(mesh):
    placed = (P("depth", "rows", None), P(None, "depth", "rows", None), P(None, "rows", None), P())
    return jax.shard_map(
        local,
        mesh=mesh,
        in_specs=placed,
        out_specs=(P("depth", "rows", None), P(None, "depth", "rows", None)),
        check_vma=False,
    )
```

```python
import functools

import jax
import jax.numpy as jnp
from jax import lax
from jax.experimental import pallas as pl
from jax.experimental.pallas import tpu as pltpu
from jax.sharding import PartitionSpec as P

optical_depth = 2.5
smooth_weight = 0.05
lanes = 128
forward_subs = 4
backward_subs = 2
forward_unroll = 32
backward_unroll = 8


log2e = 1.4426950408889634
ln2 = 0.6931471805599453


def softplus(x):
    return jnp.maximum(x, 0.0) + ln2 * jnp.log2(1.0 + jnp.exp2(jnp.abs(x) * -log2e))


def chunking(rows, width, depth_count):
    tiles = width // lanes
    per_tile = max(depth_count // tiles, 1)
    return tiles, per_tile, rows // per_tile


def forward_kernel(d_ref, c_ref, out_ref, *, step):
    slices, rows, block = d_ref.shape
    shape = (rows, lanes)
    subs = block // lanes
    per_tile = out_ref.shape[0] // subs
    chunk_rows = out_ref.shape[2]
    scale = -step * log2e

    for j in range(subs):
        cols = pl.ds(j * lanes, lanes)

        def body(z, carry):
            n, front, e0, e1, e2 = carry
            dtn = softplus(d_ref[z, :, cols].astype(jnp.float32)) * scale
            kept = jnp.exp2(dtn)
            lit = front * (1.0 - kept)
            n = n + dtn
            e0 = e0 + lit * jax.nn.sigmoid(c_ref[0, z, :, cols].astype(jnp.float32))
            e1 = e1 + lit * jax.nn.sigmoid(c_ref[1, z, :, cols].astype(jnp.float32))
            e2 = e2 + lit * jax.nn.sigmoid(c_ref[2, z, :, cols].astype(jnp.float32))
            return (n, front * kept, e0, e1, e2)

        zero = jnp.zeros(shape, jnp.float32)
        one = jnp.ones(shape, jnp.float32)
        n, _, e0, e1, e2 = lax.fori_loop(0, slices, body, (zero, one, zero, zero, zero), unroll=forward_unroll)
        values = (e0, e1, e2, jnp.exp2(n))
        for g in range(per_tile):
            for c in range(4):
                out_ref[j * per_tile + g, c] = values[c][g * chunk_rows:(g + 1) * chunk_rows]


def smooth_kernel(d_ref, zhalo_ref, rhalo_ref, out_ref):
    slices, rows, block = d_ref.shape
    shape = (rows, lanes)
    row = lax.broadcasted_iota(jnp.int32, shape, 0)
    first_row = row == 0
    last_row = row == shape[0] - 1

    for j in range(block // lanes):
        cols = pl.ds(j * lanes, lanes)

        def body(z, carry):
            d_prev, d = carry
            d_next = jnp.where(
                z + 1 < slices,
                d_ref[jnp.minimum(z + 1, slices - 1), :, cols].astype(jnp.float32),
                zhalo_ref[1, :, cols],
            )
            rims = rhalo_ref[z, :, cols]
            upper = jnp.where(first_row, rims[0:1], pltpu.roll(d, 1, 0))
            lower = jnp.where(last_row, rims[1:2], pltpu.roll(d, shape[0] - 1, 0))
            out_ref[z, :, cols] = 2.0 * smooth_weight * (
                (d - d_prev) + (d - d_next) + (d - upper) + (d - lower)
            )
            return (d, d_next)

        start = (zhalo_ref[0, :, cols], d_ref[0, :, cols].astype(jnp.float32))
        lax.fori_loop(0, slices, body, start, unroll=2)


def backward_kernel(d_ref, c_ref, ans_ref, smooth_ref, gd_ref, gc_ref, *, step, slices_total):
    slices, rows, block = d_ref.shape
    shape = (rows, lanes)
    subs = block // lanes
    per_tile = ans_ref.shape[0] // (pl.num_programs(0) * subs)
    scale = -step * log2e
    gain = optical_depth / slices_total

    for j in range(subs):
        cols = pl.ds(j * lanes, lanes)
        base = (pl.program_id(0) * subs + j) * per_tile

        def pixel(c):
            if per_tile == 1:
                return ans_ref[base, c]
            return jnp.concatenate([ans_ref[base + g, c] for g in range(per_tile)], axis=0)

        def body(z, carry):
            n, front, w0, w1, w2 = carry
            d = d_ref[z, :, cols].astype(jnp.float32)
            dtn = softplus(d) * scale
            lit = front * (1.0 - jnp.exp2(dtn))
            n_next = n + dtn
            through = jnp.exp2(n_next)
            inv = jnp.exp2(-n_next)
            col = [jax.nn.sigmoid(c_ref[c, z, :, cols].astype(jnp.float32)) for c in range(3)]
            lit_col = [lit * col[c] for c in range(3)]
            w = [w0 + lit_col[0], w1 + lit_col[1], w2 + lit_col[2]]
            res = [pixel(c) for c in range(3)]
            emitted = res[0] * col[0] + res[1] * col[1] + res[2] * col[2]
            left = res[0] * w[0] + res[1] * w[1] + res[2] * w[2]
            inner = emitted - inv * (pixel(3) - left)
            for c in range(3):
                gc_ref[c, z, :, cols] = res[c] * lit_col[c] * (1.0 - col[c])
            gd_ref[z, :, cols] = gain * through * jax.nn.sigmoid(d) * inner + smooth_ref[z, :, cols]
            return (n_next, through, w[0], w[1], w[2])

        zero = jnp.zeros(shape, jnp.float32)
        one = jnp.ones(shape, jnp.float32)
        lax.fori_loop(0, slices, body, (zero, one, zero, zero, zero), unroll=backward_unroll)


def forward_partial(density, colour_raw, step, depth_count):
    slices, rows, width = density.shape
    tiles, per_tile, chunk_rows = chunking(rows, width, depth_count)
    block = lanes * forward_subs if tiles % forward_subs == 0 else lanes
    return pl.pallas_call(
        functools.partial(forward_kernel, step=step),
        grid=(width // block,),
        in_specs=[
            pl.BlockSpec((slices, rows, block), lambda i: (0, 0, i)),
            pl.BlockSpec((3, slices, rows, block), lambda i: (0, 0, 0, i)),
        ],
        out_specs=pl.BlockSpec(
            (per_tile * (block // lanes), 4, chunk_rows, lanes), lambda i: (i, 0, 0, 0)
        ),
        out_shape=jax.ShapeDtypeStruct((tiles * per_tile, 4, chunk_rows, lanes), jnp.float32),
    )(density, colour_raw)


def smooth_term(density, zhalo, rhalo):
    slices, rows, width = density.shape
    tiles = width // lanes
    block = lanes * forward_subs if tiles % forward_subs == 0 else lanes
    slab = pl.BlockSpec((slices, rows, block), lambda i: (0, 0, i))
    return pl.pallas_call(
        smooth_kernel,
        grid=(width // block,),
        in_specs=[
            slab,
            pl.BlockSpec((2, rows, block), lambda i: (0, 0, i)),
            pl.BlockSpec((slices, 2, block), lambda i: (0, 0, i)),
        ],
        out_specs=slab,
        out_shape=jax.ShapeDtypeStruct((slices, rows, width), jnp.float32),
    )(density, zhalo, rhalo)


def backward_grads(density, colour_raw, answers, smooth, step, slices_total):
    slices, rows, width = density.shape
    tiles = width // lanes
    block = lanes * backward_subs if tiles % backward_subs == 0 else lanes
    slab = pl.BlockSpec((slices, rows, block), lambda i: (0, 0, i))
    colours = pl.BlockSpec((3, slices, rows, block), lambda i: (0, 0, 0, i))
    return pl.pallas_call(
        functools.partial(backward_kernel, step=step, slices_total=float(slices_total)),
        grid=(width // block,),
        in_specs=[slab, colours, pl.BlockSpec(memory_space=pltpu.VMEM), slab],
        out_specs=[slab, colours],
        out_shape=[
            jax.ShapeDtypeStruct((slices, rows, width), jnp.float32),
            jax.ShapeDtypeStruct((3, slices, rows, width), jnp.float32),
        ],
        input_output_aliases={3: 0},
    )(density, colour_raw, answers, smooth)


def composite(parts, slab_rank, target_piece, slices_total):
    emitted, passing = (parts[:, :3], parts[:, 3])
    earlier = (slab_rank[None, :] < slab_rank[:, None]).astype(jnp.float32)[:, :, None, None]
    later = (slab_rank[None, :] > slab_rank[:, None]).astype(jnp.float32)[:, :, None, None, None]
    front = jnp.exp(jnp.sum(earlier * jnp.log(passing)[None], axis=1))
    weighted = front[:, None] * emitted
    behind = jnp.sum(later * weighted[None], axis=1) / (front * passing)[:, None]
    residual = jnp.sum(weighted, axis=0) - target_piece
    scaled_residual = slices_total * (front[:, None] * residual[None])
    scaled_behind = slices_total * (front * jnp.sum(residual[None] * behind, axis=1))
    folded = jnp.sum(scaled_residual * emitted, axis=1) + passing * scaled_behind
    return jnp.concatenate([scaled_residual, folded[:, None]], axis=1)


def halos(density_raw):
    depth_count = lax.axis_size("depth")
    rows_count = lax.axis_size("rows")
    depth_at = lax.axis_index("depth")
    rows_at = lax.axis_index("rows")
    up_d = [(i, i + 1) for i in range(depth_count - 1)]
    up_r = [(i, i + 1) for i in range(rows_count - 1)]
    first_slice = density_raw[:1]
    last_slice = density_raw[-1:]
    first_row = density_raw[:, :1]
    last_row = density_raw[:, -1:]
    prev_slice = lax.ppermute(last_slice, "depth", up_d)
    next_slice = lax.ppermute(first_slice, "depth", [(j, i) for i, j in up_d])
    prev_row = lax.ppermute(last_row, "rows", up_r)
    next_row = lax.ppermute(first_row, "rows", [(j, i) for i, j in up_r])
    prev_slice = jnp.where(depth_at > 0, prev_slice, first_slice)
    next_slice = jnp.where(depth_at < depth_count - 1, next_slice, last_slice)
    prev_row = jnp.where(rows_at > 0, prev_row, first_row)
    next_row = jnp.where(rows_at < rows_count - 1, next_row, last_row)
    zhalo = jnp.concatenate([prev_slice, next_slice], axis=0).astype(jnp.float32)
    rhalo = jnp.concatenate([prev_row, next_row], axis=1).astype(jnp.float32)
    return zhalo, rhalo


def local(density_raw, colour_raw, target, slab_rank):
    slices_dev, rows_dev, width = density_raw.shape
    depth_count = lax.axis_size("depth")
    slices_total = slices_dev * depth_count
    step = optical_depth / slices_total
    tiles, per_tile, chunk_rows = chunking(rows_dev, width, depth_count)
    partial_value = forward_partial(density_raw, colour_raw, step, depth_count)
    partial_value, after_forward = lax.optimization_barrier((partial_value, density_raw))
    zhalo, rhalo = halos(after_forward)
    received = lax.all_to_all(partial_value, "depth", 0, 0, tiled=True)
    position = lax.axis_index("depth")
    target_piece = lax.dynamic_slice(
        target,
        (0, (position % per_tile) * chunk_rows, (position // per_tile) * lanes),
        (3, chunk_rows, lanes),
    )
    answers = composite(received, slab_rank, target_piece, float(slices_total))
    returned = lax.all_to_all(answers, "depth", 0, 0, tiled=True)
    smooth = smooth_term(density_raw, zhalo, rhalo)
    return backward_grads(density_raw, colour_raw, returned, smooth, step, slices_total)


def solution(mesh):
    placed = (P("depth", "rows", None), P(None, "depth", "rows", None), P(None, "rows", None), P())
    return jax.shard_map(
        local,
        mesh=mesh,
        in_specs=placed,
        out_specs=(P("depth", "rows", None), P(None, "depth", "rows", None)),
        check_vma=False,
    )
```

```python
import functools

import jax
import jax.numpy as jnp
from jax import lax
from jax.experimental import pallas as pl
from jax.experimental.pallas import tpu as pltpu
from jax.sharding import PartitionSpec as P

optical_depth = 2.5
smooth_weight = 0.05
lanes = 128
forward_subs = 4
backward_subs = 2
forward_unroll = 32
backward_unroll = 8


log2e = 1.4426950408889634
ln2 = 0.6931471805599453


def softplus(x):
    return jnp.maximum(x, 0.0) + ln2 * jnp.log2(1.0 + jnp.exp2(jnp.abs(x) * -log2e))


def chunking(rows, width, depth_count):
    tiles = width // lanes
    per_tile = max(depth_count // tiles, 1)
    return tiles, per_tile, rows // per_tile


def forward_kernel(d_ref, c_ref, out_ref, *, step):
    slices, rows, block = d_ref.shape
    shape = (rows, lanes)
    subs = block // lanes
    per_tile = out_ref.shape[0] // subs
    chunk_rows = out_ref.shape[2]
    scale = -step * log2e

    for j in range(subs):
        cols = pl.ds(j * lanes, lanes)

        def body(z, carry):
            n, front, e0, e1, e2 = carry
            dtn = softplus(d_ref[z, :, cols].astype(jnp.float32)) * scale
            kept = jnp.exp2(dtn)
            lit = front * (1.0 - kept)
            n = n + dtn
            e0 = e0 + lit * jax.nn.sigmoid(c_ref[0, z, :, cols].astype(jnp.float32))
            e1 = e1 + lit * jax.nn.sigmoid(c_ref[1, z, :, cols].astype(jnp.float32))
            e2 = e2 + lit * jax.nn.sigmoid(c_ref[2, z, :, cols].astype(jnp.float32))
            return (n, front * kept, e0, e1, e2)

        zero = jnp.zeros(shape, jnp.float32)
        one = jnp.ones(shape, jnp.float32)
        n, _, e0, e1, e2 = lax.fori_loop(0, slices, body, (zero, one, zero, zero, zero), unroll=forward_unroll)
        values = (e0, e1, e2, jnp.exp2(n))
        for g in range(per_tile):
            for c in range(4):
                out_ref[j * per_tile + g, c] = values[c][g * chunk_rows:(g + 1) * chunk_rows]


def smooth_kernel(d_ref, zhalo_ref, rhalo_ref, out_ref):
    slices, rows, block = d_ref.shape
    shape = (rows, lanes)
    row = lax.broadcasted_iota(jnp.int32, shape, 0)
    first_row = row == 0
    last_row = row == shape[0] - 1

    for j in range(block // lanes):
        cols = pl.ds(j * lanes, lanes)

        def body(z, carry):
            d_prev, d = carry
            d_next = jnp.where(
                z + 1 < slices,
                d_ref[jnp.minimum(z + 1, slices - 1), :, cols].astype(jnp.float32),
                zhalo_ref[1, :, cols],
            )
            rims = rhalo_ref[z, :, cols]
            upper = jnp.where(first_row, rims[0:1], pltpu.roll(d, 1, 0))
            lower = jnp.where(last_row, rims[1:2], pltpu.roll(d, shape[0] - 1, 0))
            out_ref[z, :, cols] = 2.0 * smooth_weight * (
                (d - d_prev) + (d - d_next) + (d - upper) + (d - lower)
            )
            return (d, d_next)

        start = (zhalo_ref[0, :, cols], d_ref[0, :, cols].astype(jnp.float32))
        lax.fori_loop(0, slices, body, start, unroll=2)


def backward_kernel(d_ref, c_ref, ans_ref, smooth_ref, gd_ref, gc_ref, *, step, slices_total):
    slices, rows, block = d_ref.shape
    shape = (rows, lanes)
    subs = block // lanes
    per_tile = ans_ref.shape[0] // (pl.num_programs(0) * subs)
    scale = -step * log2e
    gain = optical_depth / slices_total

    for j in range(subs):
        cols = pl.ds(j * lanes, lanes)
        base = (pl.program_id(0) * subs + j) * per_tile

        def pixel(c):
            if per_tile == 1:
                return ans_ref[base, c]
            return jnp.concatenate([ans_ref[base + g, c] for g in range(per_tile)], axis=0)

        def body(z, carry):
            n, front, w0, w1, w2 = carry
            d = d_ref[z, :, cols].astype(jnp.float32)
            dtn = softplus(d) * scale
            lit = front * (1.0 - jnp.exp2(dtn))
            n_next = n + dtn
            through = jnp.exp2(n_next)
            inv = jnp.exp2(-n_next)
            col = [jax.nn.sigmoid(c_ref[c, z, :, cols].astype(jnp.float32)) for c in range(3)]
            lit_col = [lit * col[c] for c in range(3)]
            w = [w0 + lit_col[0], w1 + lit_col[1], w2 + lit_col[2]]
            res = [pixel(c) for c in range(3)]
            emitted = res[0] * col[0] + res[1] * col[1] + res[2] * col[2]
            left = res[0] * w[0] + res[1] * w[1] + res[2] * w[2]
            inner = emitted - inv * (pixel(3) - left)
            for c in range(3):
                gc_ref[c, z, :, cols] = res[c] * lit_col[c] * (1.0 - col[c])
            gd_ref[z, :, cols] = gain * through * jax.nn.sigmoid(d) * inner + smooth_ref[z, :, cols]
            return (n_next, through, w[0], w[1], w[2])

        zero = jnp.zeros(shape, jnp.float32)
        one = jnp.ones(shape, jnp.float32)
        lax.fori_loop(0, slices, body, (zero, one, zero, zero, zero), unroll=backward_unroll)


def forward_partial(density, colour_raw, step, depth_count):
    slices, rows, width = density.shape
    tiles, per_tile, chunk_rows = chunking(rows, width, depth_count)
    block = lanes * forward_subs if tiles % forward_subs == 0 else lanes
    return pl.pallas_call(
        functools.partial(forward_kernel, step=step),
        grid=(width // block,),
        in_specs=[
            pl.BlockSpec((slices, rows, block), lambda i: (0, 0, i)),
            pl.BlockSpec((3, slices, rows, block), lambda i: (0, 0, 0, i)),
        ],
        out_specs=pl.BlockSpec(
            (per_tile * (block // lanes), 4, chunk_rows, lanes), lambda i: (i, 0, 0, 0)
        ),
        out_shape=jax.ShapeDtypeStruct((tiles * per_tile, 4, chunk_rows, lanes), jnp.float32),
    )(density, colour_raw)


def smooth_term(density, zhalo, rhalo):
    slices, rows, width = density.shape
    tiles = width // lanes
    block = lanes * forward_subs if tiles % forward_subs == 0 else lanes
    slab = pl.BlockSpec((slices, rows, block), lambda i: (0, 0, i))
    return pl.pallas_call(
        smooth_kernel,
        grid=(width // block,),
        in_specs=[
            slab,
            pl.BlockSpec((2, rows, block), lambda i: (0, 0, i)),
            pl.BlockSpec((slices, 2, block), lambda i: (0, 0, i)),
        ],
        out_specs=slab,
        out_shape=jax.ShapeDtypeStruct((slices, rows, width), jnp.float32),
    )(density, zhalo, rhalo)


def backward_grads(density, colour_raw, answers, smooth, step, slices_total):
    slices, rows, width = density.shape
    tiles = width // lanes
    block = lanes * backward_subs if tiles % backward_subs == 0 else lanes
    slab = pl.BlockSpec((slices, rows, block), lambda i: (0, 0, i))
    colours = pl.BlockSpec((3, slices, rows, block), lambda i: (0, 0, 0, i))
    return pl.pallas_call(
        functools.partial(backward_kernel, step=step, slices_total=float(slices_total)),
        grid=(width // block,),
        in_specs=[slab, colours, pl.BlockSpec(memory_space=pltpu.VMEM), slab],
        out_specs=[slab, colours],
        out_shape=[
            jax.ShapeDtypeStruct((slices, rows, width), jnp.float32),
            jax.ShapeDtypeStruct((3, slices, rows, width), jnp.float32),
        ],
        input_output_aliases={3: 0},
    )(density, colour_raw, answers, smooth)


def composite_kernel(rank_ref, parts_ref, target_ref, out_ref, front_ref, *, scale):
    count = parts_ref.shape[0]
    shape = parts_ref.shape[2:]
    zero = jnp.zeros(shape, jnp.float32)

    def forward(s, total):
        acc = zero
        for j in range(count):
            acc = acc + jnp.where(rank_ref[j] < rank_ref[s], jnp.log2(parts_ref[j, 3]), 0.0)
        front = jnp.exp2(acc)
        front_ref[s] = front
        return tuple(total[c] + front * parts_ref[s, c] for c in range(3))

    total = lax.fori_loop(0, count, forward, (zero, zero, zero))
    residual = [total[c] - target_ref[c] for c in range(3)]

    def backward(s, carry):
        behind = [zero, zero, zero]
        for j in range(count):
            later = rank_ref[j] > rank_ref[s]
            for c in range(3):
                behind[c] = behind[c] + jnp.where(later, front_ref[j] * parts_ref[j, c], 0.0)
        front = front_ref[s]
        passing = parts_ref[s, 3]
        through = front * passing
        mixed = residual[0] * (behind[0] / through)
        mixed = mixed + residual[1] * (behind[1] / through)
        mixed = mixed + residual[2] * (behind[2] / through)
        scaled_behind = scale * (front * mixed)
        folded = passing * scaled_behind
        for c in range(3):
            scaled = scale * (front * residual[c])
            out_ref[s, c] = scaled
            folded = folded + scaled * parts_ref[s, c]
        out_ref[s, 3] = folded
        return carry

    lax.fori_loop(0, count, backward, 0)


def composite(parts, slab_rank, target_piece, slices_total):
    count = parts.shape[0]
    vmem = pl.BlockSpec(memory_space=pltpu.VMEM)
    return pl.pallas_call(
        functools.partial(composite_kernel, scale=slices_total),
        in_specs=[pl.BlockSpec(memory_space=pltpu.SMEM), vmem, vmem],
        out_specs=vmem,
        out_shape=jax.ShapeDtypeStruct(parts.shape, jnp.float32),
        scratch_shapes=[pltpu.VMEM((count,) + parts.shape[2:], jnp.float32)],
    )(slab_rank, parts, target_piece)


def halos(density_raw):
    depth_count = lax.axis_size("depth")
    rows_count = lax.axis_size("rows")
    depth_at = lax.axis_index("depth")
    rows_at = lax.axis_index("rows")
    up_d = [(i, i + 1) for i in range(depth_count - 1)]
    up_r = [(i, i + 1) for i in range(rows_count - 1)]
    first_slice = density_raw[:1]
    last_slice = density_raw[-1:]
    first_row = density_raw[:, :1]
    last_row = density_raw[:, -1:]
    prev_slice = lax.ppermute(last_slice, "depth", up_d)
    next_slice = lax.ppermute(first_slice, "depth", [(j, i) for i, j in up_d])
    prev_row = lax.ppermute(last_row, "rows", up_r)
    next_row = lax.ppermute(first_row, "rows", [(j, i) for i, j in up_r])
    prev_slice = jnp.where(depth_at > 0, prev_slice, first_slice)
    next_slice = jnp.where(depth_at < depth_count - 1, next_slice, last_slice)
    prev_row = jnp.where(rows_at > 0, prev_row, first_row)
    next_row = jnp.where(rows_at < rows_count - 1, next_row, last_row)
    zhalo = jnp.concatenate([prev_slice, next_slice], axis=0).astype(jnp.float32)
    rhalo = jnp.concatenate([prev_row, next_row], axis=1).astype(jnp.float32)
    return zhalo, rhalo


def local(density_raw, colour_raw, target, slab_rank):
    slices_dev, rows_dev, width = density_raw.shape
    depth_count = lax.axis_size("depth")
    slices_total = slices_dev * depth_count
    step = optical_depth / slices_total
    tiles, per_tile, chunk_rows = chunking(rows_dev, width, depth_count)
    partial_value = forward_partial(density_raw, colour_raw, step, depth_count)
    partial_value, after_forward = lax.optimization_barrier((partial_value, density_raw))
    zhalo, rhalo = halos(after_forward)
    received = lax.all_to_all(partial_value, "depth", 0, 0, tiled=True)
    position = lax.axis_index("depth")
    target_piece = lax.dynamic_slice(
        target,
        (0, (position % per_tile) * chunk_rows, (position // per_tile) * lanes),
        (3, chunk_rows, lanes),
    )
    answers = composite(received, slab_rank, target_piece, float(slices_total))
    returned = lax.all_to_all(answers, "depth", 0, 0, tiled=True)
    smooth = smooth_term(density_raw, zhalo, rhalo)
    return backward_grads(density_raw, colour_raw, returned, smooth, step, slices_total)


def solution(mesh):
    placed = (P("depth", "rows", None), P(None, "depth", "rows", None), P(None, "rows", None), P())
    return jax.shard_map(
        local,
        mesh=mesh,
        in_specs=placed,
        out_specs=(P("depth", "rows", None), P(None, "depth", "rows", None)),
        check_vma=False,
    )
```

```python
import functools

import jax
import jax.numpy as jnp
from jax import lax
from jax.experimental import pallas as pl
from jax.experimental.pallas import tpu as pltpu
from jax.sharding import PartitionSpec as P

optical_depth = 2.5
smooth_weight = 0.05
lanes = 128
forward_subs = 4
backward_subs = 2
forward_unroll = 32
backward_unroll = 8


log2e = 1.4426950408889634
ln2 = 0.6931471805599453


def softplus(x):
    return jnp.maximum(x, 0.0) + ln2 * jnp.log2(1.0 + jnp.exp2(jnp.abs(x) * -log2e))


def chunking(rows, width, depth_count):
    tiles = width // lanes
    per_tile = max(depth_count // tiles, 1)
    return tiles, per_tile, rows // per_tile


def forward_kernel(d_ref, c_ref, out_ref, *, step):
    slices, rows, block = d_ref.shape
    shape = (rows, lanes)
    subs = block // lanes
    per_tile = out_ref.shape[0] // subs
    chunk_rows = out_ref.shape[2]
    scale = -step * log2e

    for j in range(subs):
        cols = pl.ds(j * lanes, lanes)

        def body(z, carry):
            n, front, e0, e1, e2 = carry
            dtn = softplus(d_ref[z, :, cols].astype(jnp.float32)) * scale
            kept = jnp.exp2(dtn)
            lit = front * (1.0 - kept)
            n = n + dtn
            e0 = e0 + lit * jax.nn.sigmoid(c_ref[0, z, :, cols].astype(jnp.float32))
            e1 = e1 + lit * jax.nn.sigmoid(c_ref[1, z, :, cols].astype(jnp.float32))
            e2 = e2 + lit * jax.nn.sigmoid(c_ref[2, z, :, cols].astype(jnp.float32))
            return (n, front * kept, e0, e1, e2)

        zero = jnp.zeros(shape, jnp.float32)
        one = jnp.ones(shape, jnp.float32)
        n, _, e0, e1, e2 = lax.fori_loop(0, slices, body, (zero, one, zero, zero, zero), unroll=forward_unroll)
        values = (e0, e1, e2, jnp.exp2(n))
        for g in range(per_tile):
            for c in range(4):
                out_ref[j * per_tile + g, c] = values[c][g * chunk_rows:(g + 1) * chunk_rows]


def smooth_kernel(d_ref, zhalo_ref, rhalo_ref, out_ref):
    slices, rows, block = d_ref.shape
    shape = (rows, lanes)
    row = lax.broadcasted_iota(jnp.int32, shape, 0)
    first_row = row == 0
    last_row = row == shape[0] - 1

    for j in range(block // lanes):
        cols = pl.ds(j * lanes, lanes)

        def body(z, carry):
            d_prev, d = carry
            d_next = jnp.where(
                z + 1 < slices,
                d_ref[jnp.minimum(z + 1, slices - 1), :, cols].astype(jnp.float32),
                zhalo_ref[1, :, cols],
            )
            rims = rhalo_ref[z, :, cols]
            upper = jnp.where(first_row, rims[0:1], pltpu.roll(d, 1, 0))
            lower = jnp.where(last_row, rims[1:2], pltpu.roll(d, shape[0] - 1, 0))
            out_ref[z, :, cols] = 2.0 * smooth_weight * (
                (d - d_prev) + (d - d_next) + (d - upper) + (d - lower)
            )
            return (d, d_next)

        start = (zhalo_ref[0, :, cols], d_ref[0, :, cols].astype(jnp.float32))
        lax.fori_loop(0, slices, body, start, unroll=2)


def backward_kernel(d_ref, c_ref, ans_ref, smooth_ref, gd_ref, gc_ref, *, step, slices_total):
    slices, rows, block = d_ref.shape
    shape = (rows, lanes)
    subs = block // lanes
    per_tile = ans_ref.shape[0] // (pl.num_programs(0) * subs)
    scale = -step * log2e
    gain = optical_depth / slices_total

    for j in range(subs):
        cols = pl.ds(j * lanes, lanes)
        base = (pl.program_id(0) * subs + j) * per_tile

        def pixel(c):
            if per_tile == 1:
                return ans_ref[base, c]
            return jnp.concatenate([ans_ref[base + g, c] for g in range(per_tile)], axis=0)

        def body(z, carry):
            n, front, w0, w1, w2 = carry
            d = d_ref[z, :, cols].astype(jnp.float32)
            dtn = softplus(d) * scale
            lit = front * (1.0 - jnp.exp2(dtn))
            n_next = n + dtn
            through = jnp.exp2(n_next)
            inv = jnp.exp2(-n_next)
            col = [jax.nn.sigmoid(c_ref[c, z, :, cols].astype(jnp.float32)) for c in range(3)]
            lit_col = [lit * col[c] for c in range(3)]
            w = [w0 + lit_col[0], w1 + lit_col[1], w2 + lit_col[2]]
            res = [pixel(c) for c in range(3)]
            emitted = res[0] * col[0] + res[1] * col[1] + res[2] * col[2]
            left = res[0] * w[0] + res[1] * w[1] + res[2] * w[2]
            inner = emitted - inv * (pixel(3) - left)
            for c in range(3):
                gc_ref[c, z, :, cols] = res[c] * lit_col[c] * (1.0 - col[c])
            gd_ref[z, :, cols] = gain * through * jax.nn.sigmoid(d) * inner + smooth_ref[z, :, cols]
            return (n_next, through, w[0], w[1], w[2])

        zero = jnp.zeros(shape, jnp.float32)
        one = jnp.ones(shape, jnp.float32)
        lax.fori_loop(0, slices, body, (zero, one, zero, zero, zero), unroll=backward_unroll)


def forward_partial(density, colour_raw, step, depth_count):
    slices, rows, width = density.shape
    tiles, per_tile, chunk_rows = chunking(rows, width, depth_count)
    block = lanes * forward_subs if tiles % forward_subs == 0 else lanes
    return pl.pallas_call(
        functools.partial(forward_kernel, step=step),
        grid=(width // block,),
        in_specs=[
            pl.BlockSpec((slices, rows, block), lambda i: (0, 0, i)),
            pl.BlockSpec((3, slices, rows, block), lambda i: (0, 0, 0, i)),
        ],
        out_specs=pl.BlockSpec(
            (per_tile * (block // lanes), 4, chunk_rows, lanes), lambda i: (i, 0, 0, 0)
        ),
        out_shape=jax.ShapeDtypeStruct((tiles * per_tile, 4, chunk_rows, lanes), jnp.float32),
    )(density, colour_raw)


def smooth_term(density, zhalo, rhalo):
    slices, rows, width = density.shape
    tiles = width // lanes
    block = lanes * forward_subs if tiles % forward_subs == 0 else lanes
    slab = pl.BlockSpec((slices, rows, block), lambda i: (0, 0, i))
    return pl.pallas_call(
        smooth_kernel,
        grid=(width // block,),
        in_specs=[
            slab,
            pl.BlockSpec((2, rows, block), lambda i: (0, 0, i)),
            pl.BlockSpec((slices, 2, block), lambda i: (0, 0, i)),
        ],
        out_specs=slab,
        out_shape=jax.ShapeDtypeStruct((slices, rows, width), jnp.float32),
    )(density, zhalo, rhalo)


def backward_grads(density, colour_raw, answers, smooth, step, slices_total):
    slices, rows, width = density.shape
    tiles = width // lanes
    block = lanes * backward_subs if tiles % backward_subs == 0 else lanes
    slab = pl.BlockSpec((slices, rows, block), lambda i: (0, 0, i))
    colours = pl.BlockSpec((3, slices, rows, block), lambda i: (0, 0, 0, i))
    return pl.pallas_call(
        functools.partial(backward_kernel, step=step, slices_total=float(slices_total)),
        grid=(width // block,),
        in_specs=[slab, colours, pl.BlockSpec(memory_space=pltpu.VMEM), slab],
        out_specs=[slab, colours],
        out_shape=[
            jax.ShapeDtypeStruct((slices, rows, width), jnp.float32),
            jax.ShapeDtypeStruct((3, slices, rows, width), jnp.float32),
        ],
        input_output_aliases={3: 0},
    )(density, colour_raw, answers, smooth)


def composite(parts, slab_rank, target_piece, slices_total):
    emitted, passing = (parts[:, :3], parts[:, 3])
    earlier = (slab_rank[None, :] < slab_rank[:, None]).astype(jnp.float32)[:, :, None, None]
    later = (slab_rank[None, :] > slab_rank[:, None]).astype(jnp.float32)[:, :, None, None, None]
    front = jnp.exp(jnp.sum(earlier * jnp.log(passing)[None], axis=1))
    weighted = front[:, None] * emitted
    behind = jnp.sum(later * weighted[None], axis=1) / (front * passing)[:, None]
    residual = jnp.sum(weighted, axis=0) - target_piece
    scaled_residual = slices_total * (front[:, None] * residual[None])
    scaled_behind = slices_total * (front * jnp.sum(residual[None] * behind, axis=1))
    folded = jnp.sum(scaled_residual * emitted, axis=1) + passing * scaled_behind
    return jnp.concatenate([scaled_residual, folded[:, None]], axis=1)


def depth_halos(density_raw):
    depth_count = lax.axis_size("depth")
    depth_at = lax.axis_index("depth")
    up = [(i, i + 1) for i in range(depth_count - 1)]
    first_slice = density_raw[:1]
    last_slice = density_raw[-1:]
    prev_slice = lax.ppermute(last_slice, "depth", up)
    next_slice = lax.ppermute(first_slice, "depth", [(j, i) for i, j in up])
    prev_slice = jnp.where(depth_at > 0, prev_slice, first_slice)
    next_slice = jnp.where(depth_at < depth_count - 1, next_slice, last_slice)
    return jnp.concatenate([prev_slice, next_slice], axis=0).astype(jnp.float32)


def row_halos(density_raw):
    rows_count = lax.axis_size("rows")
    rows_at = lax.axis_index("rows")
    up = [(i, i + 1) for i in range(rows_count - 1)]
    first_row = density_raw[:, :1]
    last_row = density_raw[:, -1:]
    prev_row = lax.ppermute(last_row, "rows", up)
    next_row = lax.ppermute(first_row, "rows", [(j, i) for i, j in up])
    prev_row = jnp.where(rows_at > 0, prev_row, first_row)
    next_row = jnp.where(rows_at < rows_count - 1, next_row, last_row)
    return jnp.concatenate([prev_row, next_row], axis=1).astype(jnp.float32)


def local(density_raw, colour_raw, target, slab_rank):
    slices_dev, rows_dev, width = density_raw.shape
    depth_count = lax.axis_size("depth")
    slices_total = slices_dev * depth_count
    step = optical_depth / slices_total
    tiles, per_tile, chunk_rows = chunking(rows_dev, width, depth_count)
    partial_value = forward_partial(density_raw, colour_raw, step, depth_count)
    partial_value, after_forward = lax.optimization_barrier((partial_value, density_raw))
    zhalo = depth_halos(after_forward)
    received = lax.all_to_all(partial_value, "depth", 0, 0, tiled=True)
    position = lax.axis_index("depth")
    target_piece = lax.dynamic_slice(
        target,
        (0, (position % per_tile) * chunk_rows, (position // per_tile) * lanes),
        (3, chunk_rows, lanes),
    )
    answers = composite(received, slab_rank, target_piece, float(slices_total))
    answers, after_composite = lax.optimization_barrier((answers, density_raw))
    rhalo = row_halos(after_composite)
    returned = lax.all_to_all(answers, "depth", 0, 0, tiled=True)
    smooth = smooth_term(density_raw, zhalo, rhalo)
    return backward_grads(density_raw, colour_raw, returned, smooth, step, slices_total)


def solution(mesh):
    placed = (P("depth", "rows", None), P(None, "depth", "rows", None), P(None, "rows", None), P())
    return jax.shard_map(
        local,
        mesh=mesh,
        in_specs=placed,
        out_specs=(P("depth", "rows", None), P(None, "depth", "rows", None)),
        check_vma=False,
    )
```

```python
import functools

import jax
import jax.numpy as jnp
from jax import lax
from jax.experimental import pallas as pl
from jax.experimental.pallas import tpu as pltpu
from jax.sharding import PartitionSpec as P

optical_depth = 2.5
smooth_weight = 0.05
lanes = 128
forward_subs = 4
backward_subs = 2
forward_unroll = 32
backward_unroll = 8


log2e = 1.4426950408889634
ln2 = 0.6931471805599453


def softplus(x):
    return jnp.maximum(x, 0.0) + ln2 * jnp.log2(1.0 + jnp.exp2(jnp.abs(x) * -log2e))


def chunking(rows, width, depth_count):
    tiles = width // lanes
    per_tile = max(depth_count // tiles, 1)
    return tiles, per_tile, rows // per_tile


def forward_kernel(d_ref, c_ref, out_ref, *, step):
    slices, rows, block = d_ref.shape
    shape = (rows, lanes)
    subs = block // lanes
    per_tile = out_ref.shape[0] // subs
    chunk_rows = out_ref.shape[2]
    scale = -step * log2e

    for j in range(subs):
        cols = pl.ds(j * lanes, lanes)

        def body(z, carry):
            n, front, e0, e1, e2 = carry
            dtn = softplus(d_ref[z, :, cols].astype(jnp.float32)) * scale
            kept = jnp.exp2(dtn)
            lit = front * (1.0 - kept)
            n = n + dtn
            e0 = e0 + lit * jax.nn.sigmoid(c_ref[0, z, :, cols].astype(jnp.float32))
            e1 = e1 + lit * jax.nn.sigmoid(c_ref[1, z, :, cols].astype(jnp.float32))
            e2 = e2 + lit * jax.nn.sigmoid(c_ref[2, z, :, cols].astype(jnp.float32))
            return (n, front * kept, e0, e1, e2)

        zero = jnp.zeros(shape, jnp.float32)
        one = jnp.ones(shape, jnp.float32)
        n, _, e0, e1, e2 = lax.fori_loop(0, slices, body, (zero, one, zero, zero, zero), unroll=forward_unroll)
        values = (e0, e1, e2, jnp.exp2(n))
        for g in range(per_tile):
            for c in range(4):
                out_ref[j * per_tile + g, c] = values[c][g * chunk_rows:(g + 1) * chunk_rows]


def smooth_kernel(d_ref, zhalo_ref, rhalo_ref, out_ref):
    slices, rows, block = d_ref.shape
    shape = (rows, lanes)
    row = lax.broadcasted_iota(jnp.int32, shape, 0)
    first_row = row == 0
    last_row = row == shape[0] - 1

    for j in range(block // lanes):
        cols = pl.ds(j * lanes, lanes)

        def body(z, carry):
            d_prev, d = carry
            d_next = jnp.where(
                z + 1 < slices,
                d_ref[jnp.minimum(z + 1, slices - 1), :, cols].astype(jnp.float32),
                zhalo_ref[1, :, cols],
            )
            rims = rhalo_ref[z, :, cols]
            upper = jnp.where(first_row, rims[0:1], pltpu.roll(d, 1, 0))
            lower = jnp.where(last_row, rims[1:2], pltpu.roll(d, shape[0] - 1, 0))
            out_ref[z, :, cols] = 2.0 * smooth_weight * (
                (d - d_prev) + (d - d_next) + (d - upper) + (d - lower)
            )
            return (d, d_next)

        start = (zhalo_ref[0, :, cols], d_ref[0, :, cols].astype(jnp.float32))
        lax.fori_loop(0, slices, body, start, unroll=2)


def backward_kernel(d_ref, c_ref, ans_ref, smooth_ref, gd_ref, gc_ref, *, step, slices_total):
    slices, rows, block = d_ref.shape
    shape = (rows, lanes)
    subs = block // lanes
    per_tile = ans_ref.shape[0] // (pl.num_programs(0) * subs)
    scale = -step * log2e
    gain = optical_depth / slices_total

    for j in range(subs):
        cols = pl.ds(j * lanes, lanes)
        base = (pl.program_id(0) * subs + j) * per_tile

        def pixel(c):
            if per_tile == 1:
                return ans_ref[base, c]
            return jnp.concatenate([ans_ref[base + g, c] for g in range(per_tile)], axis=0)

        def body(z, carry):
            n, front, w0, w1, w2 = carry
            d = d_ref[z, :, cols].astype(jnp.float32)
            dtn = softplus(d) * scale
            lit = front * (1.0 - jnp.exp2(dtn))
            n_next = n + dtn
            through = jnp.exp2(n_next)
            inv = jnp.exp2(-n_next)
            col = [jax.nn.sigmoid(c_ref[c, z, :, cols].astype(jnp.float32)) for c in range(3)]
            lit_col = [lit * col[c] for c in range(3)]
            w = [w0 + lit_col[0], w1 + lit_col[1], w2 + lit_col[2]]
            res = [pixel(c) for c in range(3)]
            emitted = res[0] * col[0] + res[1] * col[1] + res[2] * col[2]
            left = res[0] * w[0] + res[1] * w[1] + res[2] * w[2]
            inner = emitted - inv * (pixel(3) - left)
            for c in range(3):
                gc_ref[c, z, :, cols] = res[c] * lit_col[c] * (1.0 - col[c])
            gd_ref[z, :, cols] = gain * through * jax.nn.sigmoid(d) * inner + smooth_ref[z, :, cols]
            return (n_next, through, w[0], w[1], w[2])

        zero = jnp.zeros(shape, jnp.float32)
        one = jnp.ones(shape, jnp.float32)
        lax.fori_loop(0, slices, body, (zero, one, zero, zero, zero), unroll=backward_unroll)


def forward_partial(density, colour_raw, step, depth_count):
    slices, rows, width = density.shape
    tiles, per_tile, chunk_rows = chunking(rows, width, depth_count)
    block = lanes * forward_subs if tiles % forward_subs == 0 else lanes
    return pl.pallas_call(
        functools.partial(forward_kernel, step=step),
        grid=(width // block,),
        in_specs=[
            pl.BlockSpec((slices, rows, block), lambda i: (0, 0, i)),
            pl.BlockSpec((3, slices, rows, block), lambda i: (0, 0, 0, i)),
        ],
        out_specs=pl.BlockSpec(
            (per_tile * (block // lanes), 4, chunk_rows, lanes), lambda i: (i, 0, 0, 0)
        ),
        out_shape=jax.ShapeDtypeStruct((tiles * per_tile, 4, chunk_rows, lanes), jnp.float32),
    )(density, colour_raw)


def smooth_term(density, zhalo, rhalo):
    slices, rows, width = density.shape
    tiles = width // lanes
    block = lanes * forward_subs if tiles % forward_subs == 0 else lanes
    slab = pl.BlockSpec((slices, rows, block), lambda i: (0, 0, i))
    return pl.pallas_call(
        smooth_kernel,
        grid=(width // block,),
        in_specs=[
            slab,
            pl.BlockSpec((2, rows, block), lambda i: (0, 0, i)),
            pl.BlockSpec((slices, 2, block), lambda i: (0, 0, i)),
        ],
        out_specs=slab,
        out_shape=jax.ShapeDtypeStruct((slices, rows, width), jnp.float32),
    )(density, zhalo, rhalo)


def backward_grads(density, colour_raw, answers, smooth, step, slices_total):
    slices, rows, width = density.shape
    tiles = width // lanes
    block = lanes * backward_subs if tiles % backward_subs == 0 else lanes
    slab = pl.BlockSpec((slices, rows, block), lambda i: (0, 0, i))
    colours = pl.BlockSpec((3, slices, rows, block), lambda i: (0, 0, 0, i))
    return pl.pallas_call(
        functools.partial(backward_kernel, step=step, slices_total=float(slices_total)),
        grid=(width // block,),
        in_specs=[slab, colours, pl.BlockSpec(memory_space=pltpu.VMEM), slab],
        out_specs=[slab, colours],
        out_shape=[
            jax.ShapeDtypeStruct((slices, rows, width), jnp.float32),
            jax.ShapeDtypeStruct((3, slices, rows, width), jnp.float32),
        ],
        input_output_aliases={3: 0},
    )(density, colour_raw, pltpu.with_memory_space_constraint(answers, pltpu.VMEM), smooth)


def composite(parts, slab_rank, target_piece, slices_total):
    emitted, passing = (parts[:, :3], parts[:, 3])
    earlier = (slab_rank[None, :] < slab_rank[:, None]).astype(jnp.float32)[:, :, None, None]
    later = (slab_rank[None, :] > slab_rank[:, None]).astype(jnp.float32)[:, :, None, None, None]
    front = jnp.exp(jnp.sum(earlier * jnp.log(passing)[None], axis=1))
    weighted = front[:, None] * emitted
    behind = jnp.sum(later * weighted[None], axis=1) / (front * passing)[:, None]
    residual = jnp.sum(weighted, axis=0) - target_piece
    scaled_residual = slices_total * (front[:, None] * residual[None])
    scaled_behind = slices_total * (front * jnp.sum(residual[None] * behind, axis=1))
    folded = jnp.sum(scaled_residual * emitted, axis=1) + passing * scaled_behind
    return jnp.concatenate([scaled_residual, folded[:, None]], axis=1)


def halos(density_raw):
    depth_count = lax.axis_size("depth")
    rows_count = lax.axis_size("rows")
    depth_at = lax.axis_index("depth")
    rows_at = lax.axis_index("rows")
    up_d = [(i, i + 1) for i in range(depth_count - 1)]
    up_r = [(i, i + 1) for i in range(rows_count - 1)]
    first_slice = density_raw[:1]
    last_slice = density_raw[-1:]
    first_row = density_raw[:, :1]
    last_row = density_raw[:, -1:]
    prev_slice = lax.ppermute(last_slice, "depth", up_d)
    next_slice = lax.ppermute(first_slice, "depth", [(j, i) for i, j in up_d])
    prev_row = lax.ppermute(last_row, "rows", up_r)
    next_row = lax.ppermute(first_row, "rows", [(j, i) for i, j in up_r])
    prev_slice = jnp.where(depth_at > 0, prev_slice, first_slice)
    next_slice = jnp.where(depth_at < depth_count - 1, next_slice, last_slice)
    prev_row = jnp.where(rows_at > 0, prev_row, first_row)
    next_row = jnp.where(rows_at < rows_count - 1, next_row, last_row)
    zhalo = jnp.concatenate([prev_slice, next_slice], axis=0).astype(jnp.float32)
    rhalo = jnp.concatenate([prev_row, next_row], axis=1).astype(jnp.float32)
    return zhalo, rhalo


def local(density_raw, colour_raw, target, slab_rank):
    slices_dev, rows_dev, width = density_raw.shape
    depth_count = lax.axis_size("depth")
    slices_total = slices_dev * depth_count
    step = optical_depth / slices_total
    tiles, per_tile, chunk_rows = chunking(rows_dev, width, depth_count)
    partial_value = forward_partial(density_raw, colour_raw, step, depth_count)
    partial_value, after_forward = lax.optimization_barrier((partial_value, density_raw))
    zhalo, rhalo = halos(after_forward)
    received = lax.all_to_all(partial_value, "depth", 0, 0, tiled=True)
    position = lax.axis_index("depth")
    target_piece = lax.dynamic_slice(
        target,
        (0, (position % per_tile) * chunk_rows, (position // per_tile) * lanes),
        (3, chunk_rows, lanes),
    )
    answers = composite(received, slab_rank, target_piece, float(slices_total))
    returned = lax.all_to_all(answers, "depth", 0, 0, tiled=True)
    smooth = smooth_term(density_raw, zhalo, rhalo)
    return backward_grads(density_raw, colour_raw, returned, smooth, step, slices_total)


def solution(mesh):
    placed = (P("depth", "rows", None), P(None, "depth", "rows", None), P(None, "rows", None), P())
    return jax.shard_map(
        local,
        mesh=mesh,
        in_specs=placed,
        out_specs=(P("depth", "rows", None), P(None, "depth", "rows", None)),
        check_vma=False,
    )
```

```python
import functools

import jax
import jax.numpy as jnp
from jax import lax
from jax.experimental import pallas as pl
from jax.experimental.pallas import tpu as pltpu
from jax.sharding import PartitionSpec as P

optical_depth = 2.5
smooth_weight = 0.05
lanes = 128
forward_subs = 4
backward_subs = 2
forward_unroll = 32
backward_unroll = 8


log2e = 1.4426950408889634
ln2 = 0.6931471805599453


def softplus(x):
    return jnp.maximum(x, 0.0) + ln2 * jnp.log2(1.0 + jnp.exp2(jnp.abs(x) * -log2e))


def chunking(rows, width, depth_count):
    tiles = width // lanes
    per_tile = max(depth_count // tiles, 1)
    return tiles, per_tile, rows // per_tile


def forward_kernel(d_ref, c_ref, out_ref, *, step):
    slices, rows, block = d_ref.shape
    shape = (rows, lanes)
    subs = block // lanes
    per_tile = out_ref.shape[0] // subs
    chunk_rows = out_ref.shape[2]
    scale = -step * log2e

    for j in range(subs):
        cols = pl.ds(j * lanes, lanes)

        def body(z, carry):
            n, front, e0, e1, e2 = carry
            dtn = softplus(d_ref[z, :, cols].astype(jnp.float32)) * scale
            kept = jnp.exp2(dtn)
            lit = front * (1.0 - kept)
            n = n + dtn
            e0 = e0 + lit * jax.nn.sigmoid(c_ref[0, z, :, cols].astype(jnp.float32))
            e1 = e1 + lit * jax.nn.sigmoid(c_ref[1, z, :, cols].astype(jnp.float32))
            e2 = e2 + lit * jax.nn.sigmoid(c_ref[2, z, :, cols].astype(jnp.float32))
            return (n, front * kept, e0, e1, e2)

        zero = jnp.zeros(shape, jnp.float32)
        one = jnp.ones(shape, jnp.float32)
        n, _, e0, e1, e2 = lax.fori_loop(0, slices, body, (zero, one, zero, zero, zero), unroll=forward_unroll)
        values = (e0, e1, e2, jnp.exp2(n))
        for g in range(per_tile):
            for c in range(4):
                out_ref[j * per_tile + g, c] = values[c][g * chunk_rows:(g + 1) * chunk_rows]


def smooth_kernel(d_ref, zhalo_ref, rhalo_ref, out_ref):
    slices, rows, block = d_ref.shape
    shape = (rows, lanes)
    row = lax.broadcasted_iota(jnp.int32, shape, 0)
    first_row = row == 0
    last_row = row == shape[0] - 1

    for j in range(block // lanes):
        cols = pl.ds(j * lanes, lanes)
        place = pl.ds(pl.multiple_of((pl.program_id(0) * (block // lanes) + j) * lanes, lanes), lanes)

        def body(z, carry):
            d_prev, d = carry
            d_next = jnp.where(
                z + 1 < slices,
                d_ref[jnp.minimum(z + 1, slices - 1), :, cols].astype(jnp.float32),
                zhalo_ref[1, :, cols],
            )
            rims = rhalo_ref[z, :, cols]
            upper = jnp.where(first_row, rims[0:1], pltpu.roll(d, 1, 0))
            lower = jnp.where(last_row, rims[1:2], pltpu.roll(d, shape[0] - 1, 0))
            out_ref[z, :, place] = 2.0 * smooth_weight * (
                (d - d_prev) + (d - d_next) + (d - upper) + (d - lower)
            )
            return (d, d_next)

        start = (zhalo_ref[0, :, cols], d_ref[0, :, cols].astype(jnp.float32))
        lax.fori_loop(0, slices, body, start, unroll=2)


def backward_kernel(d_ref, c_ref, ans_ref, smooth_ref, gd_ref, gc_ref, *, step, slices_total):
    slices, rows, block = d_ref.shape
    shape = (rows, lanes)
    subs = block // lanes
    per_tile = ans_ref.shape[0] // (pl.num_programs(0) * subs)
    scale = -step * log2e
    gain = optical_depth / slices_total

    for j in range(subs):
        cols = pl.ds(j * lanes, lanes)
        base = (pl.program_id(0) * subs + j) * per_tile
        place = pl.ds(pl.multiple_of((pl.program_id(0) * subs + j) * lanes, lanes), lanes)

        def pixel(c):
            if per_tile == 1:
                return ans_ref[base, c]
            return jnp.concatenate([ans_ref[base + g, c] for g in range(per_tile)], axis=0)

        def body(z, carry):
            n, front, w0, w1, w2 = carry
            d = d_ref[z, :, cols].astype(jnp.float32)
            dtn = softplus(d) * scale
            lit = front * (1.0 - jnp.exp2(dtn))
            n_next = n + dtn
            through = jnp.exp2(n_next)
            inv = jnp.exp2(-n_next)
            col = [jax.nn.sigmoid(c_ref[c, z, :, cols].astype(jnp.float32)) for c in range(3)]
            lit_col = [lit * col[c] for c in range(3)]
            w = [w0 + lit_col[0], w1 + lit_col[1], w2 + lit_col[2]]
            res = [pixel(c) for c in range(3)]
            emitted = res[0] * col[0] + res[1] * col[1] + res[2] * col[2]
            left = res[0] * w[0] + res[1] * w[1] + res[2] * w[2]
            inner = emitted - inv * (pixel(3) - left)
            for c in range(3):
                gc_ref[c, z, :, cols] = res[c] * lit_col[c] * (1.0 - col[c])
            gd_ref[z, :, cols] = gain * through * jax.nn.sigmoid(d) * inner + smooth_ref[z, :, place]
            return (n_next, through, w[0], w[1], w[2])

        zero = jnp.zeros(shape, jnp.float32)
        one = jnp.ones(shape, jnp.float32)
        lax.fori_loop(0, slices, body, (zero, one, zero, zero, zero), unroll=backward_unroll)


def forward_partial(density, colour_raw, step, depth_count):
    slices, rows, width = density.shape
    tiles, per_tile, chunk_rows = chunking(rows, width, depth_count)
    block = lanes * forward_subs if tiles % forward_subs == 0 else lanes
    return pl.pallas_call(
        functools.partial(forward_kernel, step=step),
        grid=(width // block,),
        in_specs=[
            pl.BlockSpec((slices, rows, block), lambda i: (0, 0, i)),
            pl.BlockSpec((3, slices, rows, block), lambda i: (0, 0, 0, i)),
        ],
        out_specs=pl.BlockSpec(
            (per_tile * (block // lanes), 4, chunk_rows, lanes), lambda i: (i, 0, 0, 0)
        ),
        out_shape=jax.ShapeDtypeStruct((tiles * per_tile, 4, chunk_rows, lanes), jnp.float32),
    )(density, colour_raw)


def smooth_term(density, zhalo, rhalo):
    slices, rows, width = density.shape
    tiles = width // lanes
    block = lanes * forward_subs if tiles % forward_subs == 0 else lanes
    slab = pl.BlockSpec((slices, rows, block), lambda i: (0, 0, i))
    return pl.pallas_call(
        smooth_kernel,
        grid=(width // block,),
        in_specs=[
            slab,
            pl.BlockSpec((2, rows, block), lambda i: (0, 0, i)),
            pl.BlockSpec((slices, 2, block), lambda i: (0, 0, i)),
        ],
        out_specs=pl.BlockSpec(memory_space=pltpu.VMEM),
        out_shape=jax.ShapeDtypeStruct((slices, rows, width), jnp.float32),
    )(density, zhalo, rhalo)


def backward_grads(density, colour_raw, answers, smooth, step, slices_total):
    slices, rows, width = density.shape
    tiles = width // lanes
    block = lanes * backward_subs if tiles % backward_subs == 0 else lanes
    slab = pl.BlockSpec((slices, rows, block), lambda i: (0, 0, i))
    colours = pl.BlockSpec((3, slices, rows, block), lambda i: (0, 0, 0, i))
    return pl.pallas_call(
        functools.partial(backward_kernel, step=step, slices_total=float(slices_total)),
        grid=(width // block,),
        in_specs=[
            slab,
            colours,
            pl.BlockSpec(memory_space=pltpu.VMEM),
            pl.BlockSpec(memory_space=pltpu.VMEM),
        ],
        out_specs=[slab, colours],
        out_shape=[
            jax.ShapeDtypeStruct((slices, rows, width), jnp.float32),
            jax.ShapeDtypeStruct((3, slices, rows, width), jnp.float32),
        ],
    )(
        density,
        colour_raw,
        pltpu.with_memory_space_constraint(answers, pltpu.VMEM),
        pltpu.with_memory_space_constraint(smooth, pltpu.VMEM),
    )


def composite(parts, slab_rank, target_piece, slices_total):
    emitted, passing = (parts[:, :3], parts[:, 3])
    earlier = (slab_rank[None, :] < slab_rank[:, None]).astype(jnp.float32)[:, :, None, None]
    later = (slab_rank[None, :] > slab_rank[:, None]).astype(jnp.float32)[:, :, None, None, None]
    front = jnp.exp(jnp.sum(earlier * jnp.log(passing)[None], axis=1))
    weighted = front[:, None] * emitted
    behind = jnp.sum(later * weighted[None], axis=1) / (front * passing)[:, None]
    residual = jnp.sum(weighted, axis=0) - target_piece
    scaled_residual = slices_total * (front[:, None] * residual[None])
    scaled_behind = slices_total * (front * jnp.sum(residual[None] * behind, axis=1))
    folded = jnp.sum(scaled_residual * emitted, axis=1) + passing * scaled_behind
    return jnp.concatenate([scaled_residual, folded[:, None]], axis=1)


def halos(density_raw):
    depth_count = lax.axis_size("depth")
    rows_count = lax.axis_size("rows")
    depth_at = lax.axis_index("depth")
    rows_at = lax.axis_index("rows")
    up_d = [(i, i + 1) for i in range(depth_count - 1)]
    up_r = [(i, i + 1) for i in range(rows_count - 1)]
    first_slice = density_raw[:1]
    last_slice = density_raw[-1:]
    first_row = density_raw[:, :1]
    last_row = density_raw[:, -1:]
    prev_slice = lax.ppermute(last_slice, "depth", up_d)
    next_slice = lax.ppermute(first_slice, "depth", [(j, i) for i, j in up_d])
    prev_row = lax.ppermute(last_row, "rows", up_r)
    next_row = lax.ppermute(first_row, "rows", [(j, i) for i, j in up_r])
    prev_slice = jnp.where(depth_at > 0, prev_slice, first_slice)
    next_slice = jnp.where(depth_at < depth_count - 1, next_slice, last_slice)
    prev_row = jnp.where(rows_at > 0, prev_row, first_row)
    next_row = jnp.where(rows_at < rows_count - 1, next_row, last_row)
    zhalo = jnp.concatenate([prev_slice, next_slice], axis=0).astype(jnp.float32)
    rhalo = jnp.concatenate([prev_row, next_row], axis=1).astype(jnp.float32)
    return zhalo, rhalo


def local(density_raw, colour_raw, target, slab_rank):
    slices_dev, rows_dev, width = density_raw.shape
    depth_count = lax.axis_size("depth")
    slices_total = slices_dev * depth_count
    step = optical_depth / slices_total
    tiles, per_tile, chunk_rows = chunking(rows_dev, width, depth_count)
    partial_value = forward_partial(density_raw, colour_raw, step, depth_count)
    partial_value, after_forward = lax.optimization_barrier((partial_value, density_raw))
    zhalo, rhalo = halos(after_forward)
    received = lax.all_to_all(partial_value, "depth", 0, 0, tiled=True)
    position = lax.axis_index("depth")
    target_piece = lax.dynamic_slice(
        target,
        (0, (position % per_tile) * chunk_rows, (position // per_tile) * lanes),
        (3, chunk_rows, lanes),
    )
    answers = composite(received, slab_rank, target_piece, float(slices_total))
    returned = lax.all_to_all(answers, "depth", 0, 0, tiled=True)
    smooth = smooth_term(density_raw, zhalo, rhalo)
    return backward_grads(density_raw, colour_raw, returned, smooth, step, slices_total)


def solution(mesh):
    placed = (P("depth", "rows", None), P(None, "depth", "rows", None), P(None, "rows", None), P())
    return jax.shard_map(
        local,
        mesh=mesh,
        in_specs=placed,
        out_specs=(P("depth", "rows", None), P(None, "depth", "rows", None)),
        check_vma=False,
    )
```

```python
import functools

import jax
import jax.numpy as jnp
from jax import lax
from jax.experimental import pallas as pl
from jax.experimental.pallas import tpu as pltpu
from jax.sharding import PartitionSpec as P

optical_depth = 2.5
smooth_weight = 0.05
lanes = 128
forward_subs = 4
backward_subs = 2
forward_unroll = 32
backward_unroll = 8


log2e = 1.4426950408889634
ln2 = 0.6931471805599453


def softplus(x):
    return jnp.maximum(x, 0.0) + ln2 * jnp.log2(1.0 + jnp.exp2(jnp.abs(x) * -log2e))


def chunking(rows, width, depth_count):
    tiles = width // lanes
    per_tile = max(depth_count // tiles, 1)
    return tiles, per_tile, rows // per_tile


def forward_kernel(d_ref, c_ref, out_ref, *, step):
    slices, rows, block = d_ref.shape
    shape = (rows, lanes)
    subs = block // lanes
    per_tile = out_ref.shape[0] // subs
    chunk_rows = out_ref.shape[2]
    scale = -step * log2e

    for j in range(subs):
        cols = pl.ds(j * lanes, lanes)

        def body(z, carry):
            n, front, e0, e1, e2 = carry
            dtn = softplus(d_ref[z, :, cols].astype(jnp.float32)) * scale
            kept = jnp.exp2(dtn)
            lit = front * (1.0 - kept)
            n = n + dtn
            e0 = e0 + lit * jax.nn.sigmoid(c_ref[0, z, :, cols].astype(jnp.float32))
            e1 = e1 + lit * jax.nn.sigmoid(c_ref[1, z, :, cols].astype(jnp.float32))
            e2 = e2 + lit * jax.nn.sigmoid(c_ref[2, z, :, cols].astype(jnp.float32))
            return (n, front * kept, e0, e1, e2)

        zero = jnp.zeros(shape, jnp.float32)
        one = jnp.ones(shape, jnp.float32)
        n, _, e0, e1, e2 = lax.fori_loop(0, slices, body, (zero, one, zero, zero, zero), unroll=forward_unroll)
        values = (e0, e1, e2, jnp.exp2(n))
        for g in range(per_tile):
            for c in range(4):
                out_ref[j * per_tile + g, c] = values[c][g * chunk_rows:(g + 1) * chunk_rows]


def smooth_kernel(d_ref, zhalo_ref, rhalo_ref, out_ref):
    slices, rows, block = d_ref.shape
    shape = (rows, lanes)
    row = lax.broadcasted_iota(jnp.int32, shape, 0)
    first_row = row == 0
    last_row = row == shape[0] - 1

    for j in range(block // lanes):
        cols = pl.ds(j * lanes, lanes)

        def body(z, carry):
            d_prev, d = carry
            d_next = jnp.where(
                z + 1 < slices,
                d_ref[jnp.minimum(z + 1, slices - 1), :, cols].astype(jnp.float32),
                zhalo_ref[1, :, cols],
            )
            rims = rhalo_ref[z, :, cols]
            upper = jnp.where(first_row, rims[0:1], pltpu.roll(d, 1, 0))
            lower = jnp.where(last_row, rims[1:2], pltpu.roll(d, shape[0] - 1, 0))
            out_ref[z, :, cols] = 2.0 * smooth_weight * (
                (d - d_prev) + (d - d_next) + (d - upper) + (d - lower)
            )
            return (d, d_next)

        start = (zhalo_ref[0, :, cols], d_ref[0, :, cols].astype(jnp.float32))
        lax.fori_loop(0, slices, body, start, unroll=2)


def backward_kernel(d_ref, c_ref, ans_ref, smooth_ref, gd_ref, gc_ref, *, step, slices_total):
    slices, rows, block = gd_ref.shape
    shape = (rows, lanes)
    subs = block // lanes
    per_tile = ans_ref.shape[0] // (pl.num_programs(0) * subs)
    scale = -step * log2e
    gain = optical_depth / slices_total

    for j in range(subs):
        cols = pl.ds(j * lanes, lanes)
        base = (pl.program_id(0) * subs + j) * per_tile
        place = pl.ds(pl.multiple_of((pl.program_id(0) * subs + j) * lanes, lanes), lanes)

        def pixel(c):
            if per_tile == 1:
                return ans_ref[base, c]
            return jnp.concatenate([ans_ref[base + g, c] for g in range(per_tile)], axis=0)

        def body(z, carry):
            n, front, w0, w1, w2 = carry
            d = d_ref[z, :, place].astype(jnp.float32)
            dtn = softplus(d) * scale
            lit = front * (1.0 - jnp.exp2(dtn))
            n_next = n + dtn
            through = jnp.exp2(n_next)
            inv = jnp.exp2(-n_next)
            col = [jax.nn.sigmoid(c_ref[c, z, :, cols].astype(jnp.float32)) for c in range(3)]
            lit_col = [lit * col[c] for c in range(3)]
            w = [w0 + lit_col[0], w1 + lit_col[1], w2 + lit_col[2]]
            res = [pixel(c) for c in range(3)]
            emitted = res[0] * col[0] + res[1] * col[1] + res[2] * col[2]
            left = res[0] * w[0] + res[1] * w[1] + res[2] * w[2]
            inner = emitted - inv * (pixel(3) - left)
            for c in range(3):
                gc_ref[c, z, :, cols] = res[c] * lit_col[c] * (1.0 - col[c])
            gd_ref[z, :, cols] = gain * through * jax.nn.sigmoid(d) * inner + smooth_ref[z, :, cols]
            return (n_next, through, w[0], w[1], w[2])

        zero = jnp.zeros(shape, jnp.float32)
        one = jnp.ones(shape, jnp.float32)
        lax.fori_loop(0, slices, body, (zero, one, zero, zero, zero), unroll=backward_unroll)


def forward_partial(density, colour_raw, step, depth_count):
    slices, rows, width = density.shape
    tiles, per_tile, chunk_rows = chunking(rows, width, depth_count)
    block = lanes * forward_subs if tiles % forward_subs == 0 else lanes
    return pl.pallas_call(
        functools.partial(forward_kernel, step=step),
        grid=(width // block,),
        in_specs=[
            pl.BlockSpec((slices, rows, block), lambda i: (0, 0, i)),
            pl.BlockSpec((3, slices, rows, block), lambda i: (0, 0, 0, i)),
        ],
        out_specs=pl.BlockSpec(
            (per_tile * (block // lanes), 4, chunk_rows, lanes), lambda i: (i, 0, 0, 0)
        ),
        out_shape=jax.ShapeDtypeStruct((tiles * per_tile, 4, chunk_rows, lanes), jnp.float32),
    )(density, colour_raw)


def smooth_term(density, zhalo, rhalo):
    slices, rows, width = density.shape
    tiles = width // lanes
    block = lanes * forward_subs if tiles % forward_subs == 0 else lanes
    slab = pl.BlockSpec((slices, rows, block), lambda i: (0, 0, i))
    return pl.pallas_call(
        smooth_kernel,
        grid=(width // block,),
        in_specs=[
            slab,
            pl.BlockSpec((2, rows, block), lambda i: (0, 0, i)),
            pl.BlockSpec((slices, 2, block), lambda i: (0, 0, i)),
        ],
        out_specs=slab,
        out_shape=jax.ShapeDtypeStruct((slices, rows, width), jnp.float32),
    )(density, zhalo, rhalo)


def backward_grads(density, colour_raw, answers, smooth, step, slices_total):
    slices, rows, width = density.shape
    tiles = width // lanes
    block = lanes * backward_subs if tiles % backward_subs == 0 else lanes
    slab = pl.BlockSpec((slices, rows, block), lambda i: (0, 0, i))
    colours = pl.BlockSpec((3, slices, rows, block), lambda i: (0, 0, 0, i))
    return pl.pallas_call(
        functools.partial(backward_kernel, step=step, slices_total=float(slices_total)),
        grid=(width // block,),
        in_specs=[
            pl.BlockSpec(memory_space=pltpu.VMEM),
            colours,
            pl.BlockSpec(memory_space=pltpu.VMEM),
            slab,
        ],
        out_specs=[slab, colours],
        out_shape=[
            jax.ShapeDtypeStruct((slices, rows, width), jnp.float32),
            jax.ShapeDtypeStruct((3, slices, rows, width), jnp.float32),
        ],
        input_output_aliases={3: 0},
    )(
        pltpu.with_memory_space_constraint(density, pltpu.VMEM),
        colour_raw,
        pltpu.with_memory_space_constraint(answers, pltpu.VMEM),
        smooth,
    )


def composite(parts, slab_rank, target_piece, slices_total):
    emitted, passing = (parts[:, :3], parts[:, 3])
    earlier = (slab_rank[None, :] < slab_rank[:, None]).astype(jnp.float32)[:, :, None, None]
    later = (slab_rank[None, :] > slab_rank[:, None]).astype(jnp.float32)[:, :, None, None, None]
    front = jnp.exp(jnp.sum(earlier * jnp.log(passing)[None], axis=1))
    weighted = front[:, None] * emitted
    behind = jnp.sum(later * weighted[None], axis=1) / (front * passing)[:, None]
    residual = jnp.sum(weighted, axis=0) - target_piece
    scaled_residual = slices_total * (front[:, None] * residual[None])
    scaled_behind = slices_total * (front * jnp.sum(residual[None] * behind, axis=1))
    folded = jnp.sum(scaled_residual * emitted, axis=1) + passing * scaled_behind
    return jnp.concatenate([scaled_residual, folded[:, None]], axis=1)


def halos(density_raw):
    depth_count = lax.axis_size("depth")
    rows_count = lax.axis_size("rows")
    depth_at = lax.axis_index("depth")
    rows_at = lax.axis_index("rows")
    up_d = [(i, i + 1) for i in range(depth_count - 1)]
    up_r = [(i, i + 1) for i in range(rows_count - 1)]
    first_slice = density_raw[:1]
    last_slice = density_raw[-1:]
    first_row = density_raw[:, :1]
    last_row = density_raw[:, -1:]
    prev_slice = lax.ppermute(last_slice, "depth", up_d)
    next_slice = lax.ppermute(first_slice, "depth", [(j, i) for i, j in up_d])
    prev_row = lax.ppermute(last_row, "rows", up_r)
    next_row = lax.ppermute(first_row, "rows", [(j, i) for i, j in up_r])
    prev_slice = jnp.where(depth_at > 0, prev_slice, first_slice)
    next_slice = jnp.where(depth_at < depth_count - 1, next_slice, last_slice)
    prev_row = jnp.where(rows_at > 0, prev_row, first_row)
    next_row = jnp.where(rows_at < rows_count - 1, next_row, last_row)
    zhalo = jnp.concatenate([prev_slice, next_slice], axis=0).astype(jnp.float32)
    rhalo = jnp.concatenate([prev_row, next_row], axis=1).astype(jnp.float32)
    return zhalo, rhalo


def local(density_raw, colour_raw, target, slab_rank):
    slices_dev, rows_dev, width = density_raw.shape
    depth_count = lax.axis_size("depth")
    slices_total = slices_dev * depth_count
    step = optical_depth / slices_total
    tiles, per_tile, chunk_rows = chunking(rows_dev, width, depth_count)
    partial_value = forward_partial(density_raw, colour_raw, step, depth_count)
    partial_value, after_forward = lax.optimization_barrier((partial_value, density_raw))
    zhalo, rhalo = halos(after_forward)
    received = lax.all_to_all(partial_value, "depth", 0, 0, tiled=True)
    position = lax.axis_index("depth")
    target_piece = lax.dynamic_slice(
        target,
        (0, (position % per_tile) * chunk_rows, (position // per_tile) * lanes),
        (3, chunk_rows, lanes),
    )
    answers = composite(received, slab_rank, target_piece, float(slices_total))
    returned = lax.all_to_all(answers, "depth", 0, 0, tiled=True)
    smooth = smooth_term(density_raw, zhalo, rhalo)
    return backward_grads(density_raw, colour_raw, returned, smooth, step, slices_total)


def solution(mesh):
    placed = (P("depth", "rows", None), P(None, "depth", "rows", None), P(None, "rows", None), P())
    return jax.shard_map(
        local,
        mesh=mesh,
        in_specs=placed,
        out_specs=(P("depth", "rows", None), P(None, "depth", "rows", None)),
        check_vma=False,
    )
```

```python
import functools

import jax
import jax.numpy as jnp
from jax import lax
from jax.experimental import pallas as pl
from jax.experimental.pallas import tpu as pltpu
from jax.sharding import PartitionSpec as P

optical_depth = 2.5
smooth_weight = 0.05
lanes = 128
forward_subs = 4
backward_subs = 2
forward_unroll = 32
backward_unroll = 8


log2e = 1.4426950408889634
ln2 = 0.6931471805599453


def softplus(x):
    return jnp.maximum(x, 0.0) + ln2 * jnp.log2(1.0 + jnp.exp2(jnp.abs(x) * -log2e))


def chunking(rows, width, depth_count):
    tiles = width // lanes
    per_tile = max(depth_count // tiles, 1)
    return tiles, per_tile, rows // per_tile


def forward_kernel(d_ref, c_ref, out_ref, *, step):
    slices, rows, block = d_ref.shape
    shape = (rows, lanes)
    subs = block // lanes
    per_tile = out_ref.shape[0] // subs
    chunk_rows = out_ref.shape[2]
    scale = -step * log2e

    for j in range(subs):
        cols = pl.ds(j * lanes, lanes)

        def body(z, carry):
            n, front, e0, e1, e2 = carry
            dtn = softplus(d_ref[z, :, cols].astype(jnp.float32)) * scale
            kept = jnp.exp2(dtn)
            lit = front * (1.0 - kept)
            n = n + dtn
            e0 = e0 + lit * jax.nn.sigmoid(c_ref[0, z, :, cols].astype(jnp.float32))
            e1 = e1 + lit * jax.nn.sigmoid(c_ref[1, z, :, cols].astype(jnp.float32))
            e2 = e2 + lit * jax.nn.sigmoid(c_ref[2, z, :, cols].astype(jnp.float32))
            return (n, front * kept, e0, e1, e2)

        zero = jnp.zeros(shape, jnp.float32)
        one = jnp.ones(shape, jnp.float32)
        n, _, e0, e1, e2 = lax.fori_loop(0, slices, body, (zero, one, zero, zero, zero), unroll=forward_unroll)
        values = (e0, e1, e2, jnp.exp2(n))
        for g in range(per_tile):
            for c in range(4):
                out_ref[j * per_tile + g, c] = values[c][g * chunk_rows:(g + 1) * chunk_rows]


def smooth_kernel(d_ref, zhalo_ref, rhalo_ref, out_ref):
    slices, rows, block = d_ref.shape
    shape = (rows, lanes)
    row = lax.broadcasted_iota(jnp.int32, shape, 0)
    first_row = row == 0
    last_row = row == shape[0] - 1

    for j in range(block // lanes):
        cols = pl.ds(j * lanes, lanes)

        def body(z, carry):
            d_prev, d = carry
            d_next = jnp.where(
                z + 1 < slices,
                d_ref[jnp.minimum(z + 1, slices - 1), :, cols].astype(jnp.float32),
                zhalo_ref[1, :, cols],
            )
            rims = rhalo_ref[z, :, cols]
            upper = jnp.where(first_row, rims[0:1], pltpu.roll(d, 1, 0))
            lower = jnp.where(last_row, rims[1:2], pltpu.roll(d, shape[0] - 1, 0))
            out_ref[z, :, cols] = 2.0 * smooth_weight * (
                (d - d_prev) + (d - d_next) + (d - upper) + (d - lower)
            )
            return (d, d_next)

        start = (zhalo_ref[0, :, cols], d_ref[0, :, cols].astype(jnp.float32))
        lax.fori_loop(0, slices, body, start, unroll=2)


def backward_kernel(
    d_ref, c0_ref, c1_ref, c2_ref, ans_ref, smooth_ref, gd_ref, gc_ref, *, step, slices_total
):
    slices, rows, block = gd_ref.shape
    shape = (rows, lanes)
    subs = block // lanes
    per_tile = ans_ref.shape[0] // (pl.num_programs(0) * subs)
    scale = -step * log2e
    gain = optical_depth / slices_total

    for j in range(subs):
        cols = pl.ds(j * lanes, lanes)
        base = (pl.program_id(0) * subs + j) * per_tile
        place = pl.ds(pl.multiple_of((pl.program_id(0) * subs + j) * lanes, lanes), lanes)

        def pixel(c):
            if per_tile == 1:
                return ans_ref[base, c]
            return jnp.concatenate([ans_ref[base + g, c] for g in range(per_tile)], axis=0)

        def body(z, carry):
            n, front, w0, w1, w2 = carry
            d = d_ref[z, :, place].astype(jnp.float32)
            dtn = softplus(d) * scale
            lit = front * (1.0 - jnp.exp2(dtn))
            n_next = n + dtn
            through = jnp.exp2(n_next)
            inv = jnp.exp2(-n_next)
            raw = (c0_ref[z, :, place], c1_ref[z, :, cols], c2_ref[z, :, cols])
            col = [jax.nn.sigmoid(raw[c].astype(jnp.float32)) for c in range(3)]
            lit_col = [lit * col[c] for c in range(3)]
            w = [w0 + lit_col[0], w1 + lit_col[1], w2 + lit_col[2]]
            res = [pixel(c) for c in range(3)]
            emitted = res[0] * col[0] + res[1] * col[1] + res[2] * col[2]
            left = res[0] * w[0] + res[1] * w[1] + res[2] * w[2]
            inner = emitted - inv * (pixel(3) - left)
            for c in range(3):
                gc_ref[c, z, :, cols] = res[c] * lit_col[c] * (1.0 - col[c])
            gd_ref[z, :, cols] = gain * through * jax.nn.sigmoid(d) * inner + smooth_ref[z, :, cols]
            return (n_next, through, w[0], w[1], w[2])

        zero = jnp.zeros(shape, jnp.float32)
        one = jnp.ones(shape, jnp.float32)
        lax.fori_loop(0, slices, body, (zero, one, zero, zero, zero), unroll=backward_unroll)


def forward_partial(density, colour_raw, step, depth_count):
    slices, rows, width = density.shape
    tiles, per_tile, chunk_rows = chunking(rows, width, depth_count)
    block = lanes * forward_subs if tiles % forward_subs == 0 else lanes
    return pl.pallas_call(
        functools.partial(forward_kernel, step=step),
        grid=(width // block,),
        in_specs=[
            pl.BlockSpec((slices, rows, block), lambda i: (0, 0, i)),
            pl.BlockSpec((3, slices, rows, block), lambda i: (0, 0, 0, i)),
        ],
        out_specs=pl.BlockSpec(
            (per_tile * (block // lanes), 4, chunk_rows, lanes), lambda i: (i, 0, 0, 0)
        ),
        out_shape=jax.ShapeDtypeStruct((tiles * per_tile, 4, chunk_rows, lanes), jnp.float32),
    )(density, colour_raw)


def smooth_term(density, zhalo, rhalo):
    slices, rows, width = density.shape
    tiles = width // lanes
    block = lanes * forward_subs if tiles % forward_subs == 0 else lanes
    slab = pl.BlockSpec((slices, rows, block), lambda i: (0, 0, i))
    return pl.pallas_call(
        smooth_kernel,
        grid=(width // block,),
        in_specs=[
            slab,
            pl.BlockSpec((2, rows, block), lambda i: (0, 0, i)),
            pl.BlockSpec((slices, 2, block), lambda i: (0, 0, i)),
        ],
        out_specs=slab,
        out_shape=jax.ShapeDtypeStruct((slices, rows, width), jnp.float32),
    )(density, zhalo, rhalo)


def backward_grads(density, colour_raw, answers, smooth, step, slices_total):
    slices, rows, width = density.shape
    tiles = width // lanes
    block = lanes * backward_subs if tiles % backward_subs == 0 else lanes
    slab = pl.BlockSpec((slices, rows, block), lambda i: (0, 0, i))
    colours = pl.BlockSpec((3, slices, rows, block), lambda i: (0, 0, 0, i))
    return pl.pallas_call(
        functools.partial(backward_kernel, step=step, slices_total=float(slices_total)),
        grid=(width // block,),
        in_specs=[
            pl.BlockSpec(memory_space=pltpu.VMEM),
            pl.BlockSpec(memory_space=pltpu.VMEM),
            pl.BlockSpec((None, slices, rows, block), lambda i: (1, 0, 0, i)),
            pl.BlockSpec((None, slices, rows, block), lambda i: (2, 0, 0, i)),
            pl.BlockSpec(memory_space=pltpu.VMEM),
            slab,
        ],
        out_specs=[slab, colours],
        out_shape=[
            jax.ShapeDtypeStruct((slices, rows, width), jnp.float32),
            jax.ShapeDtypeStruct((3, slices, rows, width), jnp.float32),
        ],
        input_output_aliases={5: 0},
    )(
        pltpu.with_memory_space_constraint(density, pltpu.VMEM),
        pltpu.with_memory_space_constraint(colour_raw[0], pltpu.VMEM),
        colour_raw,
        colour_raw,
        pltpu.with_memory_space_constraint(answers, pltpu.VMEM),
        smooth,
    )


def composite(parts, slab_rank, target_piece, slices_total):
    emitted, passing = (parts[:, :3], parts[:, 3])
    earlier = (slab_rank[None, :] < slab_rank[:, None]).astype(jnp.float32)[:, :, None, None]
    later = (slab_rank[None, :] > slab_rank[:, None]).astype(jnp.float32)[:, :, None, None, None]
    front = jnp.exp(jnp.sum(earlier * jnp.log(passing)[None], axis=1))
    weighted = front[:, None] * emitted
    behind = jnp.sum(later * weighted[None], axis=1) / (front * passing)[:, None]
    residual = jnp.sum(weighted, axis=0) - target_piece
    scaled_residual = slices_total * (front[:, None] * residual[None])
    scaled_behind = slices_total * (front * jnp.sum(residual[None] * behind, axis=1))
    folded = jnp.sum(scaled_residual * emitted, axis=1) + passing * scaled_behind
    return jnp.concatenate([scaled_residual, folded[:, None]], axis=1)


def halos(density_raw):
    depth_count = lax.axis_size("depth")
    rows_count = lax.axis_size("rows")
    depth_at = lax.axis_index("depth")
    rows_at = lax.axis_index("rows")
    up_d = [(i, i + 1) for i in range(depth_count - 1)]
    up_r = [(i, i + 1) for i in range(rows_count - 1)]
    first_slice = density_raw[:1]
    last_slice = density_raw[-1:]
    first_row = density_raw[:, :1]
    last_row = density_raw[:, -1:]
    prev_slice = lax.ppermute(last_slice, "depth", up_d)
    next_slice = lax.ppermute(first_slice, "depth", [(j, i) for i, j in up_d])
    prev_row = lax.ppermute(last_row, "rows", up_r)
    next_row = lax.ppermute(first_row, "rows", [(j, i) for i, j in up_r])
    prev_slice = jnp.where(depth_at > 0, prev_slice, first_slice)
    next_slice = jnp.where(depth_at < depth_count - 1, next_slice, last_slice)
    prev_row = jnp.where(rows_at > 0, prev_row, first_row)
    next_row = jnp.where(rows_at < rows_count - 1, next_row, last_row)
    zhalo = jnp.concatenate([prev_slice, next_slice], axis=0).astype(jnp.float32)
    rhalo = jnp.concatenate([prev_row, next_row], axis=1).astype(jnp.float32)
    return zhalo, rhalo


def local(density_raw, colour_raw, target, slab_rank):
    slices_dev, rows_dev, width = density_raw.shape
    depth_count = lax.axis_size("depth")
    slices_total = slices_dev * depth_count
    step = optical_depth / slices_total
    tiles, per_tile, chunk_rows = chunking(rows_dev, width, depth_count)
    partial_value = forward_partial(density_raw, colour_raw, step, depth_count)
    partial_value, after_forward = lax.optimization_barrier((partial_value, density_raw))
    zhalo, rhalo = halos(after_forward)
    received = lax.all_to_all(partial_value, "depth", 0, 0, tiled=True)
    position = lax.axis_index("depth")
    target_piece = lax.dynamic_slice(
        target,
        (0, (position % per_tile) * chunk_rows, (position // per_tile) * lanes),
        (3, chunk_rows, lanes),
    )
    answers = composite(received, slab_rank, target_piece, float(slices_total))
    returned = lax.all_to_all(answers, "depth", 0, 0, tiled=True)
    smooth = smooth_term(density_raw, zhalo, rhalo)
    return backward_grads(density_raw, colour_raw, returned, smooth, step, slices_total)


def solution(mesh):
    placed = (P("depth", "rows", None), P(None, "depth", "rows", None), P(None, "rows", None), P())
    return jax.shard_map(
        local,
        mesh=mesh,
        in_specs=placed,
        out_specs=(P("depth", "rows", None), P(None, "depth", "rows", None)),
        check_vma=False,
    )
```

```python
import functools

import jax
import jax.numpy as jnp
from jax import lax
from jax.experimental import pallas as pl
from jax.experimental.pallas import tpu as pltpu
from jax.sharding import PartitionSpec as P

optical_depth = 2.5
smooth_weight = 0.05
lanes = 128
forward_subs = 4
backward_subs = 2
forward_unroll = 32
backward_unroll = 8


log2e = 1.4426950408889634
ln2 = 0.6931471805599453


def softplus(x):
    return jnp.maximum(x, 0.0) + ln2 * jnp.log2(1.0 + jnp.exp2(jnp.abs(x) * -log2e))


def chunking(rows, width, depth_count):
    tiles = width // lanes
    per_tile = max(depth_count // tiles, 1)
    return tiles, per_tile, rows // per_tile


def forward_kernel(d_ref, c_ref, out_ref, *, step):
    slices, rows, block = d_ref.shape
    shape = (rows, lanes)
    subs = block // lanes
    per_tile = out_ref.shape[0] // subs
    chunk_rows = out_ref.shape[2]
    scale = -step * log2e

    for j in range(subs):
        cols = pl.ds(j * lanes, lanes)

        def body(z, carry):
            n, front, e0, e1, e2 = carry
            dtn = softplus(d_ref[z, :, cols].astype(jnp.float32)) * scale
            kept = jnp.exp2(dtn)
            lit = front * (1.0 - kept)
            n = n + dtn
            e0 = e0 + lit * jax.nn.sigmoid(c_ref[0, z, :, cols].astype(jnp.float32))
            e1 = e1 + lit * jax.nn.sigmoid(c_ref[1, z, :, cols].astype(jnp.float32))
            e2 = e2 + lit * jax.nn.sigmoid(c_ref[2, z, :, cols].astype(jnp.float32))
            return (n, front * kept, e0, e1, e2)

        zero = jnp.zeros(shape, jnp.float32)
        one = jnp.ones(shape, jnp.float32)
        n, _, e0, e1, e2 = lax.fori_loop(0, slices, body, (zero, one, zero, zero, zero), unroll=forward_unroll)
        values = (e0, e1, e2, jnp.exp2(n))
        for g in range(per_tile):
            for c in range(4):
                out_ref[j * per_tile + g, c] = values[c][g * chunk_rows:(g + 1) * chunk_rows]


def smooth_kernel(d_ref, zhalo_ref, rhalo_ref, out_ref):
    slices, rows, block = d_ref.shape
    shape = (rows, lanes)
    row = lax.broadcasted_iota(jnp.int32, shape, 0)
    first_row = row == 0
    last_row = row == shape[0] - 1

    for j in range(block // lanes):
        cols = pl.ds(j * lanes, lanes)

        def body(z, carry):
            d_prev, d = carry
            d_next = jnp.where(
                z + 1 < slices,
                d_ref[jnp.minimum(z + 1, slices - 1), :, cols].astype(jnp.float32),
                zhalo_ref[1, :, cols],
            )
            rims = rhalo_ref[z, :, cols]
            upper = jnp.where(first_row, rims[0:1], pltpu.roll(d, 1, 0))
            lower = jnp.where(last_row, rims[1:2], pltpu.roll(d, shape[0] - 1, 0))
            out_ref[z, :, cols] = 2.0 * smooth_weight * (
                (d - d_prev) + (d - d_next) + (d - upper) + (d - lower)
            )
            return (d, d_next)

        start = (zhalo_ref[0, :, cols], d_ref[0, :, cols].astype(jnp.float32))
        lax.fori_loop(0, slices, body, start, unroll=2)


def backward_kernel(
    d_ref, c_ref, ans_ref, zhalo_ref, rhalo_ref, gd_ref, gc_ref, *, step, slices_total
):
    slices, rows, block = gd_ref.shape
    shape = (rows, lanes)
    subs = block // lanes
    per_tile = ans_ref.shape[0] // (pl.num_programs(0) * subs)
    scale = -step * log2e
    gain = optical_depth / slices_total
    row = lax.broadcasted_iota(jnp.int32, shape, 0)
    first_row = row == 0
    last_row = row == shape[0] - 1

    for j in range(subs):
        cols = pl.ds(j * lanes, lanes)
        base = (pl.program_id(0) * subs + j) * per_tile
        place = pl.ds(pl.multiple_of((pl.program_id(0) * subs + j) * lanes, lanes), lanes)

        def pixel(c):
            if per_tile == 1:
                return ans_ref[base, c]
            return jnp.concatenate([ans_ref[base + g, c] for g in range(per_tile)], axis=0)

        def body(z, carry):
            n, front, w0, w1, w2, d_prev, d = carry
            d_next = jnp.where(
                z + 1 < slices,
                d_ref[jnp.minimum(z + 1, slices - 1), :, place].astype(jnp.float32),
                zhalo_ref[1, :, cols],
            )
            rims = rhalo_ref[z, :, cols]
            upper = jnp.where(first_row, rims[0:1], pltpu.roll(d, 1, 0))
            lower = jnp.where(last_row, rims[1:2], pltpu.roll(d, shape[0] - 1, 0))
            smooth = 2.0 * smooth_weight * ((d - d_prev) + (d - d_next) + (d - upper) + (d - lower))
            dtn = softplus(d) * scale
            lit = front * (1.0 - jnp.exp2(dtn))
            n_next = n + dtn
            through = jnp.exp2(n_next)
            inv = jnp.exp2(-n_next)
            col = [jax.nn.sigmoid(c_ref[c, z, :, cols].astype(jnp.float32)) for c in range(3)]
            lit_col = [lit * col[c] for c in range(3)]
            w = [w0 + lit_col[0], w1 + lit_col[1], w2 + lit_col[2]]
            res = [pixel(c) for c in range(3)]
            emitted = res[0] * col[0] + res[1] * col[1] + res[2] * col[2]
            left = res[0] * w[0] + res[1] * w[1] + res[2] * w[2]
            inner = emitted - inv * (pixel(3) - left)
            for c in range(3):
                gc_ref[c, z, :, cols] = res[c] * lit_col[c] * (1.0 - col[c])
            gd_ref[z, :, cols] = gain * through * jax.nn.sigmoid(d) * inner + smooth
            return (n_next, through, w[0], w[1], w[2], d, d_next)

        zero = jnp.zeros(shape, jnp.float32)
        one = jnp.ones(shape, jnp.float32)
        start = (
            zero, one, zero, zero, zero,
            zhalo_ref[0, :, cols],
            d_ref[0, :, place].astype(jnp.float32),
        )
        lax.fori_loop(0, slices, body, start, unroll=backward_unroll)


def forward_partial(density, colour_raw, step, depth_count):
    slices, rows, width = density.shape
    tiles, per_tile, chunk_rows = chunking(rows, width, depth_count)
    block = lanes * forward_subs if tiles % forward_subs == 0 else lanes
    return pl.pallas_call(
        functools.partial(forward_kernel, step=step),
        grid=(width // block,),
        in_specs=[
            pl.BlockSpec((slices, rows, block), lambda i: (0, 0, i)),
            pl.BlockSpec((3, slices, rows, block), lambda i: (0, 0, 0, i)),
        ],
        out_specs=pl.BlockSpec(
            (per_tile * (block // lanes), 4, chunk_rows, lanes), lambda i: (i, 0, 0, 0)
        ),
        out_shape=jax.ShapeDtypeStruct((tiles * per_tile, 4, chunk_rows, lanes), jnp.float32),
    )(density, colour_raw)


def smooth_term(density, zhalo, rhalo):
    slices, rows, width = density.shape
    tiles = width // lanes
    block = lanes * forward_subs if tiles % forward_subs == 0 else lanes
    slab = pl.BlockSpec((slices, rows, block), lambda i: (0, 0, i))
    return pl.pallas_call(
        smooth_kernel,
        grid=(width // block,),
        in_specs=[
            slab,
            pl.BlockSpec((2, rows, block), lambda i: (0, 0, i)),
            pl.BlockSpec((slices, 2, block), lambda i: (0, 0, i)),
        ],
        out_specs=slab,
        out_shape=jax.ShapeDtypeStruct((slices, rows, width), jnp.float32),
    )(density, zhalo, rhalo)


def backward_grads(density, colour_raw, answers, zhalo, rhalo, step, slices_total):
    slices, rows, width = density.shape
    tiles = width // lanes
    block = lanes * backward_subs if tiles % backward_subs == 0 else lanes
    slab = pl.BlockSpec((slices, rows, block), lambda i: (0, 0, i))
    colours = pl.BlockSpec((3, slices, rows, block), lambda i: (0, 0, 0, i))
    vmem = pl.BlockSpec(memory_space=pltpu.VMEM)
    return pl.pallas_call(
        functools.partial(backward_kernel, step=step, slices_total=float(slices_total)),
        grid=(width // block,),
        in_specs=[
            vmem,
            colours,
            vmem,
            pl.BlockSpec((2, rows, block), lambda i: (0, 0, i)),
            pl.BlockSpec((slices, 2, block), lambda i: (0, 0, i)),
        ],
        out_specs=[slab, colours],
        out_shape=[
            jax.ShapeDtypeStruct((slices, rows, width), jnp.float32),
            jax.ShapeDtypeStruct((3, slices, rows, width), jnp.float32),
        ],
    )(
        pltpu.with_memory_space_constraint(density, pltpu.VMEM),
        colour_raw,
        pltpu.with_memory_space_constraint(answers, pltpu.VMEM),
        zhalo,
        rhalo,
    )


def composite(parts, slab_rank, target_piece, slices_total):
    emitted, passing = (parts[:, :3], parts[:, 3])
    earlier = (slab_rank[None, :] < slab_rank[:, None]).astype(jnp.float32)[:, :, None, None]
    later = (slab_rank[None, :] > slab_rank[:, None]).astype(jnp.float32)[:, :, None, None, None]
    front = jnp.exp(jnp.sum(earlier * jnp.log(passing)[None], axis=1))
    weighted = front[:, None] * emitted
    behind = jnp.sum(later * weighted[None], axis=1) / (front * passing)[:, None]
    residual = jnp.sum(weighted, axis=0) - target_piece
    scaled_residual = slices_total * (front[:, None] * residual[None])
    scaled_behind = slices_total * (front * jnp.sum(residual[None] * behind, axis=1))
    folded = jnp.sum(scaled_residual * emitted, axis=1) + passing * scaled_behind
    return jnp.concatenate([scaled_residual, folded[:, None]], axis=1)


def halos(density_raw):
    depth_count = lax.axis_size("depth")
    rows_count = lax.axis_size("rows")
    depth_at = lax.axis_index("depth")
    rows_at = lax.axis_index("rows")
    up_d = [(i, i + 1) for i in range(depth_count - 1)]
    up_r = [(i, i + 1) for i in range(rows_count - 1)]
    first_slice = density_raw[:1]
    last_slice = density_raw[-1:]
    first_row = density_raw[:, :1]
    last_row = density_raw[:, -1:]
    prev_slice = lax.ppermute(last_slice, "depth", up_d)
    next_slice = lax.ppermute(first_slice, "depth", [(j, i) for i, j in up_d])
    prev_row = lax.ppermute(last_row, "rows", up_r)
    next_row = lax.ppermute(first_row, "rows", [(j, i) for i, j in up_r])
    prev_slice = jnp.where(depth_at > 0, prev_slice, first_slice)
    next_slice = jnp.where(depth_at < depth_count - 1, next_slice, last_slice)
    prev_row = jnp.where(rows_at > 0, prev_row, first_row)
    next_row = jnp.where(rows_at < rows_count - 1, next_row, last_row)
    zhalo = jnp.concatenate([prev_slice, next_slice], axis=0).astype(jnp.float32)
    rhalo = jnp.concatenate([prev_row, next_row], axis=1).astype(jnp.float32)
    return zhalo, rhalo


def local(density_raw, colour_raw, target, slab_rank):
    slices_dev, rows_dev, width = density_raw.shape
    depth_count = lax.axis_size("depth")
    slices_total = slices_dev * depth_count
    step = optical_depth / slices_total
    tiles, per_tile, chunk_rows = chunking(rows_dev, width, depth_count)
    partial_value = forward_partial(density_raw, colour_raw, step, depth_count)
    partial_value, after_forward = lax.optimization_barrier((partial_value, density_raw))
    zhalo, rhalo = halos(after_forward)
    received = lax.all_to_all(partial_value, "depth", 0, 0, tiled=True)
    position = lax.axis_index("depth")
    target_piece = lax.dynamic_slice(
        target,
        (0, (position % per_tile) * chunk_rows, (position // per_tile) * lanes),
        (3, chunk_rows, lanes),
    )
    answers = composite(received, slab_rank, target_piece, float(slices_total))
    returned = lax.all_to_all(answers, "depth", 0, 0, tiled=True)
    return backward_grads(density_raw, colour_raw, returned, zhalo, rhalo, step, slices_total)


def solution(mesh):
    placed = (P("depth", "rows", None), P(None, "depth", "rows", None), P(None, "rows", None), P())
    return jax.shard_map(
        local,
        mesh=mesh,
        in_specs=placed,
        out_specs=(P("depth", "rows", None), P(None, "depth", "rows", None)),
        check_vma=False,
    )
```

```python
import functools

import jax
import jax.numpy as jnp
from jax import lax
from jax.experimental import pallas as pl
from jax.experimental.pallas import tpu as pltpu
from jax.sharding import PartitionSpec as P

optical_depth = 2.5
smooth_weight = 0.05
lanes = 128
forward_subs = 4
backward_subs = 2
forward_unroll = 32
backward_unroll = 16


log2e = 1.4426950408889634
ln2 = 0.6931471805599453


def softplus(x):
    return jnp.maximum(x, 0.0) + ln2 * jnp.log2(1.0 + jnp.exp2(jnp.abs(x) * -log2e))


def chunking(rows, width, depth_count):
    tiles = width // lanes
    per_tile = max(depth_count // tiles, 1)
    return tiles, per_tile, rows // per_tile


def forward_kernel(d_ref, c_ref, out_ref, *, step):
    slices, rows, block = d_ref.shape
    shape = (rows, lanes)
    subs = block // lanes
    per_tile = out_ref.shape[0] // subs
    chunk_rows = out_ref.shape[2]
    scale = -step * log2e

    for j in range(subs):
        cols = pl.ds(j * lanes, lanes)

        def body(z, carry):
            n, front, e0, e1, e2 = carry
            dtn = softplus(d_ref[z, :, cols].astype(jnp.float32)) * scale
            kept = jnp.exp2(dtn)
            lit = front * (1.0 - kept)
            n = n + dtn
            e0 = e0 + lit * jax.nn.sigmoid(c_ref[0, z, :, cols].astype(jnp.float32))
            e1 = e1 + lit * jax.nn.sigmoid(c_ref[1, z, :, cols].astype(jnp.float32))
            e2 = e2 + lit * jax.nn.sigmoid(c_ref[2, z, :, cols].astype(jnp.float32))
            return (n, front * kept, e0, e1, e2)

        zero = jnp.zeros(shape, jnp.float32)
        one = jnp.ones(shape, jnp.float32)
        n, _, e0, e1, e2 = lax.fori_loop(0, slices, body, (zero, one, zero, zero, zero), unroll=forward_unroll)
        values = (e0, e1, e2, jnp.exp2(n))
        for g in range(per_tile):
            for c in range(4):
                out_ref[j * per_tile + g, c] = values[c][g * chunk_rows:(g + 1) * chunk_rows]


def smooth_kernel(d_ref, zhalo_ref, rhalo_ref, out_ref):
    slices, rows, block = d_ref.shape
    shape = (rows, lanes)
    row = lax.broadcasted_iota(jnp.int32, shape, 0)
    first_row = row == 0
    last_row = row == shape[0] - 1

    for j in range(block // lanes):
        cols = pl.ds(j * lanes, lanes)

        def body(z, carry):
            d_prev, d = carry
            d_next = jnp.where(
                z + 1 < slices,
                d_ref[jnp.minimum(z + 1, slices - 1), :, cols].astype(jnp.float32),
                zhalo_ref[1, :, cols],
            )
            rims = rhalo_ref[z, :, cols]
            upper = jnp.where(first_row, rims[0:1], pltpu.roll(d, 1, 0))
            lower = jnp.where(last_row, rims[1:2], pltpu.roll(d, shape[0] - 1, 0))
            out_ref[z, :, cols] = 2.0 * smooth_weight * (
                (d - d_prev) + (d - d_next) + (d - upper) + (d - lower)
            )
            return (d, d_next)

        start = (zhalo_ref[0, :, cols], d_ref[0, :, cols].astype(jnp.float32))
        lax.fori_loop(0, slices, body, start, unroll=2)


def backward_kernel(d_ref, c_ref, ans_ref, smooth_ref, gd_ref, gc_ref, *, step, slices_total):
    slices, rows, block = gd_ref.shape
    shape = (rows, lanes)
    subs = block // lanes
    per_tile = ans_ref.shape[0] // (pl.num_programs(0) * subs)
    scale = -step * log2e
    gain = optical_depth / slices_total

    for j in range(subs):
        cols = pl.ds(j * lanes, lanes)
        base = (pl.program_id(0) * subs + j) * per_tile
        place = pl.ds(pl.multiple_of((pl.program_id(0) * subs + j) * lanes, lanes), lanes)

        def pixel(c):
            if per_tile == 1:
                return ans_ref[base, c]
            return jnp.concatenate([ans_ref[base + g, c] for g in range(per_tile)], axis=0)

        def body(z, carry):
            n, front, w0, w1, w2 = carry
            d = d_ref[z, :, place].astype(jnp.float32)
            dtn = softplus(d) * scale
            lit = front * (1.0 - jnp.exp2(dtn))
            n_next = n + dtn
            through = jnp.exp2(n_next)
            inv = jnp.exp2(-n_next)
            col = [jax.nn.sigmoid(c_ref[c, z, :, cols].astype(jnp.float32)) for c in range(3)]
            lit_col = [lit * col[c] for c in range(3)]
            w = [w0 + lit_col[0], w1 + lit_col[1], w2 + lit_col[2]]
            res = [pixel(c) for c in range(3)]
            emitted = res[0] * col[0] + res[1] * col[1] + res[2] * col[2]
            left = res[0] * w[0] + res[1] * w[1] + res[2] * w[2]
            inner = emitted - inv * (pixel(3) - left)
            for c in range(3):
                gc_ref[c, z, :, cols] = res[c] * lit_col[c] * (1.0 - col[c])
            gd_ref[z, :, cols] = gain * through * jax.nn.sigmoid(d) * inner + smooth_ref[z, :, cols]
            return (n_next, through, w[0], w[1], w[2])

        zero = jnp.zeros(shape, jnp.float32)
        one = jnp.ones(shape, jnp.float32)
        lax.fori_loop(0, slices, body, (zero, one, zero, zero, zero), unroll=backward_unroll)


def forward_partial(density, colour_raw, step, depth_count):
    slices, rows, width = density.shape
    tiles, per_tile, chunk_rows = chunking(rows, width, depth_count)
    block = lanes * forward_subs if tiles % forward_subs == 0 else lanes
    return pl.pallas_call(
        functools.partial(forward_kernel, step=step),
        grid=(width // block,),
        in_specs=[
            pl.BlockSpec((slices, rows, block), lambda i: (0, 0, i)),
            pl.BlockSpec((3, slices, rows, block), lambda i: (0, 0, 0, i)),
        ],
        out_specs=pl.BlockSpec(
            (per_tile * (block // lanes), 4, chunk_rows, lanes), lambda i: (i, 0, 0, 0)
        ),
        out_shape=jax.ShapeDtypeStruct((tiles * per_tile, 4, chunk_rows, lanes), jnp.float32),
    )(density, colour_raw)


def smooth_term(density, zhalo, rhalo):
    slices, rows, width = density.shape
    tiles = width // lanes
    block = lanes * forward_subs if tiles % forward_subs == 0 else lanes
    slab = pl.BlockSpec((slices, rows, block), lambda i: (0, 0, i))
    return pl.pallas_call(
        smooth_kernel,
        grid=(width // block,),
        in_specs=[
            slab,
            pl.BlockSpec((2, rows, block), lambda i: (0, 0, i)),
            pl.BlockSpec((slices, 2, block), lambda i: (0, 0, i)),
        ],
        out_specs=slab,
        out_shape=jax.ShapeDtypeStruct((slices, rows, width), jnp.float32),
    )(density, zhalo, rhalo)


def backward_grads(density, colour_raw, answers, smooth, step, slices_total):
    slices, rows, width = density.shape
    tiles = width // lanes
    block = lanes * backward_subs if tiles % backward_subs == 0 else lanes
    slab = pl.BlockSpec((slices, rows, block), lambda i: (0, 0, i))
    colours = pl.BlockSpec((3, slices, rows, block), lambda i: (0, 0, 0, i))
    return pl.pallas_call(
        functools.partial(backward_kernel, step=step, slices_total=float(slices_total)),
        grid=(width // block,),
        in_specs=[
            pl.BlockSpec(memory_space=pltpu.VMEM),
            colours,
            pl.BlockSpec(memory_space=pltpu.VMEM),
            slab,
        ],
        out_specs=[slab, colours],
        out_shape=[
            jax.ShapeDtypeStruct((slices, rows, width), jnp.float32),
            jax.ShapeDtypeStruct((3, slices, rows, width), jnp.float32),
        ],
        input_output_aliases={3: 0},
    )(
        pltpu.with_memory_space_constraint(density, pltpu.VMEM),
        colour_raw,
        pltpu.with_memory_space_constraint(answers, pltpu.VMEM),
        smooth,
    )


def composite(parts, slab_rank, target_piece, slices_total):
    emitted, passing = (parts[:, :3], parts[:, 3])
    earlier = (slab_rank[None, :] < slab_rank[:, None]).astype(jnp.float32)[:, :, None, None]
    later = (slab_rank[None, :] > slab_rank[:, None]).astype(jnp.float32)[:, :, None, None, None]
    front = jnp.exp(jnp.sum(earlier * jnp.log(passing)[None], axis=1))
    weighted = front[:, None] * emitted
    behind = jnp.sum(later * weighted[None], axis=1) / (front * passing)[:, None]
    residual = jnp.sum(weighted, axis=0) - target_piece
    scaled_residual = slices_total * (front[:, None] * residual[None])
    scaled_behind = slices_total * (front * jnp.sum(residual[None] * behind, axis=1))
    folded = jnp.sum(scaled_residual * emitted, axis=1) + passing * scaled_behind
    return jnp.concatenate([scaled_residual, folded[:, None]], axis=1)


def halos(density_raw):
    depth_count = lax.axis_size("depth")
    rows_count = lax.axis_size("rows")
    depth_at = lax.axis_index("depth")
    rows_at = lax.axis_index("rows")
    up_d = [(i, i + 1) for i in range(depth_count - 1)]
    up_r = [(i, i + 1) for i in range(rows_count - 1)]
    first_slice = density_raw[:1]
    last_slice = density_raw[-1:]
    first_row = density_raw[:, :1]
    last_row = density_raw[:, -1:]
    prev_slice = lax.ppermute(last_slice, "depth", up_d)
    next_slice = lax.ppermute(first_slice, "depth", [(j, i) for i, j in up_d])
    prev_row = lax.ppermute(last_row, "rows", up_r)
    next_row = lax.ppermute(first_row, "rows", [(j, i) for i, j in up_r])
    prev_slice = jnp.where(depth_at > 0, prev_slice, first_slice)
    next_slice = jnp.where(depth_at < depth_count - 1, next_slice, last_slice)
    prev_row = jnp.where(rows_at > 0, prev_row, first_row)
    next_row = jnp.where(rows_at < rows_count - 1, next_row, last_row)
    zhalo = jnp.concatenate([prev_slice, next_slice], axis=0).astype(jnp.float32)
    rhalo = jnp.concatenate([prev_row, next_row], axis=1).astype(jnp.float32)
    return zhalo, rhalo


def local(density_raw, colour_raw, target, slab_rank):
    slices_dev, rows_dev, width = density_raw.shape
    depth_count = lax.axis_size("depth")
    slices_total = slices_dev * depth_count
    step = optical_depth / slices_total
    tiles, per_tile, chunk_rows = chunking(rows_dev, width, depth_count)
    partial_value = forward_partial(density_raw, colour_raw, step, depth_count)
    partial_value, after_forward = lax.optimization_barrier((partial_value, density_raw))
    zhalo, rhalo = halos(after_forward)
    received = lax.all_to_all(partial_value, "depth", 0, 0, tiled=True)
    position = lax.axis_index("depth")
    target_piece = lax.dynamic_slice(
        target,
        (0, (position % per_tile) * chunk_rows, (position // per_tile) * lanes),
        (3, chunk_rows, lanes),
    )
    answers = composite(received, slab_rank, target_piece, float(slices_total))
    returned = lax.all_to_all(answers, "depth", 0, 0, tiled=True)
    smooth = smooth_term(density_raw, zhalo, rhalo)
    return backward_grads(density_raw, colour_raw, returned, smooth, step, slices_total)


def solution(mesh):
    placed = (P("depth", "rows", None), P(None, "depth", "rows", None), P(None, "rows", None), P())
    return jax.shard_map(
        local,
        mesh=mesh,
        in_specs=placed,
        out_specs=(P("depth", "rows", None), P(None, "depth", "rows", None)),
        check_vma=False,
    )
```

```python
import functools

import jax
import jax.numpy as jnp
from jax import lax
from jax.experimental import pallas as pl
from jax.experimental.pallas import tpu as pltpu
from jax.sharding import PartitionSpec as P

optical_depth = 2.5
smooth_weight = 0.05
lanes = 128
forward_subs = 4
backward_subs = 2
forward_unroll = 32
backward_unroll = 16


log2e = 1.4426950408889634
ln2 = 0.6931471805599453


def softplus(x):
    return jnp.maximum(x, 0.0) + ln2 * jnp.log2(1.0 + jnp.exp2(jnp.abs(x) * -log2e))


def chunking(rows, width, depth_count):
    tiles = width // lanes
    per_tile = max(depth_count // tiles, 1)
    return tiles, per_tile, rows // per_tile


def forward_kernel(d_ref, c_ref, out_ref, *, step):
    slices, rows, block = c_ref.shape[1:]
    shape = (rows, lanes)
    subs = block // lanes
    per_tile = out_ref.shape[0] // subs
    chunk_rows = out_ref.shape[2]
    scale = -step * log2e

    for j in range(subs):
        cols = pl.ds(j * lanes, lanes)
        place = pl.ds(pl.multiple_of((pl.program_id(0) * subs + j) * lanes, lanes), lanes)

        def body(z, carry):
            n, front, e0, e1, e2 = carry
            dtn = softplus(d_ref[z, :, place].astype(jnp.float32)) * scale
            kept = jnp.exp2(dtn)
            lit = front * (1.0 - kept)
            n = n + dtn
            e0 = e0 + lit * jax.nn.sigmoid(c_ref[0, z, :, cols].astype(jnp.float32))
            e1 = e1 + lit * jax.nn.sigmoid(c_ref[1, z, :, cols].astype(jnp.float32))
            e2 = e2 + lit * jax.nn.sigmoid(c_ref[2, z, :, cols].astype(jnp.float32))
            return (n, front * kept, e0, e1, e2)

        zero = jnp.zeros(shape, jnp.float32)
        one = jnp.ones(shape, jnp.float32)
        n, _, e0, e1, e2 = lax.fori_loop(0, slices, body, (zero, one, zero, zero, zero), unroll=forward_unroll)
        values = (e0, e1, e2, jnp.exp2(n))
        for g in range(per_tile):
            for c in range(4):
                out_ref[j * per_tile + g, c] = values[c][g * chunk_rows:(g + 1) * chunk_rows]


def smooth_kernel(d_ref, zhalo_ref, rhalo_ref, out_ref):
    slices, rows, block = d_ref.shape
    shape = (rows, lanes)
    row = lax.broadcasted_iota(jnp.int32, shape, 0)
    first_row = row == 0
    last_row = row == shape[0] - 1

    for j in range(block // lanes):
        cols = pl.ds(j * lanes, lanes)

        def body(z, carry):
            d_prev, d = carry
            d_next = jnp.where(
                z + 1 < slices,
                d_ref[jnp.minimum(z + 1, slices - 1), :, cols].astype(jnp.float32),
                zhalo_ref[1, :, cols],
            )
            rims = rhalo_ref[z, :, cols]
            upper = jnp.where(first_row, rims[0:1], pltpu.roll(d, 1, 0))
            lower = jnp.where(last_row, rims[1:2], pltpu.roll(d, shape[0] - 1, 0))
            out_ref[z, :, cols] = 2.0 * smooth_weight * (
                (d - d_prev) + (d - d_next) + (d - upper) + (d - lower)
            )
            return (d, d_next)

        start = (zhalo_ref[0, :, cols], d_ref[0, :, cols].astype(jnp.float32))
        lax.fori_loop(0, slices, body, start, unroll=2)


def backward_kernel(d_ref, c_ref, ans_ref, smooth_ref, gd_ref, gc_ref, *, step, slices_total):
    slices, rows, block = gd_ref.shape
    shape = (rows, lanes)
    subs = block // lanes
    per_tile = ans_ref.shape[0] // (pl.num_programs(0) * subs)
    scale = -step * log2e
    gain = optical_depth / slices_total

    for j in range(subs):
        cols = pl.ds(j * lanes, lanes)
        base = (pl.program_id(0) * subs + j) * per_tile
        place = pl.ds(pl.multiple_of((pl.program_id(0) * subs + j) * lanes, lanes), lanes)

        def pixel(c):
            if per_tile == 1:
                return ans_ref[base, c]
            return jnp.concatenate([ans_ref[base + g, c] for g in range(per_tile)], axis=0)

        def body(z, carry):
            n, front, w0, w1, w2 = carry
            d = d_ref[z, :, place].astype(jnp.float32)
            dtn = softplus(d) * scale
            lit = front * (1.0 - jnp.exp2(dtn))
            n_next = n + dtn
            through = jnp.exp2(n_next)
            inv = jnp.exp2(-n_next)
            col = [jax.nn.sigmoid(c_ref[c, z, :, cols].astype(jnp.float32)) for c in range(3)]
            lit_col = [lit * col[c] for c in range(3)]
            w = [w0 + lit_col[0], w1 + lit_col[1], w2 + lit_col[2]]
            res = [pixel(c) for c in range(3)]
            emitted = res[0] * col[0] + res[1] * col[1] + res[2] * col[2]
            left = res[0] * w[0] + res[1] * w[1] + res[2] * w[2]
            inner = emitted - inv * (pixel(3) - left)
            for c in range(3):
                gc_ref[c, z, :, cols] = res[c] * lit_col[c] * (1.0 - col[c])
            gd_ref[z, :, cols] = gain * through * jax.nn.sigmoid(d) * inner + smooth_ref[z, :, cols]
            return (n_next, through, w[0], w[1], w[2])

        zero = jnp.zeros(shape, jnp.float32)
        one = jnp.ones(shape, jnp.float32)
        lax.fori_loop(0, slices, body, (zero, one, zero, zero, zero), unroll=backward_unroll)


def forward_partial(density, colour_raw, step, depth_count):
    slices, rows, width = density.shape
    tiles, per_tile, chunk_rows = chunking(rows, width, depth_count)
    block = lanes * forward_subs if tiles % forward_subs == 0 else lanes
    return pl.pallas_call(
        functools.partial(forward_kernel, step=step),
        grid=(width // block,),
        in_specs=[
            pl.BlockSpec(memory_space=pltpu.VMEM),
            pl.BlockSpec((3, slices, rows, block), lambda i: (0, 0, 0, i)),
        ],
        out_specs=pl.BlockSpec(
            (per_tile * (block // lanes), 4, chunk_rows, lanes), lambda i: (i, 0, 0, 0)
        ),
        out_shape=jax.ShapeDtypeStruct((tiles * per_tile, 4, chunk_rows, lanes), jnp.float32),
    )(pltpu.with_memory_space_constraint(density, pltpu.VMEM), colour_raw)


def smooth_term(density, zhalo, rhalo):
    slices, rows, width = density.shape
    tiles = width // lanes
    block = lanes * forward_subs if tiles % forward_subs == 0 else lanes
    slab = pl.BlockSpec((slices, rows, block), lambda i: (0, 0, i))
    return pl.pallas_call(
        smooth_kernel,
        grid=(width // block,),
        in_specs=[
            slab,
            pl.BlockSpec((2, rows, block), lambda i: (0, 0, i)),
            pl.BlockSpec((slices, 2, block), lambda i: (0, 0, i)),
        ],
        out_specs=slab,
        out_shape=jax.ShapeDtypeStruct((slices, rows, width), jnp.float32),
    )(density, zhalo, rhalo)


def backward_grads(density, colour_raw, answers, smooth, step, slices_total):
    slices, rows, width = density.shape
    tiles = width // lanes
    block = lanes * backward_subs if tiles % backward_subs == 0 else lanes
    slab = pl.BlockSpec((slices, rows, block), lambda i: (0, 0, i))
    colours = pl.BlockSpec((3, slices, rows, block), lambda i: (0, 0, 0, i))
    return pl.pallas_call(
        functools.partial(backward_kernel, step=step, slices_total=float(slices_total)),
        grid=(width // block,),
        in_specs=[
            pl.BlockSpec(memory_space=pltpu.VMEM),
            colours,
            pl.BlockSpec(memory_space=pltpu.VMEM),
            slab,
        ],
        out_specs=[slab, colours],
        out_shape=[
            jax.ShapeDtypeStruct((slices, rows, width), jnp.float32),
            jax.ShapeDtypeStruct((3, slices, rows, width), jnp.float32),
        ],
        input_output_aliases={3: 0},
    )(
        pltpu.with_memory_space_constraint(density, pltpu.VMEM),
        colour_raw,
        pltpu.with_memory_space_constraint(answers, pltpu.VMEM),
        smooth,
    )


def composite(parts, slab_rank, target_piece, slices_total):
    emitted, passing = (parts[:, :3], parts[:, 3])
    earlier = (slab_rank[None, :] < slab_rank[:, None]).astype(jnp.float32)[:, :, None, None]
    later = (slab_rank[None, :] > slab_rank[:, None]).astype(jnp.float32)[:, :, None, None, None]
    front = jnp.exp(jnp.sum(earlier * jnp.log(passing)[None], axis=1))
    weighted = front[:, None] * emitted
    behind = jnp.sum(later * weighted[None], axis=1) / (front * passing)[:, None]
    residual = jnp.sum(weighted, axis=0) - target_piece
    scaled_residual = slices_total * (front[:, None] * residual[None])
    scaled_behind = slices_total * (front * jnp.sum(residual[None] * behind, axis=1))
    folded = jnp.sum(scaled_residual * emitted, axis=1) + passing * scaled_behind
    return jnp.concatenate([scaled_residual, folded[:, None]], axis=1)


def halos(density_raw):
    depth_count = lax.axis_size("depth")
    rows_count = lax.axis_size("rows")
    depth_at = lax.axis_index("depth")
    rows_at = lax.axis_index("rows")
    up_d = [(i, i + 1) for i in range(depth_count - 1)]
    up_r = [(i, i + 1) for i in range(rows_count - 1)]
    first_slice = density_raw[:1]
    last_slice = density_raw[-1:]
    first_row = density_raw[:, :1]
    last_row = density_raw[:, -1:]
    prev_slice = lax.ppermute(last_slice, "depth", up_d)
    next_slice = lax.ppermute(first_slice, "depth", [(j, i) for i, j in up_d])
    prev_row = lax.ppermute(last_row, "rows", up_r)
    next_row = lax.ppermute(first_row, "rows", [(j, i) for i, j in up_r])
    prev_slice = jnp.where(depth_at > 0, prev_slice, first_slice)
    next_slice = jnp.where(depth_at < depth_count - 1, next_slice, last_slice)
    prev_row = jnp.where(rows_at > 0, prev_row, first_row)
    next_row = jnp.where(rows_at < rows_count - 1, next_row, last_row)
    zhalo = jnp.concatenate([prev_slice, next_slice], axis=0).astype(jnp.float32)
    rhalo = jnp.concatenate([prev_row, next_row], axis=1).astype(jnp.float32)
    return zhalo, rhalo


def local(density_raw, colour_raw, target, slab_rank):
    slices_dev, rows_dev, width = density_raw.shape
    depth_count = lax.axis_size("depth")
    slices_total = slices_dev * depth_count
    step = optical_depth / slices_total
    tiles, per_tile, chunk_rows = chunking(rows_dev, width, depth_count)
    partial_value = forward_partial(density_raw, colour_raw, step, depth_count)
    partial_value, after_forward = lax.optimization_barrier((partial_value, density_raw))
    zhalo, rhalo = halos(after_forward)
    received = lax.all_to_all(partial_value, "depth", 0, 0, tiled=True)
    position = lax.axis_index("depth")
    target_piece = lax.dynamic_slice(
        target,
        (0, (position % per_tile) * chunk_rows, (position // per_tile) * lanes),
        (3, chunk_rows, lanes),
    )
    answers = composite(received, slab_rank, target_piece, float(slices_total))
    returned = lax.all_to_all(answers, "depth", 0, 0, tiled=True)
    smooth = smooth_term(density_raw, zhalo, rhalo)
    return backward_grads(density_raw, colour_raw, returned, smooth, step, slices_total)


def solution(mesh):
    placed = (P("depth", "rows", None), P(None, "depth", "rows", None), P(None, "rows", None), P())
    return jax.shard_map(
        local,
        mesh=mesh,
        in_specs=placed,
        out_specs=(P("depth", "rows", None), P(None, "depth", "rows", None)),
        check_vma=False,
    )
```
